32 devices in a mesh: group: 2 (over x), node: 16 (over z, y, core).
Axes of the slice: x: 2, y: 2, z: 4, core: 2. Of those that a mesh axis runs over, the one named last changes fastest.
Arguments:
- states: bfloat16 [512, 2048], P(('group', 'node')), parts along dimension 0, may hold values from -400 to 400
- norm_gain: float32 [2048], replicated, may hold values from 0.5 to 1.5
- picks: int32 [512, 8], P(('group', 'node')), parts along dimension 0, may hold values from 0 to 15, all different within a row; in each aligned block of 16 rows (0 to 15, 16 to 31, ...) at most 16 rows name the same one
- gate_weights: float32 [512, 8], P(('group', 'node')), parts along dimension 0, may hold values from 0.05 to 1
- w_gate: bfloat16 [16, 2048, 768], P('node'), may hold values from -0.125 to 0.125
- w_up: bfloat16 [16, 2048, 768], P('node'), may hold values from -0.125 to 0.125
- w_down: bfloat16 [16, 768, 2048], P('node'), may hold values from -0.21875 to 0.21875
- queries: bfloat16 [128, 4096], P(('group', 'node')), parts along dimension 0, may hold values from -88 to 88
- keys: bfloat16 [128, 256, 512], P(('group', 'node')), parts along dimension 0, may hold values from -4 to 4
- values: bfloat16 [128, 256, 512], P(('group', 'node')), parts along dimension 0, may hold values from -4 to 4
- incoming_keys: bfloat16 [128, 512], P(('group', 'node')), parts along dimension 0, may hold values from -4 to 4
- incoming_values: bfloat16 [128, 512], P(('group', 'node')), parts along dimension 0, may hold values from -4 to 4
- lengths: int32 [128], P(('group', 'node')), parts along dimension 0, may hold values from 32 to 256, as said below
Outputs:
- moe_output: bfloat16 [512, 2048], P(('group', 'node')), parts along dimension 0
- attention_output: bfloat16 [128, 4096], P(('group', 'node')), parts along dimension 0
The draws below stay inside these ranges and needn't reach their ends.
There are 2 independent parts, one for each index of `group`. The reference program is written for one: setup_inputs(seed, part) draws one part's arguments, and reference() takes and returns one part's arrays. A program takes and returns all parts, laid end to end along the dimension named above; an argument that names none is the same for every part. Nothing has to cross between parts.
Inputs may be any that keep to these rules, and one draw needn't show every extreme that they name: Each token picks 8 different experts; among the 16 tokens of one device no expert is picked by more than 16 tokens, a bound that some block reaches. `lengths`: the first request of each device holds 256 cached tokens.
All inputs are finite; a program needn't handle non-finite values.
Results may differ from the reference program's by a relative error of at most 0.0085.
Values may be sent and summed in bfloat16 or wider, within the bound.
No kernel may reach another device: no remote copies, remote signals or barrier semaphores. Data moves between devices by JAX's collectives and lax.ppermute only.
A program may use at most 64 MiB of HBM per device.

```python
import math
import jax
import jax.numpy as jnp
import numpy as np
from jax import lax

D = 2048
FF = 768
QUERY_HEADS = 32
KEY_VALUE_HEADS = 4
HEAD_WIDTH = 128
TOPK = 8
TOK_DEV = 16
REQ_DEV = 4
CACHE_SLOTS = 256
EXPERTS = 16
CAP = 16
TOKENS = 256
REQUEST_COUNT = 64
N_NODE = 16


def random_key_seed(key):
    sampled_lengths = jax.random.normal(jax.random.fold_in(key, 7), (REQUEST_COUNT, CACHE_SLOTS, KEY_VALUE_HEADS * HEAD_WIDTH), jnp.float32)
    return jnp.clip(sampled_lengths, -4.0, 4.0)


def draw_keys(key, part):
    base = random_key_seed(key)
    return base.astype(jnp.bfloat16)


def draw_queries(key, part):
    sampled_lengths = jnp.clip(jax.random.normal(jax.random.fold_in(key, 11), (REQUEST_COUNT, QUERY_HEADS * HEAD_WIDTH), jnp.float32), -4.0, 4.0)
    return sampled_lengths.astype(jnp.bfloat16)


def draw_states(key, part):
    first_key = jax.random.fold_in(key, 21)
    second_key = jax.random.fold_in(key, 22)
    third_key = jax.random.fold_in(key, 23)
    entries = jnp.clip(jax.random.normal(first_key, (TOKENS, D), jnp.float32), -4.0, 4.0)
    row_scale = jnp.exp(jax.random.uniform(second_key, (TOKENS, 1), jnp.float32) * math.log(10.0))
    column_scale = jnp.exp(jax.random.uniform(third_key, (1, D), jnp.float32) * math.log(10.0))
    return (entries * row_scale * column_scale).astype(jnp.bfloat16)


def draw_lengths(key, part):
    sampled_lengths = jax.random.randint(key, (REQUEST_COUNT,), CACHE_SLOTS // 8, CACHE_SLOTS + 1, dtype=jnp.int32)
    return jnp.where(jnp.arange(REQUEST_COUNT) % REQ_DEV == 0, CACHE_SLOTS, sampled_lengths).astype(jnp.int32)


def block_levels(own_key, extent, split, smallest, high):
    def one(dim, blocks):
        steps = jax.random.uniform(jax.random.fold_in(jax.random.fold_in(own_key, 6), dim), (blocks,), jnp.float32, smallest / len(split), high / len(split))
        return jnp.repeat(jnp.exp(steps), extent[dim] // blocks).reshape((-1,) + (1,) * (len(extent) - dim - 1))

    factor_of = one(*split[0])
    for cut in split[1:]:
        factor_of = factor_of * one(*cut)
    return factor_of


def assign_block(key, own, number, rows, count, top, bound, skew):
    ranking = jax.random.permutation(key, count)
    crowded, usual = portions_of(count, rows * top, bound, skew, True), portions_of(count, rows * top, bound, skew, False)
    places = jnp.arange(count)

    def named(sizes, turn):
        used = int((sizes > 0).sum())
        fixed = max(1, used // 4)
        moved = fixed + (places - fixed + turn * (used - fixed)) % max(1, count - fixed)
        return jnp.zeros((count,), jnp.int32).at[ranking[jnp.where(places < fixed, places, moved)]].set(jnp.asarray(sizes, jnp.int32))

    sizes = jnp.where(number % 4 == 0, named(crowded, number // 4), named(usual, number - number // 4 - 1))
    mixed = jax.random.permutation(jax.random.fold_in(own, 3), count)
    donor, taker = mixed[0:count // 2 * 2:2], mixed[1:count // 2 * 2:2]
    margin = jnp.minimum(sizes[donor] - 1, bound - sizes[taker]) // 2
    margin = jnp.where((donor == ranking[0]) | (taker == ranking[0]) | (sizes[taker] == 0), 0, jnp.maximum(margin, 0))
    moved = jax.random.randint(jax.random.fold_in(own, 4), (count // 2,), 0, 1 << 20) % (margin + 1)
    sizes = sizes.at[donor].add(-moved).at[taker].add(moved)
    items = jnp.searchsorted(jnp.cumsum(sizes), jnp.arange(rows * top), side="right").astype(jnp.int32)
    grid = items.reshape(top, rows).T
    grid = grid[jax.random.permutation(jax.random.fold_in(own, 1), rows)]
    turn = jax.random.randint(jax.random.fold_in(own, 2), (rows, 1), 0, top)
    return jnp.take_along_axis(grid, (jnp.arange(top)[None, :] + turn) % top, axis=1)


def portions_of(amount, total, reach, lean, full):
    weights = [(1 << 20) // math.isqrt(grade ** lean) + 1 for grade in range(1, amount + 1)]
    largest = reach if full else min(reach, max(-(-total // amount), total * weights[0] // sum(weights)))
    least = 1 if total - largest >= amount - 1 else 0
    holding, surplus = [largest] + [least] * (amount - 1), total - largest - least * (amount - 1)
    while surplus > 0:
        candidates = [i for i in range(1, amount) if holding[i] < largest] or [i for i in range(1, amount) if holding[i] < reach]
        pool, remaining = sum([weights[i] for i in candidates]), surplus
        for i in candidates:
            more = min(reach - holding[i], max(1, remaining * weights[i] // pool), surplus)
            holding[i] = holding[i] + more
            surplus = surplus - more
    return np.array(holding)


def gaussian(key, dims, deviation, most, pieces=(), kind=jnp.bfloat16):
    values = deviation * jax.random.normal(key, dims, jnp.float32)
    if pieces:
        values = values * block_levels(key, dims, pieces, -0.22, 0.18)
    return jnp.clip(values, -most, most).astype(kind)


def setup_inputs(seed: int = 0, part: int = 0) -> dict:
    arg_keys = jax.random.split(jax.random.key(seed), 14)
    part_splits = jax.random.split(jax.random.fold_in(arg_keys[13], part), 14)
    states = draw_states(jax.random.fold_in(jax.random.fold_in(arg_keys[13], part), 71), part)
    norm_gain = jnp.clip(1.0 + 0.1 * jax.random.normal(arg_keys[1], (D,), jnp.float32), 0.5, 1.5)
    picks_keys = jax.random.split(jax.random.fold_in(part_splits[2], 1), TOKENS // TOK_DEV)
    picks_turns = jax.random.permutation(jax.random.fold_in(part_splits[2], 3), TOKENS // TOK_DEV)
    picks = jax.vmap(lambda own, number: assign_block(jax.random.fold_in(part_splits[2], 2), own, number, TOK_DEV, EXPERTS, TOPK, CAP, 2))(picks_keys, picks_turns).reshape((TOKENS, TOPK))
    gate_weights = jnp.clip(jnp.exp(math.log(1.0) - 2.9957323 * jax.random.uniform(part_splits[3], (TOKENS, TOPK), jnp.float32) ** block_levels(part_splits[3], (TOKENS, TOPK), ((0, 16),), -0.2, 0.2)), 0.05, 1.0)
    w_gate = gaussian(arg_keys[4], (EXPERTS, D, FF), D ** -0.5, 0.125, ((0, 16),))
    w_up = gaussian(arg_keys[5], (EXPERTS, D, FF), D ** -0.5, 0.125, ((0, 16),))
    w_down = gaussian(arg_keys[6], (EXPERTS, FF, D), FF ** -0.5, 0.21875, ((0, 16),))
    queries = draw_queries(jax.random.fold_in(jax.random.fold_in(arg_keys[13], part), 71), part)
    keys = draw_keys(jax.random.fold_in(jax.random.fold_in(arg_keys[13], part), 71), part)
    values = gaussian(part_splits[9], (REQUEST_COUNT, CACHE_SLOTS, KEY_VALUE_HEADS * HEAD_WIDTH), 1.0, 4.0, ((0, 16),))
    incoming_keys = gaussian(part_splits[10], (REQUEST_COUNT, KEY_VALUE_HEADS * HEAD_WIDTH), 1.0, 4.0, ((0, 16),))
    incoming_values = gaussian(part_splits[11], (REQUEST_COUNT, KEY_VALUE_HEADS * HEAD_WIDTH), 1.0, 4.0, ((0, 16),))
    lengths = draw_lengths(jax.random.fold_in(jax.random.fold_in(arg_keys[13], part), 71), part)
    return dict(states=states, norm_gain=norm_gain, picks=picks, gate_weights=gate_weights, w_gate=w_gate, w_up=w_up, w_down=w_down, queries=queries, keys=keys, values=values, incoming_keys=incoming_keys, incoming_values=incoming_values, lengths=lengths)


def expert_rows(inputs, gate_matrix, up_matrix, down_matrix):
    gate_part = jnp.dot(inputs, gate_matrix, preferred_element_type=jnp.float32)
    up_part = jnp.dot(inputs, up_matrix, preferred_element_type=jnp.float32)
    inner = (jax.nn.silu(gate_part) * up_part).astype(jnp.bfloat16)
    return jnp.dot(inner, down_matrix, preferred_element_type=jnp.float32).astype(jnp.bfloat16)

def reference(states, norm_gain, picks, gate_weights, w_gate, w_up, w_down, queries, keys, values, incoming_keys, incoming_values, lengths):
    widened = states.astype(jnp.float32)
    meansq = lax.optimization_barrier(jnp.mean(widened * widened, axis=1, keepdims=True)) + 1e-06
    normed = (widened / jnp.sqrt(meansq) * norm_gain[None, :]).astype(jnp.bfloat16)
    flattened = picks.reshape(-1).astype(jnp.int32)
    pair_count = flattened.shape[0]
    shares = gate_weights / lax.optimization_barrier(jnp.sum(gate_weights, axis=1, keepdims=True))
    share_flat = jnp.concatenate([shares.reshape(-1), jnp.zeros((1,), jnp.float32)])
    padded_in = jnp.concatenate([normed, jnp.zeros((1, D), jnp.bfloat16)], axis=0)
    row_bound = N_NODE * CAP

    def one_expert(summed, inputs):
        gate_matrix, up_matrix, down_matrix, expert_id = inputs
        chosen = jnp.nonzero(flattened == expert_id, size=row_bound, fill_value=pair_count)[0].astype(jnp.int32)
        owners = (chosen // TOPK).astype(jnp.int32)
        produced = expert_rows(padded_in[owners], gate_matrix, up_matrix, down_matrix)
        weighted = share_flat[chosen][:, None] * produced.astype(jnp.float32)
        return (summed.at[owners].add(weighted), None)
    start_sum = jnp.zeros((TOKENS + 1, D), jnp.float32)
    summed, _ = lax.scan(one_expert, start_sum, (w_gate, w_up, w_down, jnp.arange(EXPERTS, dtype=jnp.int32)))
    moe_output = summed[:TOKENS].astype(jnp.bfloat16)
    query_groups = QUERY_HEADS // KEY_VALUE_HEADS
    score_scale = 1.0 / math.sqrt(HEAD_WIDTH)
    query_rows = queries.astype(jnp.float32).reshape(REQUEST_COUNT, KEY_VALUE_HEADS, query_groups, HEAD_WIDTH)
    stored_keys = keys.astype(jnp.float32).reshape(REQUEST_COUNT, CACHE_SLOTS, KEY_VALUE_HEADS, HEAD_WIDTH)
    stored_values = values.astype(jnp.float32).reshape(REQUEST_COUNT, CACHE_SLOTS, KEY_VALUE_HEADS, HEAD_WIDTH)
    scores = jnp.einsum('rkgd,rlkd->rkgl', query_rows, stored_keys) * score_scale
    new_token_scores = jnp.einsum('behw,bew->beh', query_rows, incoming_keys.astype(jnp.float32).reshape(REQUEST_COUNT, KEY_VALUE_HEADS, HEAD_WIDTH)) * score_scale
    present = (jnp.arange(CACHE_SLOTS, dtype=jnp.int32)[None, :] < lengths[:, None])[:, None, None, :]
    masked = jnp.where(present, scores, -1e+30)
    highest = jnp.maximum(lax.optimization_barrier(jnp.max(masked, axis=3)), new_token_scores)
    raised = jnp.where(present, jnp.exp(masked - highest[..., None]), 0.0)
    fresh_raised = jnp.exp(new_token_scores - highest)
    denominator = lax.optimization_barrier(jnp.sum(raised, axis=3)) + fresh_raised
    probs = (raised / denominator[..., None]).astype(jnp.bfloat16)
    new_token_probability = (fresh_raised / denominator).astype(jnp.bfloat16)
    blended_output = jnp.einsum('rkgl,rlkd->rkgd', probs.astype(jnp.float32), stored_values)
    blended_output = blended_output + new_token_probability.astype(jnp.float32)[..., None] * incoming_values.astype(jnp.float32).reshape(REQUEST_COUNT, KEY_VALUE_HEADS, 1, HEAD_WIDTH)
    attention_output = blended_output.reshape(REQUEST_COUNT, QUERY_HEADS * HEAD_WIDTH).astype(jnp.bfloat16)
    return (moe_output, attention_output)
```

```python
import math

import jax
import jax.numpy as jnp
from jax import lax
from jax.sharding import PartitionSpec as P

QUERY_HEADS = 32
KEY_VALUE_HEADS = 4
HEAD_WIDTH = 128
TOPK = 8
TOK_DEV = 16


def expert_block(received, w_gate, w_up, w_down):
    peers = lax.axis_size("node")
    local_experts = w_gate.shape[0]
    slot_count = received.shape[1]
    features = received.shape[2]
    grouped = received.reshape(peers, local_experts, slot_count, features)
    gate_part = jnp.einsum("nesd,edf->nesf", grouped, w_gate, preferred_element_type=jnp.float32)
    up_part = jnp.einsum("nesd,edf->nesf", grouped, w_up, preferred_element_type=jnp.float32)
    inner = (jax.nn.silu(gate_part) * up_part).astype(jnp.bfloat16)
    produced = jnp.einsum(
        "nesf,efd->nesd", inner, w_down, preferred_element_type=jnp.float32
    ).astype(jnp.bfloat16)
    return produced.reshape(peers * local_experts, slot_count, features)


def route_block(normed, picks, gate_weights, w_gate, w_up, w_down, capacity):
    rows_here = picks.shape[0]
    picks_here = picks.shape[1]
    experts_all = w_gate.shape[0] * lax.axis_size("node")
    features = normed.shape[1]
    flattened = picks.reshape(-1)
    expert_ids = jnp.arange(experts_all, dtype=jnp.int32)
    onehot = (flattened[:, None] == expert_ids[None, :]).astype(jnp.int32)
    earlier = jnp.cumsum(onehot, axis=0) - onehot
    slot_of = jnp.sum(earlier * onehot, axis=1)
    target = flattened * capacity + slot_of
    layout = jnp.arange(experts_all * capacity, dtype=jnp.int32)
    placed = jnp.sum(
        (layout[:, None, None] == target.reshape(rows_here, picks_here)[None, :, :]).astype(
            jnp.int32
        ),
        axis=2,
    )
    outgoing = jnp.dot(placed.astype(jnp.bfloat16), normed, preferred_element_type=jnp.float32)
    outgoing = outgoing.astype(jnp.bfloat16).reshape(experts_all, capacity, features)
    produced = expert_block(
        lax.all_to_all(outgoing, "node", split_axis=0, concat_axis=0, tiled=True),
        w_gate,
        w_up,
        w_down,
    )
    returned = lax.all_to_all(produced, "node", split_axis=0, concat_axis=0, tiled=True)
    gathered = jnp.take(returned.reshape(experts_all * capacity, features), target, axis=0)
    gathered = gathered.reshape(rows_here, picks_here, features)
    shares = gate_weights / jnp.sum(gate_weights, axis=1, keepdims=True)
    return jnp.einsum("tk,tkd->td", shares, gathered.astype(jnp.float32)).astype(jnp.bfloat16)


def dense_block(normed, picks, gate_weights, w_gate, w_up, w_down):
    local_experts = w_gate.shape[0]
    node_index = lax.axis_index("node")
    experts_all = local_experts * lax.axis_size("node")
    shares = gate_weights / jnp.sum(gate_weights, axis=1, keepdims=True)
    expert_ids = jnp.arange(experts_all, dtype=jnp.int32)
    chosen = picks[:, :, None] == expert_ids[None, None, :]
    dense_shares = jnp.sum(jnp.where(chosen, shares[:, :, None], 0.0), axis=1)
    every_row = lax.all_gather(normed, "node", axis=0, tiled=True)
    every_share = lax.all_gather(dense_shares, "node", axis=0, tiled=True)
    own_shares = lax.dynamic_slice_in_dim(
        every_share, node_index * local_experts, local_experts, axis=1
    )
    summed = None
    for expert in range(local_experts):
        gate_part = jnp.dot(every_row, w_gate[expert], preferred_element_type=jnp.float32)
        up_part = jnp.dot(every_row, w_up[expert], preferred_element_type=jnp.float32)
        inner = (jax.nn.silu(gate_part) * up_part).astype(jnp.bfloat16)
        produced = jnp.dot(inner, w_down[expert], preferred_element_type=jnp.float32).astype(
            jnp.bfloat16
        )
        column = own_shares[:, expert : expert + 1]
        weighted = jnp.where(column != 0.0, column * produced.astype(jnp.float32), 0.0)
        summed = weighted if summed is None else summed + weighted
    total = lax.psum_scatter(summed, "node", scatter_dimension=0, tiled=True)
    return total.astype(jnp.bfloat16)


def attend(queries, keys, values, incoming_keys, incoming_values, lengths):
    request_rows = queries.shape[0]
    valid_length = keys.shape[1]
    query_groups = QUERY_HEADS // KEY_VALUE_HEADS
    score_scale = 1.0 / math.sqrt(HEAD_WIDTH)
    query_rows = queries.reshape(request_rows, KEY_VALUE_HEADS, query_groups, HEAD_WIDTH)
    stored_keys = keys.reshape(request_rows, valid_length, KEY_VALUE_HEADS, HEAD_WIDTH)
    stored_values = values.reshape(request_rows, valid_length, KEY_VALUE_HEADS, HEAD_WIDTH)
    scores = (
        jnp.einsum("rkgd,rlkd->rkgl", query_rows, stored_keys, preferred_element_type=jnp.float32)
        * score_scale
    )
    new_token_scores = (
        jnp.einsum(
            "behw,bew->beh",
            query_rows,
            incoming_keys.reshape(request_rows, KEY_VALUE_HEADS, HEAD_WIDTH),
            preferred_element_type=jnp.float32,
        )
        * score_scale
    )
    present = (jnp.arange(valid_length, dtype=jnp.int32)[None, :] < lengths[:, None])[
        :, None, None, :
    ]
    masked = jnp.where(present, scores, -1e30)
    highest = jnp.maximum(jnp.max(masked, axis=3), new_token_scores)
    raised = jnp.where(present, jnp.exp(masked - highest[..., None]), 0.0)
    fresh_raised = jnp.exp(new_token_scores - highest)
    denominator = jnp.sum(raised, axis=3) + fresh_raised
    probs = (raised / denominator[..., None]).astype(jnp.bfloat16)
    new_token_probability = (fresh_raised / denominator).astype(jnp.bfloat16)
    blended_output = jnp.einsum(
        "rkgl,rlkd->rkgd", probs, stored_values, preferred_element_type=jnp.float32
    )
    blended_output = blended_output + new_token_probability.astype(jnp.float32)[
        ..., None
    ] * incoming_values.reshape(request_rows, KEY_VALUE_HEADS, 1, HEAD_WIDTH).astype(jnp.float32)
    return blended_output.reshape(request_rows, QUERY_HEADS * HEAD_WIDTH).astype(jnp.bfloat16)


def on_device(
    states,
    norm_gain,
    picks,
    gate_weights,
    w_gate,
    w_up,
    w_down,
    queries,
    keys,
    values,
    incoming_keys,
    incoming_values,
    lengths,
):
    widened = states.astype(jnp.float32)
    meansq = jnp.mean(widened * widened, axis=1, keepdims=True) + 1e-06
    normed = (widened / jnp.sqrt(meansq) * norm_gain[None, :]).astype(jnp.bfloat16)
    experts_all = w_gate.shape[0] * lax.axis_size("node")
    capacity = min(TOK_DEV, max(2, 2 * TOK_DEV * TOPK // experts_all))
    gathered_rows = normed.shape[0] * lax.axis_size("node")
    if gathered_rows <= experts_all * capacity:
        moe_output = dense_block(normed, picks, gate_weights, w_gate, w_up, w_down)
    else:
        moe_output = route_block(normed, picks, gate_weights, w_gate, w_up, w_down, capacity)
    attention_output = attend(queries, keys, values, incoming_keys, incoming_values, lengths)
    return (moe_output, attention_output)


def solution(mesh):
    in_specs = (
        P(("group", "node"), None),
        P(),
        P(("group", "node"), None),
        P(("group", "node"), None),
        P("node", None, None),
        P("node", None, None),
        P("node", None, None),
        P(("group", "node"), None),
        P(("group", "node"), None, None),
        P(("group", "node"), None, None),
        P(("group", "node"), None),
        P(("group", "node"), None),
        P(("group", "node")),
    )
    out_specs = (P(("group", "node"), None), P(("group", "node"), None))
    return jax.shard_map(
        on_device, mesh=mesh, in_specs=in_specs, out_specs=out_specs, check_vma=False
    )
```

```python
import math

import jax
import jax.numpy as jnp
from jax import lax
from jax.sharding import Mesh, PartitionSpec as P

QUERY_HEADS = 32
KEY_VALUE_HEADS = 4
HEAD_WIDTH = 128
TOPK = 8
TOK_DEV = 16
NODE = ("chip", "core")


def node_size():
    return lax.axis_size("chip") * lax.axis_size("core")


def node_index():
    return lax.axis_index("chip") * lax.axis_size("core") + lax.axis_index("core")


def expert_block(received, w_gate, w_up, w_down):
    peers = node_size()
    local_experts = w_gate.shape[0]
    slot_count = received.shape[1]
    features = received.shape[2]
    grouped = received.reshape(peers, local_experts, slot_count, features)
    gate_part = jnp.einsum("nesd,edf->nesf", grouped, w_gate, preferred_element_type=jnp.float32)
    up_part = jnp.einsum("nesd,edf->nesf", grouped, w_up, preferred_element_type=jnp.float32)
    inner = (jax.nn.silu(gate_part) * up_part).astype(jnp.bfloat16)
    produced = jnp.einsum(
        "nesf,efd->nesd", inner, w_down, preferred_element_type=jnp.float32
    ).astype(jnp.bfloat16)
    return produced.reshape(peers * local_experts, slot_count, features)


def route_block(normed, picks, gate_weights, w_gate, w_up, w_down, capacity):
    rows_here = picks.shape[0]
    picks_here = picks.shape[1]
    experts_all = w_gate.shape[0] * node_size()
    features = normed.shape[1]
    flattened = picks.reshape(-1)
    expert_ids = jnp.arange(experts_all, dtype=jnp.int32)
    onehot = (flattened[:, None] == expert_ids[None, :]).astype(jnp.int32)
    earlier = jnp.cumsum(onehot, axis=0) - onehot
    slot_of = jnp.sum(earlier * onehot, axis=1)
    target = flattened * capacity + slot_of
    layout = jnp.arange(experts_all * capacity, dtype=jnp.int32)
    placed = jnp.sum(
        (layout[:, None, None] == target.reshape(rows_here, picks_here)[None, :, :]).astype(
            jnp.int32
        ),
        axis=2,
    )
    outgoing = jnp.dot(placed.astype(jnp.bfloat16), normed, preferred_element_type=jnp.float32)
    outgoing = outgoing.astype(jnp.bfloat16).reshape(experts_all, capacity, features)
    produced = expert_block(
        lax.all_to_all(outgoing, NODE, split_axis=0, concat_axis=0, tiled=True),
        w_gate,
        w_up,
        w_down,
    )
    returned = lax.all_to_all(produced, NODE, split_axis=0, concat_axis=0, tiled=True)
    gathered = jnp.take(returned.reshape(experts_all * capacity, features), target, axis=0)
    gathered = gathered.reshape(rows_here, picks_here, features)
    shares = gate_weights / jnp.sum(gate_weights, axis=1, keepdims=True)
    return jnp.einsum("tk,tkd->td", shares, gathered.astype(jnp.float32)).astype(jnp.bfloat16)


def spread_block(normed, picks, gate_weights, w_gate, w_up, w_down):
    chips = lax.axis_size("chip")
    cores = lax.axis_size("core")
    core = lax.axis_index("core")
    rows_here, features = normed.shape
    local_experts = w_gate.shape[0]
    peers = chips * cores
    experts_all = local_experts * peers
    spread = jnp.broadcast_to(normed[None], (chips, rows_here, features))
    same_core = lax.all_to_all(spread, "chip", 0, 0, tiled=True)
    other_core = lax.ppermute(same_core, "core", [(i, (i + 1) % cores) for i in range(cores)])
    both = jnp.stack([same_core, other_core, same_core], axis=1)
    ordered = lax.dynamic_slice_in_dim(both, core, cores, axis=1)
    every_row = ordered.reshape(peers * rows_here, features)
    produced = []
    for expert in range(local_experts):
        gate_part = jnp.dot(every_row, w_gate[expert], preferred_element_type=jnp.float32)
        up_part = jnp.dot(every_row, w_up[expert], preferred_element_type=jnp.float32)
        inner = (jax.nn.silu(gate_part) * up_part).astype(jnp.bfloat16)
        produced.append(
            jnp.dot(inner, w_down[expert], preferred_element_type=jnp.float32).astype(jnp.bfloat16)
        )
    produced = jnp.stack(produced, axis=0).reshape(local_experts, peers, rows_here, features)
    produced = produced.transpose(1, 0, 2, 3)
    returned = lax.all_to_all(produced, NODE, 0, 0, tiled=True)
    returned = returned.reshape(experts_all, rows_here, features)
    shares = gate_weights / jnp.sum(gate_weights, axis=1, keepdims=True)
    expert_ids = jnp.arange(experts_all, dtype=jnp.int32)
    chosen = picks[:, :, None] == expert_ids[None, None, :]
    dense_shares = jnp.sum(jnp.where(chosen, shares[:, :, None], 0.0), axis=1)
    picked = jnp.any(chosen, axis=1)
    weighted = jnp.where(
        picked.T[:, :, None], dense_shares.T[:, :, None] * returned.astype(jnp.float32), 0.0
    )
    return jnp.sum(weighted, axis=0).astype(jnp.bfloat16)


def attend(queries, keys, values, incoming_keys, incoming_values, lengths):
    request_rows = queries.shape[0]
    valid_length = keys.shape[1]
    query_groups = QUERY_HEADS // KEY_VALUE_HEADS
    score_scale = 1.0 / math.sqrt(HEAD_WIDTH)
    query_rows = queries.reshape(request_rows, KEY_VALUE_HEADS, query_groups, HEAD_WIDTH)
    stored_keys = keys.reshape(request_rows, valid_length, KEY_VALUE_HEADS, HEAD_WIDTH)
    stored_values = values.reshape(request_rows, valid_length, KEY_VALUE_HEADS, HEAD_WIDTH)
    scores = (
        jnp.einsum("rkgd,rlkd->rkgl", query_rows, stored_keys, preferred_element_type=jnp.float32)
        * score_scale
    )
    new_token_scores = (
        jnp.einsum(
            "behw,bew->beh",
            query_rows,
            incoming_keys.reshape(request_rows, KEY_VALUE_HEADS, HEAD_WIDTH),
            preferred_element_type=jnp.float32,
        )
        * score_scale
    )
    present = (jnp.arange(valid_length, dtype=jnp.int32)[None, :] < lengths[:, None])[
        :, None, None, :
    ]
    masked = jnp.where(present, scores, -1e30)
    highest = jnp.maximum(jnp.max(masked, axis=3), new_token_scores)
    raised = jnp.where(present, jnp.exp(masked - highest[..., None]), 0.0)
    fresh_raised = jnp.exp(new_token_scores - highest)
    denominator = jnp.sum(raised, axis=3) + fresh_raised
    probs = (raised / denominator[..., None]).astype(jnp.bfloat16)
    new_token_probability = (fresh_raised / denominator).astype(jnp.bfloat16)
    blended_output = jnp.einsum(
        "rkgl,rlkd->rkgd", probs, stored_values, preferred_element_type=jnp.float32
    )
    blended_output = blended_output + new_token_probability.astype(jnp.float32)[
        ..., None
    ] * incoming_values.reshape(request_rows, KEY_VALUE_HEADS, 1, HEAD_WIDTH).astype(jnp.float32)
    return blended_output.reshape(request_rows, QUERY_HEADS * HEAD_WIDTH).astype(jnp.bfloat16)


def on_device(
    states,
    norm_gain,
    picks,
    gate_weights,
    w_gate,
    w_up,
    w_down,
    queries,
    keys,
    values,
    incoming_keys,
    incoming_values,
    lengths,
):
    widened = states.astype(jnp.float32)
    meansq = jnp.mean(widened * widened, axis=1, keepdims=True) + 1e-06
    normed = (widened / jnp.sqrt(meansq) * norm_gain[None, :]).astype(jnp.bfloat16)
    experts_all = w_gate.shape[0] * node_size()
    capacity = min(TOK_DEV, max(2, 2 * TOK_DEV * TOPK // experts_all))
    gathered_rows = normed.shape[0] * node_size()
    if gathered_rows <= experts_all * capacity and lax.axis_size("core") == 2:
        moe_output = spread_block(normed, picks, gate_weights, w_gate, w_up, w_down)
    else:
        moe_output = route_block(normed, picks, gate_weights, w_gate, w_up, w_down, capacity)
    attention_output = attend(queries, keys, values, incoming_keys, incoming_values, lengths)
    return (moe_output, attention_output)


def solution(mesh):
    groups, peers = mesh.devices.shape
    cores = 2 if peers % 2 == 0 else 1
    fine = Mesh(mesh.devices.reshape(groups, peers // cores, cores), ("group", "chip", "core"))
    in_specs = (
        P(("group", "chip", "core"), None),
        P(),
        P(("group", "chip", "core"), None),
        P(("group", "chip", "core"), None),
        P(NODE, None, None),
        P(NODE, None, None),
        P(NODE, None, None),
        P(("group", "chip", "core"), None),
        P(("group", "chip", "core"), None, None),
        P(("group", "chip", "core"), None, None),
        P(("group", "chip", "core"), None),
        P(("group", "chip", "core"), None),
        P(("group", "chip", "core")),
    )
    out_specs = (P(("group", "chip", "core"), None), P(("group", "chip", "core"), None))
    return jax.shard_map(
        on_device, mesh=fine, in_specs=in_specs, out_specs=out_specs, check_vma=False
    )
```

```python
import math

import jax
import jax.numpy as jnp
from jax import lax
from jax.experimental import pallas as pl
from jax.experimental.pallas import tpu as pltpu
from jax.sharding import Mesh, PartitionSpec as P

QUERY_HEADS = 32
KEY_VALUE_HEADS = 4
HEAD_WIDTH = 128
TOPK = 8
TOK_DEV = 16
NODE = ("chip", "core")


def node_size():
    return lax.axis_size("chip") * lax.axis_size("core")


def node_index():
    return lax.axis_index("chip") * lax.axis_size("core") + lax.axis_index("core")


def expert_block(received, w_gate, w_up, w_down):
    peers = node_size()
    local_experts = w_gate.shape[0]
    slot_count = received.shape[1]
    features = received.shape[2]
    grouped = received.reshape(peers, local_experts, slot_count, features)
    gate_part = jnp.einsum("nesd,edf->nesf", grouped, w_gate, preferred_element_type=jnp.float32)
    up_part = jnp.einsum("nesd,edf->nesf", grouped, w_up, preferred_element_type=jnp.float32)
    inner = (jax.nn.silu(gate_part) * up_part).astype(jnp.bfloat16)
    produced = jnp.einsum(
        "nesf,efd->nesd", inner, w_down, preferred_element_type=jnp.float32
    ).astype(jnp.bfloat16)
    return produced.reshape(peers * local_experts, slot_count, features)


def route_block(normed, picks, gate_weights, w_gate, w_up, w_down, capacity):
    rows_here = picks.shape[0]
    picks_here = picks.shape[1]
    experts_all = w_gate.shape[0] * node_size()
    features = normed.shape[1]
    flattened = picks.reshape(-1)
    expert_ids = jnp.arange(experts_all, dtype=jnp.int32)
    onehot = (flattened[:, None] == expert_ids[None, :]).astype(jnp.int32)
    earlier = jnp.cumsum(onehot, axis=0) - onehot
    slot_of = jnp.sum(earlier * onehot, axis=1)
    target = flattened * capacity + slot_of
    layout = jnp.arange(experts_all * capacity, dtype=jnp.int32)
    placed = jnp.sum(
        (layout[:, None, None] == target.reshape(rows_here, picks_here)[None, :, :]).astype(
            jnp.int32
        ),
        axis=2,
    )
    outgoing = jnp.dot(placed.astype(jnp.bfloat16), normed, preferred_element_type=jnp.float32)
    outgoing = outgoing.astype(jnp.bfloat16).reshape(experts_all, capacity, features)
    produced = expert_block(
        lax.all_to_all(outgoing, NODE, split_axis=0, concat_axis=0, tiled=True),
        w_gate,
        w_up,
        w_down,
    )
    returned = lax.all_to_all(produced, NODE, split_axis=0, concat_axis=0, tiled=True)
    gathered = jnp.take(returned.reshape(experts_all * capacity, features), target, axis=0)
    gathered = gathered.reshape(rows_here, picks_here, features)
    shares = gate_weights / jnp.sum(gate_weights, axis=1, keepdims=True)
    return jnp.einsum("tk,tkd->td", shares, gathered.astype(jnp.float32)).astype(jnp.bfloat16)


def mlp_kernel(rows_ref, gate_ref, up_ref, down_ref, out_ref, acc_ref):
    step = pl.program_id(1)

    @pl.when(step == 0)
    def _():
        acc_ref[...] = jnp.zeros_like(acc_ref)

    rows = rows_ref[...]
    gate_part = jnp.dot(rows, gate_ref[...], preferred_element_type=jnp.float32)
    up_part = jnp.dot(rows, up_ref[...], preferred_element_type=jnp.float32)
    inner = (jax.nn.silu(gate_part) * up_part).astype(jnp.bfloat16)
    acc_ref[...] += jnp.dot(inner, down_ref[...], preferred_element_type=jnp.float32)

    @pl.when(step == pl.num_programs(1) - 1)
    def _():
        out_ref[...] = acc_ref[...].astype(out_ref.dtype)


def expert_mlp(every_row, w_gate, w_up, w_down):
    local_experts, features, hidden = w_gate.shape
    row_count = every_row.shape[0]
    chunk = 256 if hidden % 256 == 0 else hidden
    return pl.pallas_call(
        mlp_kernel,
        grid=(local_experts, hidden // chunk),
        in_specs=[
            pl.BlockSpec((row_count, features), lambda e, f: (0, 0)),
            pl.BlockSpec((None, features, chunk), lambda e, f: (e, 0, f)),
            pl.BlockSpec((None, features, chunk), lambda e, f: (e, 0, f)),
            pl.BlockSpec((None, chunk, features), lambda e, f: (e, f, 0)),
        ],
        out_specs=pl.BlockSpec((None, row_count, features), lambda e, f: (e, 0, 0)),
        out_shape=jax.ShapeDtypeStruct((local_experts, row_count, features), jnp.bfloat16),
        scratch_shapes=[pltpu.VMEM((row_count, features), jnp.float32)],
        compiler_params=pltpu.CompilerParams(
            dimension_semantics=("arbitrary", "arbitrary"), vmem_limit_bytes=48 * 1024 * 1024
        ),
    )(every_row, w_gate, w_up, w_down)


def spread_block(normed, picks, gate_weights, w_gate, w_up, w_down):
    chips = lax.axis_size("chip")
    cores = lax.axis_size("core")
    core = lax.axis_index("core")
    rows_here, features = normed.shape
    local_experts = w_gate.shape[0]
    peers = chips * cores
    experts_all = local_experts * peers
    spread = jnp.broadcast_to(normed[None], (chips, rows_here, features))
    same_core = lax.all_to_all(spread, "chip", 0, 0, tiled=True)
    other_core = lax.ppermute(same_core, "core", [(i, (i + 1) % cores) for i in range(cores)])
    both = jnp.stack([same_core, other_core, same_core], axis=1)
    ordered = lax.dynamic_slice_in_dim(both, core, cores, axis=1)
    every_row = ordered.reshape(peers * rows_here, features)
    produced = expert_mlp(every_row, w_gate, w_up, w_down)
    produced = produced.reshape(local_experts, peers, rows_here, features)
    produced = produced.transpose(1, 0, 2, 3)
    returned = lax.all_to_all(produced, NODE, 0, 0, tiled=True)
    returned = returned.reshape(experts_all, rows_here, features)
    shares = gate_weights / jnp.sum(gate_weights, axis=1, keepdims=True)
    expert_ids = jnp.arange(experts_all, dtype=jnp.int32)
    chosen = picks[:, :, None] == expert_ids[None, None, :]
    dense_shares = jnp.sum(jnp.where(chosen, shares[:, :, None], 0.0), axis=1)
    weighted = dense_shares.T[:, :, None] * returned.astype(jnp.float32)
    return jnp.sum(weighted, axis=0).astype(jnp.bfloat16)


def attend(queries, keys, values, incoming_keys, incoming_values, lengths):
    request_rows = queries.shape[0]
    valid_length = keys.shape[1]
    query_groups = QUERY_HEADS // KEY_VALUE_HEADS
    score_scale = 1.0 / math.sqrt(HEAD_WIDTH)
    query_rows = queries.reshape(request_rows, KEY_VALUE_HEADS, query_groups, HEAD_WIDTH)
    stored_keys = keys.reshape(request_rows, valid_length, KEY_VALUE_HEADS, HEAD_WIDTH)
    stored_values = values.reshape(request_rows, valid_length, KEY_VALUE_HEADS, HEAD_WIDTH)
    scores = (
        jnp.einsum("rkgd,rlkd->rkgl", query_rows, stored_keys, preferred_element_type=jnp.float32)
        * score_scale
    )
    new_token_scores = (
        jnp.einsum(
            "behw,bew->beh",
            query_rows,
            incoming_keys.reshape(request_rows, KEY_VALUE_HEADS, HEAD_WIDTH),
            preferred_element_type=jnp.float32,
        )
        * score_scale
    )
    present = (jnp.arange(valid_length, dtype=jnp.int32)[None, :] < lengths[:, None])[
        :, None, None, :
    ]
    masked = jnp.where(present, scores, -1e30)
    highest = jnp.maximum(jnp.max(masked, axis=3), new_token_scores)
    raised = jnp.where(present, jnp.exp(masked - highest[..., None]), 0.0)
    fresh_raised = jnp.exp(new_token_scores - highest)
    denominator = jnp.sum(raised, axis=3) + fresh_raised
    probs = (raised / denominator[..., None]).astype(jnp.bfloat16)
    new_token_probability = (fresh_raised / denominator).astype(jnp.bfloat16)
    blended_output = jnp.einsum(
        "rkgl,rlkd->rkgd", probs, stored_values, preferred_element_type=jnp.float32
    )
    blended_output = blended_output + new_token_probability.astype(jnp.float32)[
        ..., None
    ] * incoming_values.reshape(request_rows, KEY_VALUE_HEADS, 1, HEAD_WIDTH).astype(jnp.float32)
    return blended_output.reshape(request_rows, QUERY_HEADS * HEAD_WIDTH).astype(jnp.bfloat16)


def on_device(
    states,
    norm_gain,
    picks,
    gate_weights,
    w_gate,
    w_up,
    w_down,
    queries,
    keys,
    values,
    incoming_keys,
    incoming_values,
    lengths,
):
    widened = states.astype(jnp.float32)
    meansq = jnp.mean(widened * widened, axis=1, keepdims=True) + 1e-06
    normed = (widened / jnp.sqrt(meansq) * norm_gain[None, :]).astype(jnp.bfloat16)
    experts_all = w_gate.shape[0] * node_size()
    capacity = min(TOK_DEV, max(2, 2 * TOK_DEV * TOPK // experts_all))
    gathered_rows = normed.shape[0] * node_size()
    if gathered_rows <= experts_all * capacity and lax.axis_size("core") == 2:
        moe_output = spread_block(normed, picks, gate_weights, w_gate, w_up, w_down)
    else:
        moe_output = route_block(normed, picks, gate_weights, w_gate, w_up, w_down, capacity)
    attention_output = attend(queries, keys, values, incoming_keys, incoming_values, lengths)
    return (moe_output, attention_output)


def solution(mesh):
    groups, peers = mesh.devices.shape
    cores = 2 if peers % 2 == 0 else 1
    fine = Mesh(mesh.devices.reshape(groups, peers // cores, cores), ("group", "chip", "core"))
    in_specs = (
        P(("group", "chip", "core"), None),
        P(),
        P(("group", "chip", "core"), None),
        P(("group", "chip", "core"), None),
        P(NODE, None, None),
        P(NODE, None, None),
        P(NODE, None, None),
        P(("group", "chip", "core"), None),
        P(("group", "chip", "core"), None, None),
        P(("group", "chip", "core"), None, None),
        P(("group", "chip", "core"), None),
        P(("group", "chip", "core"), None),
        P(("group", "chip", "core")),
    )
    out_specs = (P(("group", "chip", "core"), None), P(("group", "chip", "core"), None))
    return jax.shard_map(
        on_device, mesh=fine, in_specs=in_specs, out_specs=out_specs, check_vma=False
    )
```

```python
import math

import jax
import jax.numpy as jnp
from jax import lax
from jax.experimental import pallas as pl
from jax.experimental.pallas import tpu as pltpu
from jax.sharding import Mesh, PartitionSpec as P

QUERY_HEADS = 32
KEY_VALUE_HEADS = 4
HEAD_WIDTH = 128
TOPK = 8
TOK_DEV = 16
NODE = ("chip", "core")


def node_size():
    return lax.axis_size("chip") * lax.axis_size("core")


def node_index():
    return lax.axis_index("chip") * lax.axis_size("core") + lax.axis_index("core")


def expert_block(received, w_gate, w_up, w_down):
    peers = node_size()
    local_experts = w_gate.shape[0]
    slot_count = received.shape[1]
    features = received.shape[2]
    grouped = received.reshape(peers, local_experts, slot_count, features)
    gate_part = jnp.einsum("nesd,edf->nesf", grouped, w_gate, preferred_element_type=jnp.float32)
    up_part = jnp.einsum("nesd,edf->nesf", grouped, w_up, preferred_element_type=jnp.float32)
    inner = (jax.nn.silu(gate_part) * up_part).astype(jnp.bfloat16)
    produced = jnp.einsum(
        "nesf,efd->nesd", inner, w_down, preferred_element_type=jnp.float32
    ).astype(jnp.bfloat16)
    return produced.reshape(peers * local_experts, slot_count, features)


def route_block(normed, picks, gate_weights, w_gate, w_up, w_down, capacity):
    rows_here = picks.shape[0]
    picks_here = picks.shape[1]
    experts_all = w_gate.shape[0] * node_size()
    features = normed.shape[1]
    flattened = picks.reshape(-1)
    expert_ids = jnp.arange(experts_all, dtype=jnp.int32)
    onehot = (flattened[:, None] == expert_ids[None, :]).astype(jnp.int32)
    earlier = jnp.cumsum(onehot, axis=0) - onehot
    slot_of = jnp.sum(earlier * onehot, axis=1)
    target = flattened * capacity + slot_of
    layout = jnp.arange(experts_all * capacity, dtype=jnp.int32)
    placed = jnp.sum(
        (layout[:, None, None] == target.reshape(rows_here, picks_here)[None, :, :]).astype(
            jnp.int32
        ),
        axis=2,
    )
    outgoing = jnp.dot(placed.astype(jnp.bfloat16), normed, preferred_element_type=jnp.float32)
    outgoing = outgoing.astype(jnp.bfloat16).reshape(experts_all, capacity, features)
    produced = expert_block(
        lax.all_to_all(outgoing, NODE, split_axis=0, concat_axis=0, tiled=True),
        w_gate,
        w_up,
        w_down,
    )
    returned = lax.all_to_all(produced, NODE, split_axis=0, concat_axis=0, tiled=True)
    gathered = jnp.take(returned.reshape(experts_all * capacity, features), target, axis=0)
    gathered = gathered.reshape(rows_here, picks_here, features)
    shares = gate_weights / jnp.sum(gate_weights, axis=1, keepdims=True)
    return jnp.einsum("tk,tkd->td", shares, gathered.astype(jnp.float32)).astype(jnp.bfloat16)


def mlp_kernel(rows_ref, gate_ref, up_ref, down_ref, out_ref, acc_ref):
    step = pl.program_id(1)

    @pl.when(step == 0)
    def _():
        acc_ref[...] = jnp.zeros_like(acc_ref)

    rows = rows_ref[...]
    gate_part = jnp.dot(rows, gate_ref[...], preferred_element_type=jnp.float32)
    up_part = jnp.dot(rows, up_ref[...], preferred_element_type=jnp.float32)
    inner = (jax.nn.silu(gate_part) * up_part).astype(jnp.bfloat16)
    acc_ref[...] += jnp.dot(inner, down_ref[...], preferred_element_type=jnp.float32)

    @pl.when(step == pl.num_programs(1) - 1)
    def _():
        out_ref[...] = acc_ref[...].astype(out_ref.dtype)


def expert_mlp(every_row, w_gate, w_up, w_down):
    local_experts, features, hidden = w_gate.shape
    row_count = every_row.shape[0]
    chunk = 256 if hidden % 256 == 0 else hidden
    return pl.pallas_call(
        mlp_kernel,
        grid=(local_experts, hidden // chunk),
        in_specs=[
            pl.BlockSpec((row_count, features), lambda e, f: (0, 0)),
            pl.BlockSpec((None, features, chunk), lambda e, f: (e, 0, f)),
            pl.BlockSpec((None, features, chunk), lambda e, f: (e, 0, f)),
            pl.BlockSpec((None, chunk, features), lambda e, f: (e, f, 0)),
        ],
        out_specs=pl.BlockSpec((None, row_count, features), lambda e, f: (e, 0, 0)),
        out_shape=jax.ShapeDtypeStruct((local_experts, row_count, features), jnp.bfloat16),
        scratch_shapes=[pltpu.VMEM((row_count, features), jnp.float32)],
        compiler_params=pltpu.CompilerParams(
            dimension_semantics=("arbitrary", "arbitrary"), vmem_limit_bytes=48 * 1024 * 1024
        ),
    )(every_row, w_gate, w_up, w_down)


def spread_block(normed, picks, gate_weights, w_gate, w_up, w_down):
    chips = lax.axis_size("chip")
    cores = lax.axis_size("core")
    chip = lax.axis_index("chip")
    core = lax.axis_index("core")
    rows_here, features = normed.shape
    local_experts = w_gate.shape[0]
    peers = chips * cores
    experts_all = local_experts * peers

    def shifted(block, shift):
        pairs = [(i, (i + shift) % chips) for i in range(chips)]
        return lax.ppermute(block, "chip", pairs)

    same_core = [normed] + [shifted(normed, shift) for shift in range(1, chips)]
    same_stack = jnp.stack(same_core, axis=0)
    other_stack = lax.ppermute(same_stack, "core", [(i, (i + 1) % cores) for i in range(cores)])
    every_row = jnp.concatenate([same_stack, other_stack], axis=0).reshape(
        peers * rows_here, features
    )
    produced = expert_mlp(every_row, w_gate, w_up, w_down)
    produced = produced.reshape(local_experts, cores, chips, rows_here, features)
    returned_same = [produced[:, 0, 0]]
    for shift in range(1, chips):
        returned_same.append(shifted(produced[:, 0, shift], chips - shift))
    returned_other = []
    for shift in range(chips):
        pairs = [
            (c * cores + k, ((c - shift) % chips) * cores + (k + 1) % cores)
            for c in range(chips)
            for k in range(cores)
        ]
        returned_other.append(lax.ppermute(produced[:, 1, shift], NODE, pairs))
    returned = jnp.stack(returned_same + returned_other, axis=0)
    shifts = jnp.arange(chips, dtype=jnp.int32)
    source_chip = (chip + shifts) % chips
    source_node = jnp.concatenate(
        [source_chip * cores + core, source_chip * cores + (core + 1) % cores]
    )
    source_expert = (
        source_node[:, None] * local_experts + jnp.arange(local_experts, dtype=jnp.int32)[None, :]
    )
    shares = gate_weights / jnp.sum(gate_weights, axis=1, keepdims=True)
    chosen = picks[:, :, None] == source_expert.reshape(-1)[None, None, :]
    block_shares = jnp.sum(jnp.where(chosen, shares[:, :, None], 0.0), axis=1)
    block_shares = block_shares.T.reshape(peers, local_experts, rows_here)
    weighted = block_shares[:, :, :, None] * returned.astype(jnp.float32)
    return jnp.sum(weighted, axis=(0, 1)).astype(jnp.bfloat16)

def attend(queries, keys, values, incoming_keys, incoming_values, lengths):
    request_rows = queries.shape[0]
    valid_length = keys.shape[1]
    query_groups = QUERY_HEADS // KEY_VALUE_HEADS
    score_scale = 1.0 / math.sqrt(HEAD_WIDTH)
    query_rows = queries.reshape(request_rows, KEY_VALUE_HEADS, query_groups, HEAD_WIDTH)
    stored_keys = keys.reshape(request_rows, valid_length, KEY_VALUE_HEADS, HEAD_WIDTH)
    stored_values = values.reshape(request_rows, valid_length, KEY_VALUE_HEADS, HEAD_WIDTH)
    scores = (
        jnp.einsum("rkgd,rlkd->rkgl", query_rows, stored_keys, preferred_element_type=jnp.float32)
        * score_scale
    )
    new_token_scores = (
        jnp.einsum(
            "behw,bew->beh",
            query_rows,
            incoming_keys.reshape(request_rows, KEY_VALUE_HEADS, HEAD_WIDTH),
            preferred_element_type=jnp.float32,
        )
        * score_scale
    )
    present = (jnp.arange(valid_length, dtype=jnp.int32)[None, :] < lengths[:, None])[
        :, None, None, :
    ]
    masked = jnp.where(present, scores, -1e30)
    highest = jnp.maximum(jnp.max(masked, axis=3), new_token_scores)
    raised = jnp.where(present, jnp.exp(masked - highest[..., None]), 0.0)
    fresh_raised = jnp.exp(new_token_scores - highest)
    denominator = jnp.sum(raised, axis=3) + fresh_raised
    probs = (raised / denominator[..., None]).astype(jnp.bfloat16)
    new_token_probability = (fresh_raised / denominator).astype(jnp.bfloat16)
    blended_output = jnp.einsum(
        "rkgl,rlkd->rkgd", probs, stored_values, preferred_element_type=jnp.float32
    )
    blended_output = blended_output + new_token_probability.astype(jnp.float32)[
        ..., None
    ] * incoming_values.reshape(request_rows, KEY_VALUE_HEADS, 1, HEAD_WIDTH).astype(jnp.float32)
    return blended_output.reshape(request_rows, QUERY_HEADS * HEAD_WIDTH).astype(jnp.bfloat16)


def on_device(
    states,
    norm_gain,
    picks,
    gate_weights,
    w_gate,
    w_up,
    w_down,
    queries,
    keys,
    values,
    incoming_keys,
    incoming_values,
    lengths,
):
    widened = states.astype(jnp.float32)
    meansq = jnp.mean(widened * widened, axis=1, keepdims=True) + 1e-06
    normed = (widened / jnp.sqrt(meansq) * norm_gain[None, :]).astype(jnp.bfloat16)
    experts_all = w_gate.shape[0] * node_size()
    capacity = min(TOK_DEV, max(2, 2 * TOK_DEV * TOPK // experts_all))
    gathered_rows = normed.shape[0] * node_size()
    if gathered_rows <= experts_all * capacity and lax.axis_size("core") == 2:
        moe_output = spread_block(normed, picks, gate_weights, w_gate, w_up, w_down)
    else:
        moe_output = route_block(normed, picks, gate_weights, w_gate, w_up, w_down, capacity)
    attention_output = attend(queries, keys, values, incoming_keys, incoming_values, lengths)
    return (moe_output, attention_output)


def solution(mesh):
    groups, peers = mesh.devices.shape
    cores = 2 if peers % 2 == 0 else 1
    fine = Mesh(mesh.devices.reshape(groups, peers // cores, cores), ("group", "chip", "core"))
    in_specs = (
        P(("group", "chip", "core"), None),
        P(),
        P(("group", "chip", "core"), None),
        P(("group", "chip", "core"), None),
        P(NODE, None, None),
        P(NODE, None, None),
        P(NODE, None, None),
        P(("group", "chip", "core"), None),
        P(("group", "chip", "core"), None, None),
        P(("group", "chip", "core"), None, None),
        P(("group", "chip", "core"), None),
        P(("group", "chip", "core"), None),
        P(("group", "chip", "core")),
    )
    out_specs = (P(("group", "chip", "core"), None), P(("group", "chip", "core"), None))
    return jax.shard_map(
        on_device, mesh=fine, in_specs=in_specs, out_specs=out_specs, check_vma=False
    )
```

```python
import math

import jax
import jax.numpy as jnp
from jax import lax
from jax.experimental import pallas as pl
from jax.experimental.pallas import tpu as pltpu
from jax.sharding import Mesh, PartitionSpec as P

QUERY_HEADS = 32
KEY_VALUE_HEADS = 4
HEAD_WIDTH = 128
TOPK = 8
TOK_DEV = 16
NODE = ("chip", "core")


def node_size():
    return lax.axis_size("chip") * lax.axis_size("core")


def node_index():
    return lax.axis_index("chip") * lax.axis_size("core") + lax.axis_index("core")


def expert_block(received, w_gate, w_up, w_down):
    peers = node_size()
    local_experts = w_gate.shape[0]
    slot_count = received.shape[1]
    features = received.shape[2]
    grouped = received.reshape(peers, local_experts, slot_count, features)
    gate_part = jnp.einsum("nesd,edf->nesf", grouped, w_gate, preferred_element_type=jnp.float32)
    up_part = jnp.einsum("nesd,edf->nesf", grouped, w_up, preferred_element_type=jnp.float32)
    inner = (jax.nn.silu(gate_part) * up_part).astype(jnp.bfloat16)
    produced = jnp.einsum(
        "nesf,efd->nesd", inner, w_down, preferred_element_type=jnp.float32
    ).astype(jnp.bfloat16)
    return produced.reshape(peers * local_experts, slot_count, features)


def route_block(normed, picks, gate_weights, w_gate, w_up, w_down, capacity):
    rows_here = picks.shape[0]
    picks_here = picks.shape[1]
    experts_all = w_gate.shape[0] * node_size()
    features = normed.shape[1]
    flattened = picks.reshape(-1)
    expert_ids = jnp.arange(experts_all, dtype=jnp.int32)
    onehot = (flattened[:, None] == expert_ids[None, :]).astype(jnp.int32)
    earlier = jnp.cumsum(onehot, axis=0) - onehot
    slot_of = jnp.sum(earlier * onehot, axis=1)
    target = flattened * capacity + slot_of
    layout = jnp.arange(experts_all * capacity, dtype=jnp.int32)
    placed = jnp.sum(
        (layout[:, None, None] == target.reshape(rows_here, picks_here)[None, :, :]).astype(
            jnp.int32
        ),
        axis=2,
    )
    outgoing = jnp.dot(placed.astype(jnp.bfloat16), normed, preferred_element_type=jnp.float32)
    outgoing = outgoing.astype(jnp.bfloat16).reshape(experts_all, capacity, features)
    produced = expert_block(
        lax.all_to_all(outgoing, NODE, split_axis=0, concat_axis=0, tiled=True),
        w_gate,
        w_up,
        w_down,
    )
    returned = lax.all_to_all(produced, NODE, split_axis=0, concat_axis=0, tiled=True)
    gathered = jnp.take(returned.reshape(experts_all * capacity, features), target, axis=0)
    gathered = gathered.reshape(rows_here, picks_here, features)
    shares = gate_weights / jnp.sum(gate_weights, axis=1, keepdims=True)
    return jnp.einsum("tk,tkd->td", shares, gathered.astype(jnp.float32)).astype(jnp.bfloat16)


def mlp_kernel(core_ref, same_ref, other_ref, gate_ref, up_ref, down_ref, out_ref, acc_ref):
    step = pl.program_id(1)
    half = same_ref.shape[0]

    @pl.when(step == 0)
    def _():
        acc_ref[...] = jnp.zeros_like(acc_ref)

    gate_block = gate_ref[...]
    up_block = up_ref[...]
    down_block = down_ref[...]
    for part, rows_ref in enumerate((same_ref, other_ref)):
        rows = rows_ref[...]
        gate_part = jnp.dot(rows, gate_block, preferred_element_type=jnp.float32)
        up_part = jnp.dot(rows, up_block, preferred_element_type=jnp.float32)
        inner = (jax.nn.silu(gate_part) * up_part).astype(jnp.bfloat16)
        acc_ref[part * half : (part + 1) * half, :] += jnp.dot(
            inner, down_block, preferred_element_type=jnp.float32
        )

    @pl.when(step == pl.num_programs(1) - 1)
    def _():
        core = core_ref[0]
        out_ref[core] = acc_ref[0:half, :].astype(out_ref.dtype)
        out_ref[1 - core] = acc_ref[half : 2 * half, :].astype(out_ref.dtype)


def expert_mlp(core, same_rows, other_rows, w_gate, w_up, w_down):
    local_experts, features, hidden = w_gate.shape
    half = same_rows.shape[0]
    chunk = 256 if hidden % 256 == 0 else hidden
    grid_spec = pltpu.PrefetchScalarGridSpec(
        num_scalar_prefetch=1,
        grid=(local_experts, hidden // chunk),
        in_specs=[
            pl.BlockSpec((half, features), lambda e, f, c: (0, 0)),
            pl.BlockSpec((half, features), lambda e, f, c: (0, 0)),
            pl.BlockSpec((None, features, chunk), lambda e, f, c: (e, 0, f)),
            pl.BlockSpec((None, features, chunk), lambda e, f, c: (e, 0, f)),
            pl.BlockSpec((None, chunk, features), lambda e, f, c: (e, f, 0)),
        ],
        out_specs=pl.BlockSpec((None, 2, half, features), lambda e, f, c: (e, 0, 0, 0)),
        scratch_shapes=[pltpu.VMEM((2 * half, features), jnp.float32)],
    )
    return pl.pallas_call(
        mlp_kernel,
        grid_spec=grid_spec,
        out_shape=jax.ShapeDtypeStruct((local_experts, 2, half, features), jnp.bfloat16),
        compiler_params=pltpu.CompilerParams(
            dimension_semantics=("arbitrary", "arbitrary"), vmem_limit_bytes=48 * 1024 * 1024
        ),
    )(core.reshape(1), same_rows, other_rows, w_gate, w_up, w_down)


def spread_block(normed, picks, gate_weights, w_gate, w_up, w_down):
    chips = lax.axis_size("chip")
    cores = lax.axis_size("core")
    core = lax.axis_index("core")
    rows_here, features = normed.shape
    local_experts = w_gate.shape[0]
    peers = chips * cores
    experts_all = local_experts * peers
    spread = jnp.broadcast_to(normed[None], (chips, rows_here, features))
    same_core = lax.all_to_all(spread, "chip", 0, 0, tiled=True)
    other_core = lax.ppermute(same_core, "core", [(i, (i + 1) % cores) for i in range(cores)])
    produced = expert_mlp(
        core.astype(jnp.int32),
        same_core.reshape(chips * rows_here, features),
        other_core.reshape(chips * rows_here, features),
        w_gate,
        w_up,
        w_down,
    )
    produced = produced.reshape(local_experts, peers, rows_here, features)
    produced = produced.transpose(1, 0, 2, 3)
    returned = lax.all_to_all(produced, ("core", "chip"), 0, 0, tiled=True)
    blocks = jnp.arange(peers, dtype=jnp.int32)
    source_node = (blocks % chips) * cores + blocks // chips
    source_expert = (
        source_node[:, None] * local_experts + jnp.arange(local_experts, dtype=jnp.int32)[None, :]
    ).reshape(-1)
    returned = returned.reshape(experts_all, rows_here, features)
    shares = gate_weights / jnp.sum(gate_weights, axis=1, keepdims=True)
    chosen = picks[:, :, None] == source_expert[None, None, :]
    block_shares = jnp.sum(jnp.where(chosen, shares[:, :, None], 0.0), axis=1)
    weighted = block_shares.T[:, :, None] * returned.astype(jnp.float32)
    return jnp.sum(weighted, axis=0).astype(jnp.bfloat16)

def attend(queries, keys, values, incoming_keys, incoming_values, lengths):
    request_rows = queries.shape[0]
    valid_length = keys.shape[1]
    query_groups = QUERY_HEADS // KEY_VALUE_HEADS
    score_scale = 1.0 / math.sqrt(HEAD_WIDTH)
    query_rows = queries.reshape(request_rows, KEY_VALUE_HEADS, query_groups, HEAD_WIDTH)
    stored_keys = keys.reshape(request_rows, valid_length, KEY_VALUE_HEADS, HEAD_WIDTH)
    stored_values = values.reshape(request_rows, valid_length, KEY_VALUE_HEADS, HEAD_WIDTH)
    scores = (
        jnp.einsum("rkgd,rlkd->rkgl", query_rows, stored_keys, preferred_element_type=jnp.float32)
        * score_scale
    )
    new_token_scores = (
        jnp.einsum(
            "behw,bew->beh",
            query_rows,
            incoming_keys.reshape(request_rows, KEY_VALUE_HEADS, HEAD_WIDTH),
            preferred_element_type=jnp.float32,
        )
        * score_scale
    )
    present = (jnp.arange(valid_length, dtype=jnp.int32)[None, :] < lengths[:, None])[
        :, None, None, :
    ]
    masked = jnp.where(present, scores, -1e30)
    highest = jnp.maximum(jnp.max(masked, axis=3), new_token_scores)
    raised = jnp.where(present, jnp.exp(masked - highest[..., None]), 0.0)
    fresh_raised = jnp.exp(new_token_scores - highest)
    denominator = jnp.sum(raised, axis=3) + fresh_raised
    probs = (raised / denominator[..., None]).astype(jnp.bfloat16)
    new_token_probability = (fresh_raised / denominator).astype(jnp.bfloat16)
    blended_output = jnp.einsum(
        "rkgl,rlkd->rkgd", probs, stored_values, preferred_element_type=jnp.float32
    )
    blended_output = blended_output + new_token_probability.astype(jnp.float32)[
        ..., None
    ] * incoming_values.reshape(request_rows, KEY_VALUE_HEADS, 1, HEAD_WIDTH).astype(jnp.float32)
    return blended_output.reshape(request_rows, QUERY_HEADS * HEAD_WIDTH).astype(jnp.bfloat16)


def on_device(
    states,
    norm_gain,
    picks,
    gate_weights,
    w_gate,
    w_up,
    w_down,
    queries,
    keys,
    values,
    incoming_keys,
    incoming_values,
    lengths,
):
    widened = states.astype(jnp.float32)
    meansq = jnp.mean(widened * widened, axis=1, keepdims=True) + 1e-06
    normed = (widened / jnp.sqrt(meansq) * norm_gain[None, :]).astype(jnp.bfloat16)
    experts_all = w_gate.shape[0] * node_size()
    capacity = min(TOK_DEV, max(2, 2 * TOK_DEV * TOPK // experts_all))
    gathered_rows = normed.shape[0] * node_size()
    if gathered_rows <= experts_all * capacity and lax.axis_size("core") == 2:
        moe_output = spread_block(normed, picks, gate_weights, w_gate, w_up, w_down)
    else:
        moe_output = route_block(normed, picks, gate_weights, w_gate, w_up, w_down, capacity)
    attention_output = attend(queries, keys, values, incoming_keys, incoming_values, lengths)
    return (moe_output, attention_output)


def solution(mesh):
    groups, peers = mesh.devices.shape
    cores = 2 if peers % 2 == 0 else 1
    fine = Mesh(mesh.devices.reshape(groups, peers // cores, cores), ("group", "chip", "core"))
    in_specs = (
        P(("group", "chip", "core"), None),
        P(),
        P(("group", "chip", "core"), None),
        P(("group", "chip", "core"), None),
        P(NODE, None, None),
        P(NODE, None, None),
        P(NODE, None, None),
        P(("group", "chip", "core"), None),
        P(("group", "chip", "core"), None, None),
        P(("group", "chip", "core"), None, None),
        P(("group", "chip", "core"), None),
        P(("group", "chip", "core"), None),
        P(("group", "chip", "core")),
    )
    out_specs = (P(("group", "chip", "core"), None), P(("group", "chip", "core"), None))
    return jax.shard_map(
        on_device, mesh=fine, in_specs=in_specs, out_specs=out_specs, check_vma=False
    )
```

```python
import math

import jax
import jax.numpy as jnp
from jax import lax
from jax.experimental import pallas as pl
from jax.experimental.pallas import tpu as pltpu
from jax.sharding import Mesh, PartitionSpec as P

QUERY_HEADS = 32
KEY_VALUE_HEADS = 4
HEAD_WIDTH = 128
TOPK = 8
TOK_DEV = 16
NODE = ("chip", "core")


def node_size():
    return lax.axis_size("chip") * lax.axis_size("core")


def node_index():
    return lax.axis_index("chip") * lax.axis_size("core") + lax.axis_index("core")


def expert_block(received, w_gate, w_up, w_down):
    peers = node_size()
    local_experts = w_gate.shape[0]
    slot_count = received.shape[1]
    features = received.shape[2]
    grouped = received.reshape(peers, local_experts, slot_count, features)
    gate_part = jnp.einsum("nesd,edf->nesf", grouped, w_gate, preferred_element_type=jnp.float32)
    up_part = jnp.einsum("nesd,edf->nesf", grouped, w_up, preferred_element_type=jnp.float32)
    inner = (jax.nn.silu(gate_part) * up_part).astype(jnp.bfloat16)
    produced = jnp.einsum(
        "nesf,efd->nesd", inner, w_down, preferred_element_type=jnp.float32
    ).astype(jnp.bfloat16)
    return produced.reshape(peers * local_experts, slot_count, features)


def route_block(normed, picks, gate_weights, w_gate, w_up, w_down, capacity):
    rows_here = picks.shape[0]
    picks_here = picks.shape[1]
    experts_all = w_gate.shape[0] * node_size()
    features = normed.shape[1]
    flattened = picks.reshape(-1)
    expert_ids = jnp.arange(experts_all, dtype=jnp.int32)
    onehot = (flattened[:, None] == expert_ids[None, :]).astype(jnp.int32)
    earlier = jnp.cumsum(onehot, axis=0) - onehot
    slot_of = jnp.sum(earlier * onehot, axis=1)
    target = flattened * capacity + slot_of
    layout = jnp.arange(experts_all * capacity, dtype=jnp.int32)
    placed = jnp.sum(
        (layout[:, None, None] == target.reshape(rows_here, picks_here)[None, :, :]).astype(
            jnp.int32
        ),
        axis=2,
    )
    outgoing = jnp.dot(placed.astype(jnp.bfloat16), normed, preferred_element_type=jnp.float32)
    outgoing = outgoing.astype(jnp.bfloat16).reshape(experts_all, capacity, features)
    produced = expert_block(
        lax.all_to_all(outgoing, NODE, split_axis=0, concat_axis=0, tiled=True),
        w_gate,
        w_up,
        w_down,
    )
    returned = lax.all_to_all(produced, NODE, split_axis=0, concat_axis=0, tiled=True)
    gathered = jnp.take(returned.reshape(experts_all * capacity, features), target, axis=0)
    gathered = gathered.reshape(rows_here, picks_here, features)
    shares = gate_weights / jnp.sum(gate_weights, axis=1, keepdims=True)
    return jnp.einsum("tk,tkd->td", shares, gathered.astype(jnp.float32)).astype(jnp.bfloat16)


def mlp_kernel(
    core_ref, same_ref, other_ref, gate_hbm, up_hbm, down_hbm, out_ref,
    gate_buf, up_buf, down_buf, acc_ref, sems,
):
    expert = pl.program_id(0)
    chunks, _, chunk = gate_buf.shape
    chips = out_ref.shape[0]
    half = same_ref.shape[0]
    rows_here = half // chips
    copies = []
    for f in range(chunks):
        window = pl.ds(f * chunk, chunk)
        trio = (
            pltpu.make_async_copy(gate_hbm.at[expert, :, window], gate_buf.at[f], sems.at[0, f]),
            pltpu.make_async_copy(up_hbm.at[expert, :, window], up_buf.at[f], sems.at[1, f]),
            pltpu.make_async_copy(down_hbm.at[expert, window, :], down_buf.at[f], sems.at[2, f]),
        )
        for copy in trio:
            copy.start()
        copies.append(trio)
    for f in range(chunks):
        for copy in copies[f]:
            copy.wait()
        gate_block = gate_buf[f]
        up_block = up_buf[f]
        down_block = down_buf[f]
        for part, rows_ref in enumerate((same_ref, other_ref)):
            rows = rows_ref[...]
            gate_part = jnp.dot(rows, gate_block, preferred_element_type=jnp.float32)
            up_part = jnp.dot(rows, up_block, preferred_element_type=jnp.float32)
            inner = (jax.nn.silu(gate_part) * up_part).astype(jnp.bfloat16)
            produced = jnp.dot(inner, down_block, preferred_element_type=jnp.float32)
            if f == 0:
                acc_ref[part] = produced
            else:
                acc_ref[part] += produced
    core = core_ref[0]
    for part in range(2):
        target = (core + part) % 2
        out_ref[:, pl.ds(target, 1)] = (
            acc_ref[part].reshape(chips, 1, rows_here, -1).astype(out_ref.dtype)
        )


def expert_mlp(core, same_rows, other_rows, w_gate, w_up, w_down, chips):
    local_experts, features, hidden = w_gate.shape
    half = same_rows.shape[0]
    rows_here = half // chips
    chunk = 256 if hidden % 256 == 0 else hidden
    chunks = hidden // chunk
    grid_spec = pltpu.PrefetchScalarGridSpec(
        num_scalar_prefetch=1,
        grid=(local_experts,),
        in_specs=[
            pl.BlockSpec((half, features), lambda e, c: (0, 0)),
            pl.BlockSpec((half, features), lambda e, c: (0, 0)),
            pl.BlockSpec(memory_space=pl.ANY),
            pl.BlockSpec(memory_space=pl.ANY),
            pl.BlockSpec(memory_space=pl.ANY),
        ],
        out_specs=pl.BlockSpec(
            (None, chips, 2, rows_here, features), lambda e, c: (e, 0, 0, 0, 0)
        ),
        scratch_shapes=[
            pltpu.VMEM((chunks, features, chunk), jnp.bfloat16),
            pltpu.VMEM((chunks, features, chunk), jnp.bfloat16),
            pltpu.VMEM((chunks, chunk, features), jnp.bfloat16),
            pltpu.VMEM((2, half, features), jnp.float32),
            pltpu.SemaphoreType.DMA((3, chunks)),
        ],
    )
    return pl.pallas_call(
        mlp_kernel,
        grid_spec=grid_spec,
        out_shape=jax.ShapeDtypeStruct(
            (local_experts, chips, 2, rows_here, features), jnp.bfloat16
        ),
        compiler_params=pltpu.CompilerParams(
            dimension_semantics=("arbitrary",), vmem_limit_bytes=48 * 1024 * 1024
        ),
    )(core.reshape(1), same_rows, other_rows, w_gate, w_up, w_down)


def spread_block(normed, picks, gate_weights, w_gate, w_up, w_down):
    chips = lax.axis_size("chip")
    cores = lax.axis_size("core")
    core = lax.axis_index("core")
    rows_here, features = normed.shape
    local_experts = w_gate.shape[0]
    peers = chips * cores
    experts_all = local_experts * peers
    spread = jnp.broadcast_to(normed[None], (chips, rows_here, features))
    same_core = lax.all_to_all(spread, "chip", 0, 0, tiled=True)
    other_core = lax.ppermute(same_core, "core", [(i, (i + 1) % cores) for i in range(cores)])
    produced = expert_mlp(
        core.astype(jnp.int32),
        same_core.reshape(chips * rows_here, features),
        other_core.reshape(chips * rows_here, features),
        w_gate,
        w_up,
        w_down,
        chips,
    )
    produced = produced.reshape(local_experts, peers, rows_here, features)
    produced = produced.transpose(1, 0, 2, 3)
    returned = lax.all_to_all(produced, NODE, 0, 0, tiled=True)
    returned = returned.reshape(experts_all, rows_here, features)
    shares = gate_weights / jnp.sum(gate_weights, axis=1, keepdims=True)
    expert_ids = jnp.arange(experts_all, dtype=jnp.int32)
    chosen = picks[:, :, None] == expert_ids[None, None, :]
    dense_shares = jnp.sum(jnp.where(chosen, shares[:, :, None], 0.0), axis=1)
    weighted = dense_shares.T[:, :, None] * returned.astype(jnp.float32)
    return jnp.sum(weighted, axis=0).astype(jnp.bfloat16)

def attend(queries, keys, values, incoming_keys, incoming_values, lengths):
    request_rows = queries.shape[0]
    valid_length = keys.shape[1]
    query_groups = QUERY_HEADS // KEY_VALUE_HEADS
    score_scale = 1.0 / math.sqrt(HEAD_WIDTH)
    query_rows = queries.reshape(request_rows, KEY_VALUE_HEADS, query_groups, HEAD_WIDTH)
    stored_keys = keys.reshape(request_rows, valid_length, KEY_VALUE_HEADS, HEAD_WIDTH)
    stored_values = values.reshape(request_rows, valid_length, KEY_VALUE_HEADS, HEAD_WIDTH)
    scores = (
        jnp.einsum("rkgd,rlkd->rkgl", query_rows, stored_keys, preferred_element_type=jnp.float32)
        * score_scale
    )
    new_token_scores = (
        jnp.einsum(
            "behw,bew->beh",
            query_rows,
            incoming_keys.reshape(request_rows, KEY_VALUE_HEADS, HEAD_WIDTH),
            preferred_element_type=jnp.float32,
        )
        * score_scale
    )
    present = (jnp.arange(valid_length, dtype=jnp.int32)[None, :] < lengths[:, None])[
        :, None, None, :
    ]
    masked = jnp.where(present, scores, -1e30)
    highest = jnp.maximum(jnp.max(masked, axis=3), new_token_scores)
    raised = jnp.where(present, jnp.exp(masked - highest[..., None]), 0.0)
    fresh_raised = jnp.exp(new_token_scores - highest)
    denominator = jnp.sum(raised, axis=3) + fresh_raised
    probs = (raised / denominator[..., None]).astype(jnp.bfloat16)
    new_token_probability = (fresh_raised / denominator).astype(jnp.bfloat16)
    blended_output = jnp.einsum(
        "rkgl,rlkd->rkgd", probs, stored_values, preferred_element_type=jnp.float32
    )
    blended_output = blended_output + new_token_probability.astype(jnp.float32)[
        ..., None
    ] * incoming_values.reshape(request_rows, KEY_VALUE_HEADS, 1, HEAD_WIDTH).astype(jnp.float32)
    return blended_output.reshape(request_rows, QUERY_HEADS * HEAD_WIDTH).astype(jnp.bfloat16)


def on_device(
    states,
    norm_gain,
    picks,
    gate_weights,
    w_gate,
    w_up,
    w_down,
    queries,
    keys,
    values,
    incoming_keys,
    incoming_values,
    lengths,
):
    widened = states.astype(jnp.float32)
    meansq = jnp.mean(widened * widened, axis=1, keepdims=True) + 1e-06
    normed = (widened / jnp.sqrt(meansq) * norm_gain[None, :]).astype(jnp.bfloat16)
    experts_all = w_gate.shape[0] * node_size()
    capacity = min(TOK_DEV, max(2, 2 * TOK_DEV * TOPK // experts_all))
    gathered_rows = normed.shape[0] * node_size()
    if gathered_rows <= experts_all * capacity and lax.axis_size("core") == 2:
        moe_output = spread_block(normed, picks, gate_weights, w_gate, w_up, w_down)
    else:
        moe_output = route_block(normed, picks, gate_weights, w_gate, w_up, w_down, capacity)
    attention_output = attend(queries, keys, values, incoming_keys, incoming_values, lengths)
    return (moe_output, attention_output)


def solution(mesh):
    groups, peers = mesh.devices.shape
    cores = 2 if peers % 2 == 0 else 1
    fine = Mesh(mesh.devices.reshape(groups, peers // cores, cores), ("group", "chip", "core"))
    in_specs = (
        P(("group", "chip", "core"), None),
        P(),
        P(("group", "chip", "core"), None),
        P(("group", "chip", "core"), None),
        P(NODE, None, None),
        P(NODE, None, None),
        P(NODE, None, None),
        P(("group", "chip", "core"), None),
        P(("group", "chip", "core"), None, None),
        P(("group", "chip", "core"), None, None),
        P(("group", "chip", "core"), None),
        P(("group", "chip", "core"), None),
        P(("group", "chip", "core")),
    )
    out_specs = (P(("group", "chip", "core"), None), P(("group", "chip", "core"), None))
    return jax.shard_map(
        on_device, mesh=fine, in_specs=in_specs, out_specs=out_specs, check_vma=False
    )
```

```python
import math

import jax
import jax.numpy as jnp
from jax import lax
from jax.experimental import pallas as pl
from jax.experimental.pallas import tpu as pltpu
from jax.sharding import Mesh, PartitionSpec as P

QUERY_HEADS = 32
KEY_VALUE_HEADS = 4
HEAD_WIDTH = 128
TOPK = 8
TOK_DEV = 16
NODE = ("chip", "core")


def node_size():
    return lax.axis_size("chip") * lax.axis_size("core")


def node_index():
    return lax.axis_index("chip") * lax.axis_size("core") + lax.axis_index("core")


def expert_block(received, w_gate, w_up, w_down):
    peers = node_size()
    local_experts = w_gate.shape[0]
    slot_count = received.shape[1]
    features = received.shape[2]
    grouped = received.reshape(peers, local_experts, slot_count, features)
    gate_part = jnp.einsum("nesd,edf->nesf", grouped, w_gate, preferred_element_type=jnp.float32)
    up_part = jnp.einsum("nesd,edf->nesf", grouped, w_up, preferred_element_type=jnp.float32)
    inner = (jax.nn.silu(gate_part) * up_part).astype(jnp.bfloat16)
    produced = jnp.einsum(
        "nesf,efd->nesd", inner, w_down, preferred_element_type=jnp.float32
    ).astype(jnp.bfloat16)
    return produced.reshape(peers * local_experts, slot_count, features)


def route_block(normed, picks, gate_weights, w_gate, w_up, w_down, capacity):
    rows_here = picks.shape[0]
    picks_here = picks.shape[1]
    experts_all = w_gate.shape[0] * node_size()
    features = normed.shape[1]
    flattened = picks.reshape(-1)
    expert_ids = jnp.arange(experts_all, dtype=jnp.int32)
    onehot = (flattened[:, None] == expert_ids[None, :]).astype(jnp.int32)
    earlier = jnp.cumsum(onehot, axis=0) - onehot
    slot_of = jnp.sum(earlier * onehot, axis=1)
    target = flattened * capacity + slot_of
    layout = jnp.arange(experts_all * capacity, dtype=jnp.int32)
    placed = jnp.sum(
        (layout[:, None, None] == target.reshape(rows_here, picks_here)[None, :, :]).astype(
            jnp.int32
        ),
        axis=2,
    )
    outgoing = jnp.dot(placed.astype(jnp.bfloat16), normed, preferred_element_type=jnp.float32)
    outgoing = outgoing.astype(jnp.bfloat16).reshape(experts_all, capacity, features)
    produced = expert_block(
        lax.all_to_all(outgoing, NODE, split_axis=0, concat_axis=0, tiled=True),
        w_gate,
        w_up,
        w_down,
    )
    returned = lax.all_to_all(produced, NODE, split_axis=0, concat_axis=0, tiled=True)
    gathered = jnp.take(returned.reshape(experts_all * capacity, features), target, axis=0)
    gathered = gathered.reshape(rows_here, picks_here, features)
    shares = gate_weights / jnp.sum(gate_weights, axis=1, keepdims=True)
    return jnp.einsum("tk,tkd->td", shares, gathered.astype(jnp.float32)).astype(jnp.bfloat16)


def mlp_kernel(
    core_ref, same_ref, other_ref, gate_hbm, up_hbm, down_hbm, out_ref,
    gate_buf, up_buf, down_buf, inner_buf, sems,
):
    expert = pl.program_id(0)
    chunks, _, chunk = gate_buf.shape
    chips = out_ref.shape[0]
    half = same_ref.shape[0]
    rows_here = half // chips
    copies = []
    for f in range(chunks):
        window = pl.ds(f * chunk, chunk)
        pair = (
            pltpu.make_async_copy(gate_hbm.at[expert, :, window], gate_buf.at[f], sems.at[0, f]),
            pltpu.make_async_copy(up_hbm.at[expert, :, window], up_buf.at[f], sems.at[1, f]),
        )
        for copy in pair:
            copy.start()
        copies.append(pair)
    down_copy = pltpu.make_async_copy(down_hbm.at[expert], down_buf, sems.at[2, 0])
    down_copy.start()
    for f in range(chunks):
        for copy in copies[f]:
            copy.wait()
        gate_block = gate_buf[f]
        up_block = up_buf[f]
        for part, rows_ref in enumerate((same_ref, other_ref)):
            rows = rows_ref[...]
            gate_part = jnp.dot(rows, gate_block, preferred_element_type=jnp.float32)
            up_part = jnp.dot(rows, up_block, preferred_element_type=jnp.float32)
            inner_buf[part, :, f * chunk : (f + 1) * chunk] = (
                jax.nn.silu(gate_part) * up_part
            ).astype(jnp.bfloat16)
    down_copy.wait()
    down_block = down_buf[...]
    core = core_ref[0]
    for part in range(2):
        produced = jnp.dot(inner_buf[part], down_block, preferred_element_type=jnp.float32)
        target = (core + part) % 2
        out_ref[:, pl.ds(target, 1)] = (
            produced.reshape(chips, 1, rows_here, -1).astype(out_ref.dtype)
        )


def expert_mlp(core, same_rows, other_rows, w_gate, w_up, w_down, chips):
    local_experts, features, hidden = w_gate.shape
    half = same_rows.shape[0]
    rows_here = half // chips
    chunk = 256 if hidden % 256 == 0 else hidden
    chunks = hidden // chunk
    grid_spec = pltpu.PrefetchScalarGridSpec(
        num_scalar_prefetch=1,
        grid=(local_experts,),
        in_specs=[
            pl.BlockSpec((half, features), lambda e, c: (0, 0)),
            pl.BlockSpec((half, features), lambda e, c: (0, 0)),
            pl.BlockSpec(memory_space=pltpu.HBM),
            pl.BlockSpec(memory_space=pltpu.HBM),
            pl.BlockSpec(memory_space=pltpu.HBM),
        ],
        out_specs=pl.BlockSpec(
            (None, chips, 2, rows_here, features), lambda e, c: (e, 0, 0, 0, 0)
        ),
        scratch_shapes=[
            pltpu.VMEM((chunks, features, chunk), jnp.bfloat16),
            pltpu.VMEM((chunks, features, chunk), jnp.bfloat16),
            pltpu.VMEM((hidden, features), jnp.bfloat16),
            pltpu.VMEM((2, half, hidden), jnp.bfloat16),
            pltpu.SemaphoreType.DMA((3, chunks)),
        ],
    )
    return pl.pallas_call(
        mlp_kernel,
        grid_spec=grid_spec,
        out_shape=jax.ShapeDtypeStruct(
            (local_experts, chips, 2, rows_here, features), jnp.bfloat16
        ),
        compiler_params=pltpu.CompilerParams(
            dimension_semantics=("arbitrary",), vmem_limit_bytes=48 * 1024 * 1024
        ),
    )(core.reshape(1), same_rows, other_rows, w_gate, w_up, w_down)


def spread_block(normed, picks, gate_weights, w_gate, w_up, w_down):
    chips = lax.axis_size("chip")
    cores = lax.axis_size("core")
    core = lax.axis_index("core")
    rows_here, features = normed.shape
    local_experts = w_gate.shape[0]
    peers = chips * cores
    experts_all = local_experts * peers
    spread = jnp.broadcast_to(normed[None], (chips, rows_here, features))
    same_core = lax.all_to_all(spread, "chip", 0, 0, tiled=True)
    other_core = lax.ppermute(same_core, "core", [(i, (i + 1) % cores) for i in range(cores)])
    produced = expert_mlp(
        core.astype(jnp.int32),
        same_core.reshape(chips * rows_here, features),
        other_core.reshape(chips * rows_here, features),
        w_gate,
        w_up,
        w_down,
        chips,
    )
    produced = produced.reshape(local_experts, peers, rows_here, features)
    produced = produced.transpose(1, 0, 2, 3)
    returned = lax.all_to_all(produced, NODE, 0, 0, tiled=True)
    returned = returned.reshape(experts_all, rows_here, features)
    shares = gate_weights / jnp.sum(gate_weights, axis=1, keepdims=True)
    expert_ids = jnp.arange(experts_all, dtype=jnp.int32)
    chosen = picks[:, :, None] == expert_ids[None, None, :]
    dense_shares = jnp.sum(jnp.where(chosen, shares[:, :, None], 0.0), axis=1)
    weighted = dense_shares.T[:, :, None] * returned.astype(jnp.float32)
    return jnp.sum(weighted, axis=0).astype(jnp.bfloat16)

def attend(queries, keys, values, incoming_keys, incoming_values, lengths):
    request_rows = queries.shape[0]
    valid_length = keys.shape[1]
    query_groups = QUERY_HEADS // KEY_VALUE_HEADS
    score_scale = 1.0 / math.sqrt(HEAD_WIDTH)
    query_rows = queries.reshape(request_rows, KEY_VALUE_HEADS, query_groups, HEAD_WIDTH)
    stored_keys = keys.reshape(request_rows, valid_length, KEY_VALUE_HEADS, HEAD_WIDTH)
    stored_values = values.reshape(request_rows, valid_length, KEY_VALUE_HEADS, HEAD_WIDTH)
    scores = (
        jnp.einsum("rkgd,rlkd->rkgl", query_rows, stored_keys, preferred_element_type=jnp.float32)
        * score_scale
    )
    new_token_scores = (
        jnp.einsum(
            "behw,bew->beh",
            query_rows,
            incoming_keys.reshape(request_rows, KEY_VALUE_HEADS, HEAD_WIDTH),
            preferred_element_type=jnp.float32,
        )
        * score_scale
    )
    present = (jnp.arange(valid_length, dtype=jnp.int32)[None, :] < lengths[:, None])[
        :, None, None, :
    ]
    masked = jnp.where(present, scores, -1e30)
    highest = jnp.maximum(jnp.max(masked, axis=3), new_token_scores)
    raised = jnp.where(present, jnp.exp(masked - highest[..., None]), 0.0)
    fresh_raised = jnp.exp(new_token_scores - highest)
    denominator = jnp.sum(raised, axis=3) + fresh_raised
    probs = (raised / denominator[..., None]).astype(jnp.bfloat16)
    new_token_probability = (fresh_raised / denominator).astype(jnp.bfloat16)
    blended_output = jnp.einsum(
        "rkgl,rlkd->rkgd", probs, stored_values, preferred_element_type=jnp.float32
    )
    blended_output = blended_output + new_token_probability.astype(jnp.float32)[
        ..., None
    ] * incoming_values.reshape(request_rows, KEY_VALUE_HEADS, 1, HEAD_WIDTH).astype(jnp.float32)
    return blended_output.reshape(request_rows, QUERY_HEADS * HEAD_WIDTH).astype(jnp.bfloat16)


def on_device(
    states,
    norm_gain,
    picks,
    gate_weights,
    w_gate,
    w_up,
    w_down,
    queries,
    keys,
    values,
    incoming_keys,
    incoming_values,
    lengths,
):
    widened = states.astype(jnp.float32)
    meansq = jnp.mean(widened * widened, axis=1, keepdims=True) + 1e-06
    normed = (widened / jnp.sqrt(meansq) * norm_gain[None, :]).astype(jnp.bfloat16)
    experts_all = w_gate.shape[0] * node_size()
    capacity = min(TOK_DEV, max(2, 2 * TOK_DEV * TOPK // experts_all))
    gathered_rows = normed.shape[0] * node_size()
    if gathered_rows <= experts_all * capacity and lax.axis_size("core") == 2:
        moe_output = spread_block(normed, picks, gate_weights, w_gate, w_up, w_down)
    else:
        moe_output = route_block(normed, picks, gate_weights, w_gate, w_up, w_down, capacity)
    attention_output = attend(queries, keys, values, incoming_keys, incoming_values, lengths)
    return (moe_output, attention_output)


def solution(mesh):
    groups, peers = mesh.devices.shape
    cores = 2 if peers % 2 == 0 else 1
    fine = Mesh(mesh.devices.reshape(groups, peers // cores, cores), ("group", "chip", "core"))
    in_specs = (
        P(("group", "chip", "core"), None),
        P(),
        P(("group", "chip", "core"), None),
        P(("group", "chip", "core"), None),
        P(NODE, None, None),
        P(NODE, None, None),
        P(NODE, None, None),
        P(("group", "chip", "core"), None),
        P(("group", "chip", "core"), None, None),
        P(("group", "chip", "core"), None, None),
        P(("group", "chip", "core"), None),
        P(("group", "chip", "core"), None),
        P(("group", "chip", "core")),
    )
    out_specs = (P(("group", "chip", "core"), None), P(("group", "chip", "core"), None))
    return jax.shard_map(
        on_device, mesh=fine, in_specs=in_specs, out_specs=out_specs, check_vma=False
    )
```

```python
import math

import jax
import jax.numpy as jnp
from jax import lax
from jax.experimental import pallas as pl
from jax.experimental.pallas import tpu as pltpu
from jax.sharding import Mesh, PartitionSpec as P

QUERY_HEADS = 32
KEY_VALUE_HEADS = 4
HEAD_WIDTH = 128
TOPK = 8
TOK_DEV = 16
NODE = ("chip", "core")


def node_size():
    return lax.axis_size("chip") * lax.axis_size("core")


def node_index():
    return lax.axis_index("chip") * lax.axis_size("core") + lax.axis_index("core")


def expert_block(received, w_gate, w_up, w_down):
    peers = node_size()
    local_experts = w_gate.shape[0]
    slot_count = received.shape[1]
    features = received.shape[2]
    grouped = received.reshape(peers, local_experts, slot_count, features)
    gate_part = jnp.einsum("nesd,edf->nesf", grouped, w_gate, preferred_element_type=jnp.float32)
    up_part = jnp.einsum("nesd,edf->nesf", grouped, w_up, preferred_element_type=jnp.float32)
    inner = (jax.nn.silu(gate_part) * up_part).astype(jnp.bfloat16)
    produced = jnp.einsum(
        "nesf,efd->nesd", inner, w_down, preferred_element_type=jnp.float32
    ).astype(jnp.bfloat16)
    return produced.reshape(peers * local_experts, slot_count, features)


def route_block(normed, picks, gate_weights, w_gate, w_up, w_down, capacity):
    rows_here = picks.shape[0]
    picks_here = picks.shape[1]
    experts_all = w_gate.shape[0] * node_size()
    features = normed.shape[1]
    flattened = picks.reshape(-1)
    expert_ids = jnp.arange(experts_all, dtype=jnp.int32)
    onehot = (flattened[:, None] == expert_ids[None, :]).astype(jnp.int32)
    earlier = jnp.cumsum(onehot, axis=0) - onehot
    slot_of = jnp.sum(earlier * onehot, axis=1)
    target = flattened * capacity + slot_of
    layout = jnp.arange(experts_all * capacity, dtype=jnp.int32)
    placed = jnp.sum(
        (layout[:, None, None] == target.reshape(rows_here, picks_here)[None, :, :]).astype(
            jnp.int32
        ),
        axis=2,
    )
    outgoing = jnp.dot(placed.astype(jnp.bfloat16), normed, preferred_element_type=jnp.float32)
    outgoing = outgoing.astype(jnp.bfloat16).reshape(experts_all, capacity, features)
    produced = expert_block(
        lax.all_to_all(outgoing, NODE, split_axis=0, concat_axis=0, tiled=True),
        w_gate,
        w_up,
        w_down,
    )
    returned = lax.all_to_all(produced, NODE, split_axis=0, concat_axis=0, tiled=True)
    gathered = jnp.take(returned.reshape(experts_all * capacity, features), target, axis=0)
    gathered = gathered.reshape(rows_here, picks_here, features)
    shares = gate_weights / jnp.sum(gate_weights, axis=1, keepdims=True)
    return jnp.einsum("tk,tkd->td", shares, gathered.astype(jnp.float32)).astype(jnp.bfloat16)


def mlp_kernel(
    core_ref, same_ref, other_ref, gate_hbm, up_hbm, down_hbm, out_ref,
    gate_buf, up_buf, down_buf, inner_buf, sems,
):
    expert = pl.program_id(0)
    chunks, _, chunk = gate_buf.shape
    chips = out_ref.shape[0]
    half = same_ref.shape[0]
    rows_here = half // chips
    copies = []
    for f in range(chunks):
        window = pl.ds(f * chunk, chunk)
        pair = (
            pltpu.make_async_copy(gate_hbm.at[expert, :, window], gate_buf.at[f], sems.at[0, f]),
            pltpu.make_async_copy(up_hbm.at[expert, :, window], up_buf.at[f], sems.at[1, f]),
        )
        for copy in pair:
            copy.start()
        copies.append(pair)
    down_copy = pltpu.make_async_copy(down_hbm.at[expert], down_buf, sems.at[2, 0])
    down_copy.start()
    for f in range(chunks):
        for copy in copies[f]:
            copy.wait()
        gate_block = gate_buf[f]
        up_block = up_buf[f]
        for part, rows_ref in enumerate((same_ref, other_ref)):
            rows = rows_ref[...]
            gate_part = jnp.dot(rows, gate_block, preferred_element_type=jnp.float32)
            up_part = jnp.dot(rows, up_block, preferred_element_type=jnp.float32)
            inner_buf[part, :, f * chunk : (f + 1) * chunk] = (
                jax.nn.silu(gate_part) * up_part
            ).astype(jnp.bfloat16)
    down_copy.wait()
    down_block = down_buf[...]
    core = core_ref[0]
    for part in range(2):
        produced = jnp.dot(inner_buf[part], down_block, preferred_element_type=jnp.float32)
        target = (core + part) % 2
        out_ref[:, pl.ds(target, 1)] = (
            produced.reshape(chips, 1, rows_here, -1).astype(out_ref.dtype)
        )


def expert_mlp(core, same_rows, other_rows, w_gate, w_up, w_down, chips):
    local_experts, features, hidden = w_gate.shape
    half = same_rows.shape[0]
    rows_here = half // chips
    chunk = 256 if hidden % 256 == 0 else hidden
    chunks = hidden // chunk
    grid_spec = pltpu.PrefetchScalarGridSpec(
        num_scalar_prefetch=1,
        grid=(local_experts,),
        in_specs=[
            pl.BlockSpec((half, features), lambda e, c: (0, 0)),
            pl.BlockSpec((half, features), lambda e, c: (0, 0)),
            pl.BlockSpec(memory_space=pltpu.HBM),
            pl.BlockSpec(memory_space=pltpu.HBM),
            pl.BlockSpec(memory_space=pltpu.HBM),
        ],
        out_specs=pl.BlockSpec(
            (None, chips, 2, rows_here, features), lambda e, c: (e, 0, 0, 0, 0)
        ),
        scratch_shapes=[
            pltpu.VMEM((chunks, features, chunk), jnp.bfloat16),
            pltpu.VMEM((chunks, features, chunk), jnp.bfloat16),
            pltpu.VMEM((hidden, features), jnp.bfloat16),
            pltpu.VMEM((2, half, hidden), jnp.bfloat16),
            pltpu.SemaphoreType.DMA((3, chunks)),
        ],
    )
    return pl.pallas_call(
        mlp_kernel,
        grid_spec=grid_spec,
        out_shape=jax.ShapeDtypeStruct(
            (local_experts, chips, 2, rows_here, features), jnp.bfloat16
        ),
        compiler_params=pltpu.CompilerParams(
            dimension_semantics=("arbitrary",), vmem_limit_bytes=50 * 1024 * 1024
        ),
    )(core.reshape(1), same_rows, other_rows, w_gate, w_up, w_down)


def spread_block(normed, picks, gate_weights, w_gate, w_up, w_down):
    chips = lax.axis_size("chip")
    cores = lax.axis_size("core")
    core = lax.axis_index("core")
    rows_here, features = normed.shape
    local_experts = w_gate.shape[0]
    peers = chips * cores
    experts_all = local_experts * peers
    spread = jnp.broadcast_to(normed[None], (chips, rows_here, features))
    same_core = lax.all_to_all(spread, "chip", 0, 0, tiled=True)
    other_core = lax.ppermute(same_core, "core", [(i, (i + 1) % cores) for i in range(cores)])
    produced = expert_mlp(
        core.astype(jnp.int32),
        same_core.reshape(chips * rows_here, features),
        other_core.reshape(chips * rows_here, features),
        w_gate,
        w_up,
        w_down,
        chips,
    )
    produced = produced.reshape(local_experts, peers, rows_here, features)
    produced = produced.transpose(1, 0, 2, 3)
    returned = lax.all_to_all(produced, NODE, 0, 0, tiled=True)
    returned = returned.reshape(experts_all, rows_here, features)
    shares = gate_weights / jnp.sum(gate_weights, axis=1, keepdims=True)
    expert_ids = jnp.arange(experts_all, dtype=jnp.int32)
    chosen = picks[:, :, None] == expert_ids[None, None, :]
    dense_shares = jnp.sum(jnp.where(chosen, shares[:, :, None], 0.0), axis=1)
    weighted = dense_shares.T[:, :, None] * returned.astype(jnp.float32)
    return jnp.sum(weighted, axis=0).astype(jnp.bfloat16)

def attend(queries, keys, values, incoming_keys, incoming_values, lengths):
    request_rows = queries.shape[0]
    valid_length = keys.shape[1]
    query_groups = QUERY_HEADS // KEY_VALUE_HEADS
    score_scale = 1.0 / math.sqrt(HEAD_WIDTH)
    query_rows = queries.reshape(request_rows, KEY_VALUE_HEADS, query_groups, HEAD_WIDTH)
    stored_keys = keys.reshape(request_rows, valid_length, KEY_VALUE_HEADS, HEAD_WIDTH)
    stored_values = values.reshape(request_rows, valid_length, KEY_VALUE_HEADS, HEAD_WIDTH)
    scores = (
        jnp.einsum("rkgd,rlkd->rkgl", query_rows, stored_keys, preferred_element_type=jnp.float32)
        * score_scale
    )
    new_token_scores = (
        jnp.einsum(
            "behw,bew->beh",
            query_rows,
            incoming_keys.reshape(request_rows, KEY_VALUE_HEADS, HEAD_WIDTH),
            preferred_element_type=jnp.float32,
        )
        * score_scale
    )
    present = (jnp.arange(valid_length, dtype=jnp.int32)[None, :] < lengths[:, None])[
        :, None, None, :
    ]
    masked = jnp.where(present, scores, -1e30)
    highest = jnp.maximum(jnp.max(masked, axis=3), new_token_scores)
    raised = jnp.where(present, jnp.exp(masked - highest[..., None]), 0.0)
    fresh_raised = jnp.exp(new_token_scores - highest)
    denominator = jnp.sum(raised, axis=3) + fresh_raised
    probs = (raised / denominator[..., None]).astype(jnp.bfloat16)
    new_token_probability = (fresh_raised / denominator).astype(jnp.bfloat16)
    blended_output = jnp.einsum(
        "rkgl,rlkd->rkgd", probs, stored_values, preferred_element_type=jnp.float32
    )
    blended_output = blended_output + new_token_probability.astype(jnp.float32)[
        ..., None
    ] * incoming_values.reshape(request_rows, KEY_VALUE_HEADS, 1, HEAD_WIDTH).astype(jnp.float32)
    return blended_output.reshape(request_rows, QUERY_HEADS * HEAD_WIDTH).astype(jnp.bfloat16)


def on_device(
    states,
    norm_gain,
    picks,
    gate_weights,
    w_gate,
    w_up,
    w_down,
    queries,
    keys,
    values,
    incoming_keys,
    incoming_values,
    lengths,
):
    widened = states.astype(jnp.float32)
    meansq = jnp.mean(widened * widened, axis=1, keepdims=True) + 1e-06
    normed = (widened / jnp.sqrt(meansq) * norm_gain[None, :]).astype(jnp.bfloat16)
    experts_all = w_gate.shape[0] * node_size()
    capacity = min(TOK_DEV, max(2, 2 * TOK_DEV * TOPK // experts_all))
    gathered_rows = normed.shape[0] * node_size()
    if gathered_rows <= experts_all * capacity and lax.axis_size("core") == 2:
        moe_output = spread_block(normed, picks, gate_weights, w_gate, w_up, w_down)
    else:
        moe_output = route_block(normed, picks, gate_weights, w_gate, w_up, w_down, capacity)
    attention_output = attend(queries, keys, values, incoming_keys, incoming_values, lengths)
    return (moe_output, attention_output)


def solution(mesh):
    groups, peers = mesh.devices.shape
    cores = 2 if peers % 2 == 0 else 1
    fine = Mesh(mesh.devices.reshape(groups, peers // cores, cores), ("group", "chip", "core"))
    in_specs = (
        P(("group", "chip", "core"), None),
        P(),
        P(("group", "chip", "core"), None),
        P(("group", "chip", "core"), None),
        P(NODE, None, None),
        P(NODE, None, None),
        P(NODE, None, None),
        P(("group", "chip", "core"), None),
        P(("group", "chip", "core"), None, None),
        P(("group", "chip", "core"), None, None),
        P(("group", "chip", "core"), None),
        P(("group", "chip", "core"), None),
        P(("group", "chip", "core")),
    )
    out_specs = (P(("group", "chip", "core"), None), P(("group", "chip", "core"), None))
    return jax.shard_map(
        on_device, mesh=fine, in_specs=in_specs, out_specs=out_specs, check_vma=False
    )
```

```python
import math

import jax
import jax.numpy as jnp
from jax import lax
from jax.experimental import pallas as pl
from jax.experimental.pallas import tpu as pltpu
from jax.sharding import Mesh, PartitionSpec as P

QUERY_HEADS = 32
KEY_VALUE_HEADS = 4
HEAD_WIDTH = 128
TOPK = 8
TOK_DEV = 16
NODE = ("chip", "core")


def node_size():
    return lax.axis_size("chip") * lax.axis_size("core")


def node_index():
    return lax.axis_index("chip") * lax.axis_size("core") + lax.axis_index("core")


def expert_block(received, w_gate, w_up, w_down):
    peers = node_size()
    local_experts = w_gate.shape[0]
    slot_count = received.shape[1]
    features = received.shape[2]
    grouped = received.reshape(peers, local_experts, slot_count, features)
    gate_part = jnp.einsum("nesd,edf->nesf", grouped, w_gate, preferred_element_type=jnp.float32)
    up_part = jnp.einsum("nesd,edf->nesf", grouped, w_up, preferred_element_type=jnp.float32)
    inner = (jax.nn.silu(gate_part) * up_part).astype(jnp.bfloat16)
    produced = jnp.einsum(
        "nesf,efd->nesd", inner, w_down, preferred_element_type=jnp.float32
    ).astype(jnp.bfloat16)
    return produced.reshape(peers * local_experts, slot_count, features)


def route_block(normed, picks, gate_weights, w_gate, w_up, w_down, capacity):
    rows_here = picks.shape[0]
    picks_here = picks.shape[1]
    experts_all = w_gate.shape[0] * node_size()
    features = normed.shape[1]
    flattened = picks.reshape(-1)
    expert_ids = jnp.arange(experts_all, dtype=jnp.int32)
    onehot = (flattened[:, None] == expert_ids[None, :]).astype(jnp.int32)
    earlier = jnp.cumsum(onehot, axis=0) - onehot
    slot_of = jnp.sum(earlier * onehot, axis=1)
    target = flattened * capacity + slot_of
    layout = jnp.arange(experts_all * capacity, dtype=jnp.int32)
    placed = jnp.sum(
        (layout[:, None, None] == target.reshape(rows_here, picks_here)[None, :, :]).astype(
            jnp.int32
        ),
        axis=2,
    )
    outgoing = jnp.dot(placed.astype(jnp.bfloat16), normed, preferred_element_type=jnp.float32)
    outgoing = outgoing.astype(jnp.bfloat16).reshape(experts_all, capacity, features)
    produced = expert_block(
        lax.all_to_all(outgoing, NODE, split_axis=0, concat_axis=0, tiled=True),
        w_gate,
        w_up,
        w_down,
    )
    returned = lax.all_to_all(produced, NODE, split_axis=0, concat_axis=0, tiled=True)
    gathered = jnp.take(returned.reshape(experts_all * capacity, features), target, axis=0)
    gathered = gathered.reshape(rows_here, picks_here, features)
    shares = gate_weights / jnp.sum(gate_weights, axis=1, keepdims=True)
    return jnp.einsum("tk,tkd->td", shares, gathered.astype(jnp.float32)).astype(jnp.bfloat16)


def mlp_kernel(
    core_ref, gain_ref, same_ref, other_ref, gate_hbm, up_hbm, down_hbm, out_ref,
    gate_buf, up_buf, down_buf, inner_buf, normed_buf, sems,
):
    expert = pl.program_id(0)
    chunks, _, chunk = gate_buf.shape
    chips = out_ref.shape[0]
    half = same_ref.shape[0]
    rows_here = half // chips
    copies = []
    for f in range(chunks):
        window = pl.ds(f * chunk, chunk)
        pair = (
            pltpu.make_async_copy(gate_hbm.at[expert, :, window], gate_buf.at[f], sems.at[0, f]),
            pltpu.make_async_copy(up_hbm.at[expert, :, window], up_buf.at[f], sems.at[1, f]),
        )
        for copy in pair:
            copy.start()
        copies.append(pair)
    down_copy = pltpu.make_async_copy(down_hbm.at[expert], down_buf, sems.at[2, 0])
    down_copy.start()
    gain = gain_ref[...]
    for part, rows_ref in enumerate((same_ref, other_ref)):
        widened = rows_ref[...].astype(jnp.float32)
        meansq = jnp.mean(widened * widened, axis=1, keepdims=True) + 1e-06
        normed_buf[part] = (widened / jnp.sqrt(meansq) * gain).astype(jnp.bfloat16)
    for f in range(chunks):
        for copy in copies[f]:
            copy.wait()
        gate_block = gate_buf[f]
        up_block = up_buf[f]
        for part in range(2):
            rows = normed_buf[part]
            gate_part = jnp.dot(rows, gate_block, preferred_element_type=jnp.float32)
            up_part = jnp.dot(rows, up_block, preferred_element_type=jnp.float32)
            inner_buf[part, :, f * chunk : (f + 1) * chunk] = (
                jax.nn.silu(gate_part) * up_part
            ).astype(jnp.bfloat16)
    down_copy.wait()
    down_block = down_buf[...]
    core = core_ref[0]
    for part in range(2):
        produced = jnp.dot(inner_buf[part], down_block, preferred_element_type=jnp.float32)
        target = (core + part) % 2
        out_ref[:, pl.ds(target, 1)] = (
            produced.reshape(chips, 1, rows_here, -1).astype(out_ref.dtype)
        )


def expert_mlp(core, norm_gain, same_rows, other_rows, w_gate, w_up, w_down, chips):
    local_experts, features, hidden = w_gate.shape
    half = same_rows.shape[0]
    rows_here = half // chips
    chunk = 256 if hidden % 256 == 0 else hidden
    chunks = hidden // chunk
    grid_spec = pltpu.PrefetchScalarGridSpec(
        num_scalar_prefetch=1,
        grid=(local_experts,),
        in_specs=[
            pl.BlockSpec((1, features), lambda e, c: (0, 0)),
            pl.BlockSpec((half, features), lambda e, c: (0, 0)),
            pl.BlockSpec((half, features), lambda e, c: (0, 0)),
            pl.BlockSpec(memory_space=pltpu.HBM),
            pl.BlockSpec(memory_space=pltpu.HBM),
            pl.BlockSpec(memory_space=pltpu.HBM),
        ],
        out_specs=pl.BlockSpec(
            (None, chips, 2, rows_here, features), lambda e, c: (e, 0, 0, 0, 0)
        ),
        scratch_shapes=[
            pltpu.VMEM((chunks, features, chunk), jnp.bfloat16),
            pltpu.VMEM((chunks, features, chunk), jnp.bfloat16),
            pltpu.VMEM((hidden, features), jnp.bfloat16),
            pltpu.VMEM((2, half, hidden), jnp.bfloat16),
            pltpu.VMEM((2, half, features), jnp.bfloat16),
            pltpu.SemaphoreType.DMA((3, chunks)),
        ],
    )
    return pl.pallas_call(
        mlp_kernel,
        grid_spec=grid_spec,
        out_shape=jax.ShapeDtypeStruct(
            (local_experts, chips, 2, rows_here, features), jnp.bfloat16
        ),
        compiler_params=pltpu.CompilerParams(
            dimension_semantics=("arbitrary",), vmem_limit_bytes=50 * 1024 * 1024
        ),
    )(core.reshape(1), norm_gain.reshape(1, -1), same_rows, other_rows, w_gate, w_up, w_down)


def spread_block(states, norm_gain, picks, gate_weights, w_gate, w_up, w_down):
    chips = lax.axis_size("chip")
    cores = lax.axis_size("core")
    core = lax.axis_index("core")
    rows_here, features = states.shape
    local_experts = w_gate.shape[0]
    peers = chips * cores
    experts_all = local_experts * peers
    spread = jnp.broadcast_to(states[None], (chips, rows_here, features))
    same_core = lax.all_to_all(spread, "chip", 0, 0, tiled=True)
    other_core = lax.ppermute(same_core, "core", [(i, (i + 1) % cores) for i in range(cores)])
    produced = expert_mlp(
        core.astype(jnp.int32),
        norm_gain,
        same_core.reshape(chips * rows_here, features),
        other_core.reshape(chips * rows_here, features),
        w_gate,
        w_up,
        w_down,
        chips,
    )
    produced = produced.reshape(local_experts, peers, rows_here, features)
    produced = produced.transpose(1, 0, 2, 3)
    returned = lax.all_to_all(produced, NODE, 0, 0, tiled=True)
    returned = returned.reshape(experts_all, rows_here, features)
    shares = gate_weights / jnp.sum(gate_weights, axis=1, keepdims=True)
    expert_ids = jnp.arange(experts_all, dtype=jnp.int32)
    chosen = picks[:, :, None] == expert_ids[None, None, :]
    dense_shares = jnp.sum(jnp.where(chosen, shares[:, :, None], 0.0), axis=1)
    weighted = dense_shares.T[:, :, None] * returned.astype(jnp.float32)
    return jnp.sum(weighted, axis=0).astype(jnp.bfloat16)

def attend(queries, keys, values, incoming_keys, incoming_values, lengths):
    request_rows = queries.shape[0]
    valid_length = keys.shape[1]
    query_groups = QUERY_HEADS // KEY_VALUE_HEADS
    score_scale = 1.0 / math.sqrt(HEAD_WIDTH)
    query_rows = queries.reshape(request_rows, KEY_VALUE_HEADS, query_groups, HEAD_WIDTH)
    stored_keys = keys.reshape(request_rows, valid_length, KEY_VALUE_HEADS, HEAD_WIDTH)
    stored_values = values.reshape(request_rows, valid_length, KEY_VALUE_HEADS, HEAD_WIDTH)
    scores = (
        jnp.einsum("rkgd,rlkd->rkgl", query_rows, stored_keys, preferred_element_type=jnp.float32)
        * score_scale
    )
    new_token_scores = (
        jnp.einsum(
            "behw,bew->beh",
            query_rows,
            incoming_keys.reshape(request_rows, KEY_VALUE_HEADS, HEAD_WIDTH),
            preferred_element_type=jnp.float32,
        )
        * score_scale
    )
    present = (jnp.arange(valid_length, dtype=jnp.int32)[None, :] < lengths[:, None])[
        :, None, None, :
    ]
    masked = jnp.where(present, scores, -1e30)
    highest = jnp.maximum(jnp.max(masked, axis=3), new_token_scores)
    raised = jnp.where(present, jnp.exp(masked - highest[..., None]), 0.0)
    fresh_raised = jnp.exp(new_token_scores - highest)
    denominator = jnp.sum(raised, axis=3) + fresh_raised
    probs = (raised / denominator[..., None]).astype(jnp.bfloat16)
    new_token_probability = (fresh_raised / denominator).astype(jnp.bfloat16)
    blended_output = jnp.einsum(
        "rkgl,rlkd->rkgd", probs, stored_values, preferred_element_type=jnp.float32
    )
    blended_output = blended_output + new_token_probability.astype(jnp.float32)[
        ..., None
    ] * incoming_values.reshape(request_rows, KEY_VALUE_HEADS, 1, HEAD_WIDTH).astype(jnp.float32)
    return blended_output.reshape(request_rows, QUERY_HEADS * HEAD_WIDTH).astype(jnp.bfloat16)


def on_device(
    states,
    norm_gain,
    picks,
    gate_weights,
    w_gate,
    w_up,
    w_down,
    queries,
    keys,
    values,
    incoming_keys,
    incoming_values,
    lengths,
):
    widened = states.astype(jnp.float32)
    meansq = jnp.mean(widened * widened, axis=1, keepdims=True) + 1e-06
    normed = (widened / jnp.sqrt(meansq) * norm_gain[None, :]).astype(jnp.bfloat16)
    experts_all = w_gate.shape[0] * node_size()
    capacity = min(TOK_DEV, max(2, 2 * TOK_DEV * TOPK // experts_all))
    gathered_rows = normed.shape[0] * node_size()
    if gathered_rows <= experts_all * capacity and lax.axis_size("core") == 2:
        moe_output = spread_block(states, norm_gain, picks, gate_weights, w_gate, w_up, w_down)
    else:
        moe_output = route_block(normed, picks, gate_weights, w_gate, w_up, w_down, capacity)
    attention_output = attend(queries, keys, values, incoming_keys, incoming_values, lengths)
    return (moe_output, attention_output)


def solution(mesh):
    groups, peers = mesh.devices.shape
    cores = 2 if peers % 2 == 0 else 1
    fine = Mesh(mesh.devices.reshape(groups, peers // cores, cores), ("group", "chip", "core"))
    in_specs = (
        P(("group", "chip", "core"), None),
        P(),
        P(("group", "chip", "core"), None),
        P(("group", "chip", "core"), None),
        P(NODE, None, None),
        P(NODE, None, None),
        P(NODE, None, None),
        P(("group", "chip", "core"), None),
        P(("group", "chip", "core"), None, None),
        P(("group", "chip", "core"), None, None),
        P(("group", "chip", "core"), None),
        P(("group", "chip", "core"), None),
        P(("group", "chip", "core")),
    )
    out_specs = (P(("group", "chip", "core"), None), P(("group", "chip", "core"), None))
    return jax.shard_map(
        on_device, mesh=fine, in_specs=in_specs, out_specs=out_specs, check_vma=False
    )
```

```python
import math

import jax
import jax.numpy as jnp
from jax import lax
from jax.experimental import pallas as pl
from jax.experimental.pallas import tpu as pltpu
from jax.sharding import Mesh, PartitionSpec as P

QUERY_HEADS = 32
KEY_VALUE_HEADS = 4
HEAD_WIDTH = 128
TOPK = 8
TOK_DEV = 16
NODE = ("chip", "core")


def node_size():
    return lax.axis_size("chip") * lax.axis_size("core")


def node_index():
    return lax.axis_index("chip") * lax.axis_size("core") + lax.axis_index("core")


def expert_block(received, w_gate, w_up, w_down):
    peers = node_size()
    local_experts = w_gate.shape[0]
    slot_count = received.shape[1]
    features = received.shape[2]
    grouped = received.reshape(peers, local_experts, slot_count, features)
    gate_part = jnp.einsum("nesd,edf->nesf", grouped, w_gate, preferred_element_type=jnp.float32)
    up_part = jnp.einsum("nesd,edf->nesf", grouped, w_up, preferred_element_type=jnp.float32)
    inner = (jax.nn.silu(gate_part) * up_part).astype(jnp.bfloat16)
    produced = jnp.einsum(
        "nesf,efd->nesd", inner, w_down, preferred_element_type=jnp.float32
    ).astype(jnp.bfloat16)
    return produced.reshape(peers * local_experts, slot_count, features)


def route_block(normed, picks, gate_weights, w_gate, w_up, w_down, capacity):
    rows_here = picks.shape[0]
    picks_here = picks.shape[1]
    experts_all = w_gate.shape[0] * node_size()
    features = normed.shape[1]
    flattened = picks.reshape(-1)
    expert_ids = jnp.arange(experts_all, dtype=jnp.int32)
    onehot = (flattened[:, None] == expert_ids[None, :]).astype(jnp.int32)
    earlier = jnp.cumsum(onehot, axis=0) - onehot
    slot_of = jnp.sum(earlier * onehot, axis=1)
    target = flattened * capacity + slot_of
    layout = jnp.arange(experts_all * capacity, dtype=jnp.int32)
    placed = jnp.sum(
        (layout[:, None, None] == target.reshape(rows_here, picks_here)[None, :, :]).astype(
            jnp.int32
        ),
        axis=2,
    )
    outgoing = jnp.dot(placed.astype(jnp.bfloat16), normed, preferred_element_type=jnp.float32)
    outgoing = outgoing.astype(jnp.bfloat16).reshape(experts_all, capacity, features)
    produced = expert_block(
        lax.all_to_all(outgoing, NODE, split_axis=0, concat_axis=0, tiled=True),
        w_gate,
        w_up,
        w_down,
    )
    returned = lax.all_to_all(produced, NODE, split_axis=0, concat_axis=0, tiled=True)
    gathered = jnp.take(returned.reshape(experts_all * capacity, features), target, axis=0)
    gathered = gathered.reshape(rows_here, picks_here, features)
    shares = gate_weights / jnp.sum(gate_weights, axis=1, keepdims=True)
    return jnp.einsum("tk,tkd->td", shares, gathered.astype(jnp.float32)).astype(jnp.bfloat16)


def mlp_kernel(
    core_ref, gain_ref, same_ref, other_ref, gate_hbm, up_hbm, down_hbm, out_ref,
    gate_buf, up_buf, down_buf, inner_buf, normed_buf, gain_buf, sems,
):
    expert = pl.program_id(0)
    chunks, _, chunk = gate_buf.shape
    chips = out_ref.shape[0]
    half = same_ref.shape[0]
    rows_here = half // chips
    gain_copy = pltpu.make_async_copy(gain_ref, gain_buf, sems.at[2, 1])
    gain_copy.start()
    copies = []
    for f in range(chunks):
        window = pl.ds(f * chunk, chunk)
        pair = (
            pltpu.make_async_copy(gate_hbm.at[expert, :, window], gate_buf.at[f], sems.at[0, f]),
            pltpu.make_async_copy(up_hbm.at[expert, :, window], up_buf.at[f], sems.at[1, f]),
        )
        for copy in pair:
            copy.start()
        copies.append(pair)
    down_copy = pltpu.make_async_copy(down_hbm.at[expert], down_buf, sems.at[2, 0])
    down_copy.start()
    gain_copy.wait()
    gain = gain_buf[...]
    for part, rows_ref in enumerate((same_ref, other_ref)):
        widened = rows_ref[...].astype(jnp.float32)
        meansq = jnp.mean(widened * widened, axis=1, keepdims=True) + 1e-06
        normed_buf[part] = (widened / jnp.sqrt(meansq) * gain).astype(jnp.bfloat16)
    for f in range(chunks):
        for copy in copies[f]:
            copy.wait()
        gate_block = gate_buf[f]
        up_block = up_buf[f]
        for part in range(2):
            rows = normed_buf[part]
            gate_part = jnp.dot(rows, gate_block, preferred_element_type=jnp.float32)
            up_part = jnp.dot(rows, up_block, preferred_element_type=jnp.float32)
            inner_buf[part, :, f * chunk : (f + 1) * chunk] = (
                jax.nn.silu(gate_part) * up_part
            ).astype(jnp.bfloat16)
    down_copy.wait()
    down_block = down_buf[...]
    core = core_ref[0]
    for part in range(2):
        produced = jnp.dot(inner_buf[part], down_block, preferred_element_type=jnp.float32)
        target = (core + part) % 2
        out_ref[:, pl.ds(target, 1)] = (
            produced.reshape(chips, 1, rows_here, -1).astype(out_ref.dtype)
        )


def expert_mlp(core, norm_gain, same_rows, other_rows, w_gate, w_up, w_down, chips):
    local_experts, features, hidden = w_gate.shape
    half = same_rows.shape[0]
    rows_here = half // chips
    chunk = 256 if hidden % 256 == 0 else hidden
    chunks = hidden // chunk
    grid_spec = pltpu.PrefetchScalarGridSpec(
        num_scalar_prefetch=1,
        grid=(local_experts,),
        in_specs=[
            pl.BlockSpec(memory_space=pltpu.HBM),
            pl.BlockSpec((half, features), lambda e, c: (0, 0)),
            pl.BlockSpec((half, features), lambda e, c: (0, 0)),
            pl.BlockSpec(memory_space=pltpu.HBM),
            pl.BlockSpec(memory_space=pltpu.HBM),
            pl.BlockSpec(memory_space=pltpu.HBM),
        ],
        out_specs=pl.BlockSpec(
            (None, chips, 2, rows_here, features), lambda e, c: (e, 0, 0, 0, 0)
        ),
        scratch_shapes=[
            pltpu.VMEM((chunks, features, chunk), jnp.bfloat16),
            pltpu.VMEM((chunks, features, chunk), jnp.bfloat16),
            pltpu.VMEM((hidden, features), jnp.bfloat16),
            pltpu.VMEM((2, half, hidden), jnp.bfloat16),
            pltpu.VMEM((2, half, features), jnp.bfloat16),
            pltpu.VMEM((1, features), jnp.float32),
            pltpu.SemaphoreType.DMA((3, max(chunks, 2))),
        ],
    )
    return pl.pallas_call(
        mlp_kernel,
        grid_spec=grid_spec,
        out_shape=jax.ShapeDtypeStruct(
            (local_experts, chips, 2, rows_here, features), jnp.bfloat16
        ),
        compiler_params=pltpu.CompilerParams(
            dimension_semantics=("arbitrary",), vmem_limit_bytes=50 * 1024 * 1024
        ),
    )(core.reshape(1), norm_gain.reshape(1, -1), same_rows, other_rows, w_gate, w_up, w_down)


def spread_block(states, norm_gain, picks, gate_weights, w_gate, w_up, w_down):
    chips = lax.axis_size("chip")
    cores = lax.axis_size("core")
    core = lax.axis_index("core")
    rows_here, features = states.shape
    local_experts = w_gate.shape[0]
    peers = chips * cores
    experts_all = local_experts * peers
    spread = jnp.broadcast_to(states[None], (chips, rows_here, features))
    same_core = lax.all_to_all(spread, "chip", 0, 0, tiled=True)
    other_core = lax.ppermute(same_core, "core", [(i, (i + 1) % cores) for i in range(cores)])
    produced = expert_mlp(
        core.astype(jnp.int32),
        norm_gain,
        same_core.reshape(chips * rows_here, features),
        other_core.reshape(chips * rows_here, features),
        w_gate,
        w_up,
        w_down,
        chips,
    )
    produced = produced.reshape(local_experts, peers, rows_here, features)
    produced = produced.transpose(1, 0, 2, 3)
    returned = lax.all_to_all(produced, NODE, 0, 0, tiled=True)
    returned = returned.reshape(experts_all, rows_here, features)
    shares = gate_weights / jnp.sum(gate_weights, axis=1, keepdims=True)
    expert_ids = jnp.arange(experts_all, dtype=jnp.int32)
    chosen = picks[:, :, None] == expert_ids[None, None, :]
    dense_shares = jnp.sum(jnp.where(chosen, shares[:, :, None], 0.0), axis=1)
    weighted = dense_shares.T[:, :, None] * returned.astype(jnp.float32)
    return jnp.sum(weighted, axis=0).astype(jnp.bfloat16)

def attend(queries, keys, values, incoming_keys, incoming_values, lengths):
    request_rows = queries.shape[0]
    valid_length = keys.shape[1]
    query_groups = QUERY_HEADS // KEY_VALUE_HEADS
    score_scale = 1.0 / math.sqrt(HEAD_WIDTH)
    query_rows = queries.reshape(request_rows, KEY_VALUE_HEADS, query_groups, HEAD_WIDTH)
    stored_keys = keys.reshape(request_rows, valid_length, KEY_VALUE_HEADS, HEAD_WIDTH)
    stored_values = values.reshape(request_rows, valid_length, KEY_VALUE_HEADS, HEAD_WIDTH)
    scores = (
        jnp.einsum("rkgd,rlkd->rkgl", query_rows, stored_keys, preferred_element_type=jnp.float32)
        * score_scale
    )
    new_token_scores = (
        jnp.einsum(
            "behw,bew->beh",
            query_rows,
            incoming_keys.reshape(request_rows, KEY_VALUE_HEADS, HEAD_WIDTH),
            preferred_element_type=jnp.float32,
        )
        * score_scale
    )
    present = (jnp.arange(valid_length, dtype=jnp.int32)[None, :] < lengths[:, None])[
        :, None, None, :
    ]
    masked = jnp.where(present, scores, -1e30)
    highest = jnp.maximum(jnp.max(masked, axis=3), new_token_scores)
    raised = jnp.where(present, jnp.exp(masked - highest[..., None]), 0.0)
    fresh_raised = jnp.exp(new_token_scores - highest)
    denominator = jnp.sum(raised, axis=3) + fresh_raised
    probs = (raised / denominator[..., None]).astype(jnp.bfloat16)
    new_token_probability = (fresh_raised / denominator).astype(jnp.bfloat16)
    blended_output = jnp.einsum(
        "rkgl,rlkd->rkgd", probs, stored_values, preferred_element_type=jnp.float32
    )
    blended_output = blended_output + new_token_probability.astype(jnp.float32)[
        ..., None
    ] * incoming_values.reshape(request_rows, KEY_VALUE_HEADS, 1, HEAD_WIDTH).astype(jnp.float32)
    return blended_output.reshape(request_rows, QUERY_HEADS * HEAD_WIDTH).astype(jnp.bfloat16)


def on_device(
    states,
    norm_gain,
    picks,
    gate_weights,
    w_gate,
    w_up,
    w_down,
    queries,
    keys,
    values,
    incoming_keys,
    incoming_values,
    lengths,
):
    widened = states.astype(jnp.float32)
    meansq = jnp.mean(widened * widened, axis=1, keepdims=True) + 1e-06
    normed = (widened / jnp.sqrt(meansq) * norm_gain[None, :]).astype(jnp.bfloat16)
    experts_all = w_gate.shape[0] * node_size()
    capacity = min(TOK_DEV, max(2, 2 * TOK_DEV * TOPK // experts_all))
    gathered_rows = normed.shape[0] * node_size()
    if gathered_rows <= experts_all * capacity and lax.axis_size("core") == 2:
        moe_output = spread_block(states, norm_gain, picks, gate_weights, w_gate, w_up, w_down)
    else:
        moe_output = route_block(normed, picks, gate_weights, w_gate, w_up, w_down, capacity)
    attention_output = attend(queries, keys, values, incoming_keys, incoming_values, lengths)
    return (moe_output, attention_output)


def solution(mesh):
    groups, peers = mesh.devices.shape
    cores = 2 if peers % 2 == 0 else 1
    fine = Mesh(mesh.devices.reshape(groups, peers // cores, cores), ("group", "chip", "core"))
    in_specs = (
        P(("group", "chip", "core"), None),
        P(),
        P(("group", "chip", "core"), None),
        P(("group", "chip", "core"), None),
        P(NODE, None, None),
        P(NODE, None, None),
        P(NODE, None, None),
        P(("group", "chip", "core"), None),
        P(("group", "chip", "core"), None, None),
        P(("group", "chip", "core"), None, None),
        P(("group", "chip", "core"), None),
        P(("group", "chip", "core"), None),
        P(("group", "chip", "core")),
    )
    out_specs = (P(("group", "chip", "core"), None), P(("group", "chip", "core"), None))
    return jax.shard_map(
        on_device, mesh=fine, in_specs=in_specs, out_specs=out_specs, check_vma=False
    )
```

```python
import math

import jax
import jax.numpy as jnp
from jax import lax
from jax.experimental import pallas as pl
from jax.experimental.pallas import tpu as pltpu
from jax.sharding import Mesh, PartitionSpec as P

QUERY_HEADS = 32
KEY_VALUE_HEADS = 4
HEAD_WIDTH = 128
TOPK = 8
TOK_DEV = 16
NODE = ("chip", "core")


def node_size():
    return lax.axis_size("chip") * lax.axis_size("core")


def node_index():
    return lax.axis_index("chip") * lax.axis_size("core") + lax.axis_index("core")


def expert_block(received, w_gate, w_up, w_down):
    peers = node_size()
    local_experts = w_gate.shape[0]
    slot_count = received.shape[1]
    features = received.shape[2]
    grouped = received.reshape(peers, local_experts, slot_count, features)
    gate_part = jnp.einsum("nesd,edf->nesf", grouped, w_gate, preferred_element_type=jnp.float32)
    up_part = jnp.einsum("nesd,edf->nesf", grouped, w_up, preferred_element_type=jnp.float32)
    inner = (jax.nn.silu(gate_part) * up_part).astype(jnp.bfloat16)
    produced = jnp.einsum(
        "nesf,efd->nesd", inner, w_down, preferred_element_type=jnp.float32
    ).astype(jnp.bfloat16)
    return produced.reshape(peers * local_experts, slot_count, features)


def route_block(normed, picks, gate_weights, w_gate, w_up, w_down, capacity):
    rows_here = picks.shape[0]
    picks_here = picks.shape[1]
    experts_all = w_gate.shape[0] * node_size()
    features = normed.shape[1]
    flattened = picks.reshape(-1)
    expert_ids = jnp.arange(experts_all, dtype=jnp.int32)
    onehot = (flattened[:, None] == expert_ids[None, :]).astype(jnp.int32)
    earlier = jnp.cumsum(onehot, axis=0) - onehot
    slot_of = jnp.sum(earlier * onehot, axis=1)
    target = flattened * capacity + slot_of
    layout = jnp.arange(experts_all * capacity, dtype=jnp.int32)
    placed = jnp.sum(
        (layout[:, None, None] == target.reshape(rows_here, picks_here)[None, :, :]).astype(
            jnp.int32
        ),
        axis=2,
    )
    outgoing = jnp.dot(placed.astype(jnp.bfloat16), normed, preferred_element_type=jnp.float32)
    outgoing = outgoing.astype(jnp.bfloat16).reshape(experts_all, capacity, features)
    produced = expert_block(
        lax.all_to_all(outgoing, NODE, split_axis=0, concat_axis=0, tiled=True),
        w_gate,
        w_up,
        w_down,
    )
    returned = lax.all_to_all(produced, NODE, split_axis=0, concat_axis=0, tiled=True)
    gathered = jnp.take(returned.reshape(experts_all * capacity, features), target, axis=0)
    gathered = gathered.reshape(rows_here, picks_here, features)
    shares = gate_weights / jnp.sum(gate_weights, axis=1, keepdims=True)
    return jnp.einsum("tk,tkd->td", shares, gathered.astype(jnp.float32)).astype(jnp.bfloat16)


def mlp_kernel(
    core_ref, gain_ref, same_ref, other_ref, gate_hbm, up_hbm, down_hbm, out_ref,
    gate_buf, up_buf, down_buf, inner_buf, normed_buf, gain_buf, sems,
):
    expert = pl.program_id(0)
    chunks, _, chunk = gate_buf.shape
    chips = out_ref.shape[0]
    half = same_ref.shape[0]
    rows_here = half // chips
    gain_copy = pltpu.make_async_copy(gain_ref, gain_buf, sems.at[2, 1])
    gain_copy.start()
    copies = []
    for f in range(chunks):
        window = pl.ds(f * chunk, chunk)
        pair = (
            pltpu.make_async_copy(gate_hbm.at[expert, :, window], gate_buf.at[f], sems.at[0, f]),
            pltpu.make_async_copy(up_hbm.at[expert, :, window], up_buf.at[f], sems.at[1, f]),
        )
        for copy in pair:
            copy.start()
        copies.append(pair)
    down_copy = pltpu.make_async_copy(down_hbm.at[expert], down_buf, sems.at[2, 0])
    down_copy.start()
    gain_copy.wait()
    gain = gain_buf[0:1, :]
    for part, rows_ref in enumerate((same_ref, other_ref)):
        widened = rows_ref[...].astype(jnp.float32)
        meansq = jnp.mean(widened * widened, axis=1, keepdims=True) + 1e-06
        normed_buf[part] = (widened / jnp.sqrt(meansq) * gain).astype(jnp.bfloat16)
    for f in range(chunks):
        for copy in copies[f]:
            copy.wait()
        gate_block = gate_buf[f]
        up_block = up_buf[f]
        for part in range(2):
            rows = normed_buf[part]
            gate_part = jnp.dot(rows, gate_block, preferred_element_type=jnp.float32)
            up_part = jnp.dot(rows, up_block, preferred_element_type=jnp.float32)
            inner_buf[part, :, f * chunk : (f + 1) * chunk] = (
                jax.nn.silu(gate_part) * up_part
            ).astype(jnp.bfloat16)
    down_copy.wait()
    down_block = down_buf[...]
    core = core_ref[0]
    for part in range(2):
        produced = jnp.dot(inner_buf[part], down_block, preferred_element_type=jnp.float32)
        target = (core + part) % 2
        out_ref[:, pl.ds(target, 1)] = (
            produced.reshape(chips, 1, rows_here, -1).astype(out_ref.dtype)
        )


def expert_mlp(core, norm_gain, same_rows, other_rows, w_gate, w_up, w_down, chips):
    local_experts, features, hidden = w_gate.shape
    half = same_rows.shape[0]
    rows_here = half // chips
    chunk = 256 if hidden % 256 == 0 else hidden
    chunks = hidden // chunk
    grid_spec = pltpu.PrefetchScalarGridSpec(
        num_scalar_prefetch=1,
        grid=(local_experts,),
        in_specs=[
            pl.BlockSpec(memory_space=pltpu.HBM),
            pl.BlockSpec((half, features), lambda e, c: (0, 0)),
            pl.BlockSpec((half, features), lambda e, c: (0, 0)),
            pl.BlockSpec(memory_space=pltpu.HBM),
            pl.BlockSpec(memory_space=pltpu.HBM),
            pl.BlockSpec(memory_space=pltpu.HBM),
        ],
        out_specs=pl.BlockSpec(
            (None, chips, 2, rows_here, features), lambda e, c: (e, 0, 0, 0, 0)
        ),
        scratch_shapes=[
            pltpu.VMEM((chunks, features, chunk), jnp.bfloat16),
            pltpu.VMEM((chunks, features, chunk), jnp.bfloat16),
            pltpu.VMEM((hidden, features), jnp.bfloat16),
            pltpu.VMEM((2, half, hidden), jnp.bfloat16),
            pltpu.VMEM((2, half, features), jnp.bfloat16),
            pltpu.VMEM((8, features), jnp.float32),
            pltpu.SemaphoreType.DMA((3, max(chunks, 2))),
        ],
    )
    return pl.pallas_call(
        mlp_kernel,
        grid_spec=grid_spec,
        out_shape=jax.ShapeDtypeStruct(
            (local_experts, chips, 2, rows_here, features), jnp.bfloat16
        ),
        compiler_params=pltpu.CompilerParams(
            dimension_semantics=("arbitrary",), vmem_limit_bytes=50 * 1024 * 1024
        ),
    )(core.reshape(1), norm_gain, same_rows, other_rows, w_gate, w_up, w_down)


def spread_block(states, norm_gain, picks, gate_weights, w_gate, w_up, w_down):
    chips = lax.axis_size("chip")
    cores = lax.axis_size("core")
    core = lax.axis_index("core")
    rows_here, features = states.shape
    local_experts = w_gate.shape[0]
    peers = chips * cores
    experts_all = local_experts * peers
    spread = jnp.broadcast_to(states[None], (chips, rows_here, features))
    same_core = lax.all_to_all(spread, "chip", 0, 0, tiled=True)
    other_core = lax.ppermute(same_core, "core", [(i, (i + 1) % cores) for i in range(cores)])
    gain_rows = jnp.broadcast_to(norm_gain[None, :], (8, features))
    produced = expert_mlp(
        core.astype(jnp.int32),
        gain_rows,
        same_core.reshape(chips * rows_here, features),
        other_core.reshape(chips * rows_here, features),
        w_gate,
        w_up,
        w_down,
        chips,
    )
    produced = produced.reshape(local_experts, peers, rows_here, features)
    produced = produced.transpose(1, 0, 2, 3)
    returned = lax.all_to_all(produced, NODE, 0, 0, tiled=True)
    returned = returned.reshape(experts_all, rows_here, features)
    shares = gate_weights / jnp.sum(gate_weights, axis=1, keepdims=True)
    expert_ids = jnp.arange(experts_all, dtype=jnp.int32)
    chosen = picks[:, :, None] == expert_ids[None, None, :]
    dense_shares = jnp.sum(jnp.where(chosen, shares[:, :, None], 0.0), axis=1)
    weighted = dense_shares.T[:, :, None] * returned.astype(jnp.float32)
    return jnp.sum(weighted, axis=0).astype(jnp.bfloat16)

def attend(queries, keys, values, incoming_keys, incoming_values, lengths):
    request_rows = queries.shape[0]
    valid_length = keys.shape[1]
    query_groups = QUERY_HEADS // KEY_VALUE_HEADS
    score_scale = 1.0 / math.sqrt(HEAD_WIDTH)
    query_rows = queries.reshape(request_rows, KEY_VALUE_HEADS, query_groups, HEAD_WIDTH)
    stored_keys = keys.reshape(request_rows, valid_length, KEY_VALUE_HEADS, HEAD_WIDTH)
    stored_values = values.reshape(request_rows, valid_length, KEY_VALUE_HEADS, HEAD_WIDTH)
    scores = (
        jnp.einsum("rkgd,rlkd->rkgl", query_rows, stored_keys, preferred_element_type=jnp.float32)
        * score_scale
    )
    new_token_scores = (
        jnp.einsum(
            "behw,bew->beh",
            query_rows,
            incoming_keys.reshape(request_rows, KEY_VALUE_HEADS, HEAD_WIDTH),
            preferred_element_type=jnp.float32,
        )
        * score_scale
    )
    present = (jnp.arange(valid_length, dtype=jnp.int32)[None, :] < lengths[:, None])[
        :, None, None, :
    ]
    masked = jnp.where(present, scores, -1e30)
    highest = jnp.maximum(jnp.max(masked, axis=3), new_token_scores)
    raised = jnp.where(present, jnp.exp(masked - highest[..., None]), 0.0)
    fresh_raised = jnp.exp(new_token_scores - highest)
    denominator = jnp.sum(raised, axis=3) + fresh_raised
    probs = (raised / denominator[..., None]).astype(jnp.bfloat16)
    new_token_probability = (fresh_raised / denominator).astype(jnp.bfloat16)
    blended_output = jnp.einsum(
        "rkgl,rlkd->rkgd", probs, stored_values, preferred_element_type=jnp.float32
    )
    blended_output = blended_output + new_token_probability.astype(jnp.float32)[
        ..., None
    ] * incoming_values.reshape(request_rows, KEY_VALUE_HEADS, 1, HEAD_WIDTH).astype(jnp.float32)
    return blended_output.reshape(request_rows, QUERY_HEADS * HEAD_WIDTH).astype(jnp.bfloat16)


def on_device(
    states,
    norm_gain,
    picks,
    gate_weights,
    w_gate,
    w_up,
    w_down,
    queries,
    keys,
    values,
    incoming_keys,
    incoming_values,
    lengths,
):
    widened = states.astype(jnp.float32)
    meansq = jnp.mean(widened * widened, axis=1, keepdims=True) + 1e-06
    normed = (widened / jnp.sqrt(meansq) * norm_gain[None, :]).astype(jnp.bfloat16)
    experts_all = w_gate.shape[0] * node_size()
    capacity = min(TOK_DEV, max(2, 2 * TOK_DEV * TOPK // experts_all))
    gathered_rows = normed.shape[0] * node_size()
    if gathered_rows <= experts_all * capacity and lax.axis_size("core") == 2:
        moe_output = spread_block(states, norm_gain, picks, gate_weights, w_gate, w_up, w_down)
    else:
        moe_output = route_block(normed, picks, gate_weights, w_gate, w_up, w_down, capacity)
    attention_output = attend(queries, keys, values, incoming_keys, incoming_values, lengths)
    return (moe_output, attention_output)


def solution(mesh):
    groups, peers = mesh.devices.shape
    cores = 2 if peers % 2 == 0 else 1
    fine = Mesh(mesh.devices.reshape(groups, peers // cores, cores), ("group", "chip", "core"))
    in_specs = (
        P(("group", "chip", "core"), None),
        P(),
        P(("group", "chip", "core"), None),
        P(("group", "chip", "core"), None),
        P(NODE, None, None),
        P(NODE, None, None),
        P(NODE, None, None),
        P(("group", "chip", "core"), None),
        P(("group", "chip", "core"), None, None),
        P(("group", "chip", "core"), None, None),
        P(("group", "chip", "core"), None),
        P(("group", "chip", "core"), None),
        P(("group", "chip", "core")),
    )
    out_specs = (P(("group", "chip", "core"), None), P(("group", "chip", "core"), None))
    return jax.shard_map(
        on_device, mesh=fine, in_specs=in_specs, out_specs=out_specs, check_vma=False
    )
```

```python
import math

import jax
import jax.numpy as jnp
from jax import lax
from jax.experimental import pallas as pl
from jax.experimental.pallas import tpu as pltpu
from jax.sharding import Mesh, PartitionSpec as P

QUERY_HEADS = 32
KEY_VALUE_HEADS = 4
HEAD_WIDTH = 128
TOPK = 8
TOK_DEV = 16
NODE = ("chip", "core")


def node_size():
    return lax.axis_size("chip") * lax.axis_size("core")


def node_index():
    return lax.axis_index("chip") * lax.axis_size("core") + lax.axis_index("core")


def expert_block(received, w_gate, w_up, w_down):
    peers = node_size()
    local_experts = w_gate.shape[0]
    slot_count = received.shape[1]
    features = received.shape[2]
    grouped = received.reshape(peers, local_experts, slot_count, features)
    gate_part = jnp.einsum("nesd,edf->nesf", grouped, w_gate, preferred_element_type=jnp.float32)
    up_part = jnp.einsum("nesd,edf->nesf", grouped, w_up, preferred_element_type=jnp.float32)
    inner = (jax.nn.silu(gate_part) * up_part).astype(jnp.bfloat16)
    produced = jnp.einsum(
        "nesf,efd->nesd", inner, w_down, preferred_element_type=jnp.float32
    ).astype(jnp.bfloat16)
    return produced.reshape(peers * local_experts, slot_count, features)


def route_block(normed, picks, gate_weights, w_gate, w_up, w_down, capacity):
    rows_here = picks.shape[0]
    picks_here = picks.shape[1]
    experts_all = w_gate.shape[0] * node_size()
    features = normed.shape[1]
    flattened = picks.reshape(-1)
    expert_ids = jnp.arange(experts_all, dtype=jnp.int32)
    onehot = (flattened[:, None] == expert_ids[None, :]).astype(jnp.int32)
    earlier = jnp.cumsum(onehot, axis=0) - onehot
    slot_of = jnp.sum(earlier * onehot, axis=1)
    target = flattened * capacity + slot_of
    layout = jnp.arange(experts_all * capacity, dtype=jnp.int32)
    placed = jnp.sum(
        (layout[:, None, None] == target.reshape(rows_here, picks_here)[None, :, :]).astype(
            jnp.int32
        ),
        axis=2,
    )
    outgoing = jnp.dot(placed.astype(jnp.bfloat16), normed, preferred_element_type=jnp.float32)
    outgoing = outgoing.astype(jnp.bfloat16).reshape(experts_all, capacity, features)
    produced = expert_block(
        lax.all_to_all(outgoing, NODE, split_axis=0, concat_axis=0, tiled=True),
        w_gate,
        w_up,
        w_down,
    )
    returned = lax.all_to_all(produced, NODE, split_axis=0, concat_axis=0, tiled=True)
    gathered = jnp.take(returned.reshape(experts_all * capacity, features), target, axis=0)
    gathered = gathered.reshape(rows_here, picks_here, features)
    shares = gate_weights / jnp.sum(gate_weights, axis=1, keepdims=True)
    return jnp.einsum("tk,tkd->td", shares, gathered.astype(jnp.float32)).astype(jnp.bfloat16)


def mlp_kernel(
    core_ref, gain_ref, same_ref, other_ref, gate_hbm, up_hbm, down_hbm, out_ref,
    gate_buf, up_buf, down_buf, inner_buf, normed_buf, gain_buf, sems,
):
    expert = pl.program_id(0)
    gain_copy = pltpu.make_async_copy(gain_ref, gain_buf, sems.at[3, 0])
    gain_copy.start()
    chunks, _, chunk = gate_buf.shape
    columns, _, width = down_buf.shape
    chips = out_ref.shape[0]
    half = same_ref.shape[0]
    rows_here = half // chips
    stages = []
    for f in range(chunks):
        window = pl.ds(f * chunk, chunk)
        stages.append((
            pltpu.make_async_copy(gate_hbm.at[expert, :, window], gate_buf.at[f], sems.at[0, f]),
            pltpu.make_async_copy(up_hbm.at[expert, :, window], up_buf.at[f], sems.at[1, f]),
        ))
    for j in range(columns):
        window = pl.ds(j * width, width)
        stages.append(
            (pltpu.make_async_copy(down_hbm.at[expert, :, window], down_buf.at[j], sems.at[2, j]),)
        )
    for stage in stages[:2]:
        for copy in stage:
            copy.start()
    gain_copy.wait()
    gain = gain_buf[0:1, :]
    for part, rows_ref in enumerate((same_ref, other_ref)):
        widened = rows_ref[...].astype(jnp.float32)
        meansq = jnp.mean(widened * widened, axis=1, keepdims=True) + 1e-06
        normed_buf[part] = (widened / jnp.sqrt(meansq) * gain).astype(jnp.bfloat16)
    core = core_ref[0]
    for index, stage in enumerate(stages):
        for copy in stage:
            copy.wait()
        if index + 2 < len(stages):
            for copy in stages[index + 2]:
                copy.start()
        if index < chunks:
            gate_block = gate_buf[index]
            up_block = up_buf[index]
            for part in range(2):
                rows = normed_buf[part]
                gate_part = jnp.dot(rows, gate_block, preferred_element_type=jnp.float32)
                up_part = jnp.dot(rows, up_block, preferred_element_type=jnp.float32)
                inner_buf[part, :, index * chunk : (index + 1) * chunk] = (
                    jax.nn.silu(gate_part) * up_part
                ).astype(jnp.bfloat16)
        else:
            j = index - chunks
            down_block = down_buf[j]
            for part in range(2):
                produced = jnp.dot(inner_buf[part], down_block, preferred_element_type=jnp.float32)
                target = (core + part) % 2
                out_ref[:, pl.ds(target, 1), :, j * width : (j + 1) * width] = (
                    produced.reshape(chips, 1, rows_here, width).astype(out_ref.dtype)
                )


def expert_mlp(core, norm_gain, same_rows, other_rows, w_gate, w_up, w_down, chips):
    local_experts, features, hidden = w_gate.shape
    half = same_rows.shape[0]
    rows_here = half // chips
    chunk = 256 if hidden % 256 == 0 else hidden
    chunks = hidden // chunk
    columns = 4 if features % 512 == 0 else 1
    grid_spec = pltpu.PrefetchScalarGridSpec(
        num_scalar_prefetch=1,
        grid=(local_experts,),
        in_specs=[
            pl.BlockSpec(memory_space=pltpu.HBM),
            pl.BlockSpec((half, features), lambda e, c: (0, 0)),
            pl.BlockSpec((half, features), lambda e, c: (0, 0)),
            pl.BlockSpec(memory_space=pltpu.HBM),
            pl.BlockSpec(memory_space=pltpu.HBM),
            pl.BlockSpec(memory_space=pltpu.HBM),
        ],
        out_specs=pl.BlockSpec(
            (None, chips, 2, rows_here, features), lambda e, c: (e, 0, 0, 0, 0)
        ),
        scratch_shapes=[
            pltpu.VMEM((chunks, features, chunk), jnp.bfloat16),
            pltpu.VMEM((chunks, features, chunk), jnp.bfloat16),
            pltpu.VMEM((columns, hidden, features // columns), jnp.bfloat16),
            pltpu.VMEM((2, half, hidden), jnp.bfloat16),
            pltpu.VMEM((2, half, features), jnp.bfloat16),
            pltpu.VMEM((8, features), jnp.float32),
            pltpu.SemaphoreType.DMA((4, max(chunks, columns))),
        ],
    )
    return pl.pallas_call(
        mlp_kernel,
        grid_spec=grid_spec,
        out_shape=jax.ShapeDtypeStruct(
            (local_experts, chips, 2, rows_here, features), jnp.bfloat16
        ),
        compiler_params=pltpu.CompilerParams(
            dimension_semantics=("arbitrary",), vmem_limit_bytes=50 * 1024 * 1024
        ),
    )(core.reshape(1), norm_gain, same_rows, other_rows, w_gate, w_up, w_down)


def spread_block(states, norm_gain, picks, gate_weights, w_gate, w_up, w_down):
    chips = lax.axis_size("chip")
    cores = lax.axis_size("core")
    core = lax.axis_index("core")
    rows_here, features = states.shape
    local_experts = w_gate.shape[0]
    peers = chips * cores
    experts_all = local_experts * peers
    spread = jnp.broadcast_to(states[None], (chips, rows_here, features))
    same_core = lax.all_to_all(spread, "chip", 0, 0, tiled=True)
    other_core = lax.ppermute(same_core, "core", [(i, (i + 1) % cores) for i in range(cores)])
    gain_rows = jnp.broadcast_to(norm_gain[None, :], (8, features))
    produced = expert_mlp(
        core.astype(jnp.int32),
        gain_rows,
        same_core.reshape(chips * rows_here, features),
        other_core.reshape(chips * rows_here, features),
        w_gate,
        w_up,
        w_down,
        chips,
    )
    produced = produced.reshape(local_experts, peers, rows_here, features)
    produced = produced.transpose(1, 0, 2, 3)
    returned = lax.all_to_all(produced, NODE, 0, 0, tiled=True)
    returned = returned.reshape(experts_all, rows_here, features)
    shares = gate_weights / jnp.sum(gate_weights, axis=1, keepdims=True)
    expert_ids = jnp.arange(experts_all, dtype=jnp.int32)
    chosen = picks[:, :, None] == expert_ids[None, None, :]
    dense_shares = jnp.sum(jnp.where(chosen, shares[:, :, None], 0.0), axis=1)
    weighted = dense_shares.T[:, :, None] * returned.astype(jnp.float32)
    return jnp.sum(weighted, axis=0).astype(jnp.bfloat16)

def attend(queries, keys, values, incoming_keys, incoming_values, lengths):
    request_rows = queries.shape[0]
    valid_length = keys.shape[1]
    query_groups = QUERY_HEADS // KEY_VALUE_HEADS
    score_scale = 1.0 / math.sqrt(HEAD_WIDTH)
    query_rows = queries.reshape(request_rows, KEY_VALUE_HEADS, query_groups, HEAD_WIDTH)
    stored_keys = keys.reshape(request_rows, valid_length, KEY_VALUE_HEADS, HEAD_WIDTH)
    stored_values = values.reshape(request_rows, valid_length, KEY_VALUE_HEADS, HEAD_WIDTH)
    scores = (
        jnp.einsum("rkgd,rlkd->rkgl", query_rows, stored_keys, preferred_element_type=jnp.float32)
        * score_scale
    )
    new_token_scores = (
        jnp.einsum(
            "behw,bew->beh",
            query_rows,
            incoming_keys.reshape(request_rows, KEY_VALUE_HEADS, HEAD_WIDTH),
            preferred_element_type=jnp.float32,
        )
        * score_scale
    )
    present = (jnp.arange(valid_length, dtype=jnp.int32)[None, :] < lengths[:, None])[
        :, None, None, :
    ]
    masked = jnp.where(present, scores, -1e30)
    highest = jnp.maximum(jnp.max(masked, axis=3), new_token_scores)
    raised = jnp.where(present, jnp.exp(masked - highest[..., None]), 0.0)
    fresh_raised = jnp.exp(new_token_scores - highest)
    denominator = jnp.sum(raised, axis=3) + fresh_raised
    probs = (raised / denominator[..., None]).astype(jnp.bfloat16)
    new_token_probability = (fresh_raised / denominator).astype(jnp.bfloat16)
    blended_output = jnp.einsum(
        "rkgl,rlkd->rkgd", probs, stored_values, preferred_element_type=jnp.float32
    )
    blended_output = blended_output + new_token_probability.astype(jnp.float32)[
        ..., None
    ] * incoming_values.reshape(request_rows, KEY_VALUE_HEADS, 1, HEAD_WIDTH).astype(jnp.float32)
    return blended_output.reshape(request_rows, QUERY_HEADS * HEAD_WIDTH).astype(jnp.bfloat16)


def on_device(
    states,
    norm_gain,
    picks,
    gate_weights,
    w_gate,
    w_up,
    w_down,
    queries,
    keys,
    values,
    incoming_keys,
    incoming_values,
    lengths,
):
    widened = states.astype(jnp.float32)
    meansq = jnp.mean(widened * widened, axis=1, keepdims=True) + 1e-06
    normed = (widened / jnp.sqrt(meansq) * norm_gain[None, :]).astype(jnp.bfloat16)
    experts_all = w_gate.shape[0] * node_size()
    capacity = min(TOK_DEV, max(2, 2 * TOK_DEV * TOPK // experts_all))
    gathered_rows = normed.shape[0] * node_size()
    if gathered_rows <= experts_all * capacity and lax.axis_size("core") == 2:
        moe_output = spread_block(states, norm_gain, picks, gate_weights, w_gate, w_up, w_down)
    else:
        moe_output = route_block(normed, picks, gate_weights, w_gate, w_up, w_down, capacity)
    attention_output = attend(queries, keys, values, incoming_keys, incoming_values, lengths)
    return (moe_output, attention_output)


def solution(mesh):
    groups, peers = mesh.devices.shape
    cores = 2 if peers % 2 == 0 else 1
    fine = Mesh(mesh.devices.reshape(groups, peers // cores, cores), ("group", "chip", "core"))
    in_specs = (
        P(("group", "chip", "core"), None),
        P(),
        P(("group", "chip", "core"), None),
        P(("group", "chip", "core"), None),
        P(NODE, None, None),
        P(NODE, None, None),
        P(NODE, None, None),
        P(("group", "chip", "core"), None),
        P(("group", "chip", "core"), None, None),
        P(("group", "chip", "core"), None, None),
        P(("group", "chip", "core"), None),
        P(("group", "chip", "core"), None),
        P(("group", "chip", "core")),
    )
    out_specs = (P(("group", "chip", "core"), None), P(("group", "chip", "core"), None))
    return jax.shard_map(
        on_device, mesh=fine, in_specs=in_specs, out_specs=out_specs, check_vma=False
    )
```

```python
import math

import jax
import jax.numpy as jnp
from jax import lax
from jax.experimental import pallas as pl
from jax.experimental.pallas import tpu as pltpu
from jax.sharding import Mesh, PartitionSpec as P

QUERY_HEADS = 32
KEY_VALUE_HEADS = 4
HEAD_WIDTH = 128
TOPK = 8
TOK_DEV = 16
NODE = ("chip", "core")


def node_size():
    return lax.axis_size("chip") * lax.axis_size("core")


def node_index():
    return lax.axis_index("chip") * lax.axis_size("core") + lax.axis_index("core")


def expert_block(received, w_gate, w_up, w_down):
    peers = node_size()
    local_experts = w_gate.shape[0]
    slot_count = received.shape[1]
    features = received.shape[2]
    grouped = received.reshape(peers, local_experts, slot_count, features)
    gate_part = jnp.einsum("nesd,edf->nesf", grouped, w_gate, preferred_element_type=jnp.float32)
    up_part = jnp.einsum("nesd,edf->nesf", grouped, w_up, preferred_element_type=jnp.float32)
    inner = (jax.nn.silu(gate_part) * up_part).astype(jnp.bfloat16)
    produced = jnp.einsum(
        "nesf,efd->nesd", inner, w_down, preferred_element_type=jnp.float32
    ).astype(jnp.bfloat16)
    return produced.reshape(peers * local_experts, slot_count, features)


def route_block(normed, picks, gate_weights, w_gate, w_up, w_down, capacity):
    rows_here = picks.shape[0]
    picks_here = picks.shape[1]
    experts_all = w_gate.shape[0] * node_size()
    features = normed.shape[1]
    flattened = picks.reshape(-1)
    expert_ids = jnp.arange(experts_all, dtype=jnp.int32)
    onehot = (flattened[:, None] == expert_ids[None, :]).astype(jnp.int32)
    earlier = jnp.cumsum(onehot, axis=0) - onehot
    slot_of = jnp.sum(earlier * onehot, axis=1)
    target = flattened * capacity + slot_of
    layout = jnp.arange(experts_all * capacity, dtype=jnp.int32)
    placed = jnp.sum(
        (layout[:, None, None] == target.reshape(rows_here, picks_here)[None, :, :]).astype(
            jnp.int32
        ),
        axis=2,
    )
    outgoing = jnp.dot(placed.astype(jnp.bfloat16), normed, preferred_element_type=jnp.float32)
    outgoing = outgoing.astype(jnp.bfloat16).reshape(experts_all, capacity, features)
    produced = expert_block(
        lax.all_to_all(outgoing, NODE, split_axis=0, concat_axis=0, tiled=True),
        w_gate,
        w_up,
        w_down,
    )
    returned = lax.all_to_all(produced, NODE, split_axis=0, concat_axis=0, tiled=True)
    gathered = jnp.take(returned.reshape(experts_all * capacity, features), target, axis=0)
    gathered = gathered.reshape(rows_here, picks_here, features)
    shares = gate_weights / jnp.sum(gate_weights, axis=1, keepdims=True)
    return jnp.einsum("tk,tkd->td", shares, gathered.astype(jnp.float32)).astype(jnp.bfloat16)


def mlp_kernel(
    core_ref, gain_ref, same_ref, other_ref, gate_hbm, up_hbm, down_hbm, out_ref,
    gate_buf, up_buf, down_buf, inner_buf, normed_buf, gain_buf, sems,
):
    expert = pl.program_id(0)
    gain_copy = pltpu.make_async_copy(gain_ref, gain_buf, sems.at[3, 0])
    gain_copy.start()
    chunks, _, chunk = gate_buf.shape
    columns, _, width = down_buf.shape
    chips = out_ref.shape[0]
    half = same_ref.shape[0]
    rows_here = half // chips
    stages = []
    for f in range(chunks):
        window = pl.ds(f * chunk, chunk)
        stages.append((
            pltpu.make_async_copy(gate_hbm.at[expert, :, window], gate_buf.at[f], sems.at[0, f]),
            pltpu.make_async_copy(up_hbm.at[expert, :, window], up_buf.at[f], sems.at[1, f]),
        ))
    for j in range(columns):
        window = pl.ds(j * width, width)
        stages.append(
            (pltpu.make_async_copy(down_hbm.at[expert, :, window], down_buf.at[j], sems.at[2, j]),)
        )
    for stage in stages:
        for copy in stage:
            copy.start()
    gain_copy.wait()
    gain = gain_buf[0:1, :]
    for part, rows_ref in enumerate((same_ref, other_ref)):
        widened = rows_ref[...].astype(jnp.float32)
        meansq = jnp.mean(widened * widened, axis=1, keepdims=True) + 1e-06
        normed_buf[part] = (widened / jnp.sqrt(meansq) * gain).astype(jnp.bfloat16)
    core = core_ref[0]
    for index, stage in enumerate(stages):
        for copy in stage:
            copy.wait()
        if index < chunks:
            gate_block = gate_buf[index]
            up_block = up_buf[index]
            for part in range(2):
                rows = normed_buf[part]
                gate_part = jnp.dot(rows, gate_block, preferred_element_type=jnp.float32)
                up_part = jnp.dot(rows, up_block, preferred_element_type=jnp.float32)
                inner_buf[part, :, index * chunk : (index + 1) * chunk] = (
                    jax.nn.silu(gate_part) * up_part
                ).astype(jnp.bfloat16)
        else:
            j = index - chunks
            down_block = down_buf[j]
            for part in range(2):
                produced = jnp.dot(inner_buf[part], down_block, preferred_element_type=jnp.float32)
                target = (core + part) % 2
                out_ref[:, pl.ds(target, 1), :, j * width : (j + 1) * width] = (
                    produced.reshape(chips, 1, rows_here, width).astype(out_ref.dtype)
                )


def expert_mlp(core, norm_gain, same_rows, other_rows, w_gate, w_up, w_down, chips):
    local_experts, features, hidden = w_gate.shape
    half = same_rows.shape[0]
    rows_here = half // chips
    chunk = 256 if hidden % 256 == 0 else hidden
    chunks = hidden // chunk
    columns = 4 if features % 512 == 0 else 1
    grid_spec = pltpu.PrefetchScalarGridSpec(
        num_scalar_prefetch=1,
        grid=(local_experts,),
        in_specs=[
            pl.BlockSpec(memory_space=pltpu.HBM),
            pl.BlockSpec((half, features), lambda e, c: (0, 0)),
            pl.BlockSpec((half, features), lambda e, c: (0, 0)),
            pl.BlockSpec(memory_space=pltpu.HBM),
            pl.BlockSpec(memory_space=pltpu.HBM),
            pl.BlockSpec(memory_space=pltpu.HBM),
        ],
        out_specs=pl.BlockSpec(
            (None, chips, 2, rows_here, features), lambda e, c: (e, 0, 0, 0, 0)
        ),
        scratch_shapes=[
            pltpu.VMEM((chunks, features, chunk), jnp.bfloat16),
            pltpu.VMEM((chunks, features, chunk), jnp.bfloat16),
            pltpu.VMEM((columns, hidden, features // columns), jnp.bfloat16),
            pltpu.VMEM((2, half, hidden), jnp.bfloat16),
            pltpu.VMEM((2, half, features), jnp.bfloat16),
            pltpu.VMEM((8, features), jnp.float32),
            pltpu.SemaphoreType.DMA((4, max(chunks, columns))),
        ],
    )
    return pl.pallas_call(
        mlp_kernel,
        grid_spec=grid_spec,
        out_shape=jax.ShapeDtypeStruct(
            (local_experts, chips, 2, rows_here, features), jnp.bfloat16
        ),
        compiler_params=pltpu.CompilerParams(
            dimension_semantics=("arbitrary",), vmem_limit_bytes=50 * 1024 * 1024
        ),
    )(core.reshape(1), norm_gain, same_rows, other_rows, w_gate, w_up, w_down)


def spread_block(states, norm_gain, picks, gate_weights, w_gate, w_up, w_down):
    chips = lax.axis_size("chip")
    cores = lax.axis_size("core")
    core = lax.axis_index("core")
    rows_here, features = states.shape
    local_experts = w_gate.shape[0]
    peers = chips * cores
    experts_all = local_experts * peers
    spread = jnp.broadcast_to(states[None], (chips, rows_here, features))
    same_core = lax.all_to_all(spread, "chip", 0, 0, tiled=True)
    other_core = lax.ppermute(same_core, "core", [(i, (i + 1) % cores) for i in range(cores)])
    gain_rows = jnp.broadcast_to(norm_gain[None, :], (8, features))
    produced = expert_mlp(
        core.astype(jnp.int32),
        gain_rows,
        same_core.reshape(chips * rows_here, features),
        other_core.reshape(chips * rows_here, features),
        w_gate,
        w_up,
        w_down,
        chips,
    )
    produced = produced.reshape(local_experts, peers, rows_here, features)
    produced = produced.transpose(1, 0, 2, 3)
    returned = lax.all_to_all(produced, NODE, 0, 0, tiled=True)
    returned = returned.reshape(experts_all, rows_here, features)
    shares = gate_weights / jnp.sum(gate_weights, axis=1, keepdims=True)
    expert_ids = jnp.arange(experts_all, dtype=jnp.int32)
    chosen = picks[:, :, None] == expert_ids[None, None, :]
    dense_shares = jnp.sum(jnp.where(chosen, shares[:, :, None], 0.0), axis=1)
    weighted = dense_shares.T[:, :, None] * returned.astype(jnp.float32)
    return jnp.sum(weighted, axis=0).astype(jnp.bfloat16)

def attend(queries, keys, values, incoming_keys, incoming_values, lengths):
    request_rows = queries.shape[0]
    valid_length = keys.shape[1]
    query_groups = QUERY_HEADS // KEY_VALUE_HEADS
    score_scale = 1.0 / math.sqrt(HEAD_WIDTH)
    query_rows = queries.reshape(request_rows, KEY_VALUE_HEADS, query_groups, HEAD_WIDTH)
    stored_keys = keys.reshape(request_rows, valid_length, KEY_VALUE_HEADS, HEAD_WIDTH)
    stored_values = values.reshape(request_rows, valid_length, KEY_VALUE_HEADS, HEAD_WIDTH)
    scores = (
        jnp.einsum("rkgd,rlkd->rkgl", query_rows, stored_keys, preferred_element_type=jnp.float32)
        * score_scale
    )
    new_token_scores = (
        jnp.einsum(
            "behw,bew->beh",
            query_rows,
            incoming_keys.reshape(request_rows, KEY_VALUE_HEADS, HEAD_WIDTH),
            preferred_element_type=jnp.float32,
        )
        * score_scale
    )
    present = (jnp.arange(valid_length, dtype=jnp.int32)[None, :] < lengths[:, None])[
        :, None, None, :
    ]
    masked = jnp.where(present, scores, -1e30)
    highest = jnp.maximum(jnp.max(masked, axis=3), new_token_scores)
    raised = jnp.where(present, jnp.exp(masked - highest[..., None]), 0.0)
    fresh_raised = jnp.exp(new_token_scores - highest)
    denominator = jnp.sum(raised, axis=3) + fresh_raised
    probs = (raised / denominator[..., None]).astype(jnp.bfloat16)
    new_token_probability = (fresh_raised / denominator).astype(jnp.bfloat16)
    blended_output = jnp.einsum(
        "rkgl,rlkd->rkgd", probs, stored_values, preferred_element_type=jnp.float32
    )
    blended_output = blended_output + new_token_probability.astype(jnp.float32)[
        ..., None
    ] * incoming_values.reshape(request_rows, KEY_VALUE_HEADS, 1, HEAD_WIDTH).astype(jnp.float32)
    return blended_output.reshape(request_rows, QUERY_HEADS * HEAD_WIDTH).astype(jnp.bfloat16)


def on_device(
    states,
    norm_gain,
    picks,
    gate_weights,
    w_gate,
    w_up,
    w_down,
    queries,
    keys,
    values,
    incoming_keys,
    incoming_values,
    lengths,
):
    widened = states.astype(jnp.float32)
    meansq = jnp.mean(widened * widened, axis=1, keepdims=True) + 1e-06
    normed = (widened / jnp.sqrt(meansq) * norm_gain[None, :]).astype(jnp.bfloat16)
    experts_all = w_gate.shape[0] * node_size()
    capacity = min(TOK_DEV, max(2, 2 * TOK_DEV * TOPK // experts_all))
    gathered_rows = normed.shape[0] * node_size()
    if gathered_rows <= experts_all * capacity and lax.axis_size("core") == 2:
        moe_output = spread_block(states, norm_gain, picks, gate_weights, w_gate, w_up, w_down)
    else:
        moe_output = route_block(normed, picks, gate_weights, w_gate, w_up, w_down, capacity)
    attention_output = attend(queries, keys, values, incoming_keys, incoming_values, lengths)
    return (moe_output, attention_output)


def solution(mesh):
    groups, peers = mesh.devices.shape
    cores = 2 if peers % 2 == 0 else 1
    fine = Mesh(mesh.devices.reshape(groups, peers // cores, cores), ("group", "chip", "core"))
    in_specs = (
        P(("group", "chip", "core"), None),
        P(),
        P(("group", "chip", "core"), None),
        P(("group", "chip", "core"), None),
        P(NODE, None, None),
        P(NODE, None, None),
        P(NODE, None, None),
        P(("group", "chip", "core"), None),
        P(("group", "chip", "core"), None, None),
        P(("group", "chip", "core"), None, None),
        P(("group", "chip", "core"), None),
        P(("group", "chip", "core"), None),
        P(("group", "chip", "core")),
    )
    out_specs = (P(("group", "chip", "core"), None), P(("group", "chip", "core"), None))
    return jax.shard_map(
        on_device, mesh=fine, in_specs=in_specs, out_specs=out_specs, check_vma=False
    )
```

```python
import math

import jax
import jax.numpy as jnp
from jax import lax
from jax.experimental import pallas as pl
from jax.experimental.pallas import tpu as pltpu
from jax.sharding import Mesh, PartitionSpec as P

QUERY_HEADS = 32
KEY_VALUE_HEADS = 4
HEAD_WIDTH = 128
TOPK = 8
TOK_DEV = 16
NODE = ("chip", "core")


def node_size():
    return lax.axis_size("chip") * lax.axis_size("core")


def node_index():
    return lax.axis_index("chip") * lax.axis_size("core") + lax.axis_index("core")


def expert_block(received, w_gate, w_up, w_down):
    peers = node_size()
    local_experts = w_gate.shape[0]
    slot_count = received.shape[1]
    features = received.shape[2]
    grouped = received.reshape(peers, local_experts, slot_count, features)
    gate_part = jnp.einsum("nesd,edf->nesf", grouped, w_gate, preferred_element_type=jnp.float32)
    up_part = jnp.einsum("nesd,edf->nesf", grouped, w_up, preferred_element_type=jnp.float32)
    inner = (jax.nn.silu(gate_part) * up_part).astype(jnp.bfloat16)
    produced = jnp.einsum(
        "nesf,efd->nesd", inner, w_down, preferred_element_type=jnp.float32
    ).astype(jnp.bfloat16)
    return produced.reshape(peers * local_experts, slot_count, features)


def route_block(normed, picks, gate_weights, w_gate, w_up, w_down, capacity):
    rows_here = picks.shape[0]
    picks_here = picks.shape[1]
    experts_all = w_gate.shape[0] * node_size()
    features = normed.shape[1]
    flattened = picks.reshape(-1)
    expert_ids = jnp.arange(experts_all, dtype=jnp.int32)
    onehot = (flattened[:, None] == expert_ids[None, :]).astype(jnp.int32)
    earlier = jnp.cumsum(onehot, axis=0) - onehot
    slot_of = jnp.sum(earlier * onehot, axis=1)
    target = flattened * capacity + slot_of
    layout = jnp.arange(experts_all * capacity, dtype=jnp.int32)
    placed = jnp.sum(
        (layout[:, None, None] == target.reshape(rows_here, picks_here)[None, :, :]).astype(
            jnp.int32
        ),
        axis=2,
    )
    outgoing = jnp.dot(placed.astype(jnp.bfloat16), normed, preferred_element_type=jnp.float32)
    outgoing = outgoing.astype(jnp.bfloat16).reshape(experts_all, capacity, features)
    produced = expert_block(
        lax.all_to_all(outgoing, NODE, split_axis=0, concat_axis=0, tiled=True),
        w_gate,
        w_up,
        w_down,
    )
    returned = lax.all_to_all(produced, NODE, split_axis=0, concat_axis=0, tiled=True)
    gathered = jnp.take(returned.reshape(experts_all * capacity, features), target, axis=0)
    gathered = gathered.reshape(rows_here, picks_here, features)
    shares = gate_weights / jnp.sum(gate_weights, axis=1, keepdims=True)
    return jnp.einsum("tk,tkd->td", shares, gathered.astype(jnp.float32)).astype(jnp.bfloat16)


def mlp_kernel(
    core_ref, gain_ref, same_ref, other_ref, gate_hbm, up_hbm, down_hbm, out_ref,
    gate_buf, up_buf, down_buf, inner_buf, normed_buf, gain_buf, sems,
):
    expert = pl.program_id(0)
    chunks, _, chunk = gate_buf.shape
    chips = out_ref.shape[0]
    half = same_ref.shape[0]
    rows_here = half // chips
    gain_copy = pltpu.make_async_copy(gain_ref, gain_buf, sems.at[2, 1])
    gain_copy.start()
    copies = []
    for f in range(chunks):
        window = pl.ds(f * chunk, chunk)
        pair = (
            pltpu.make_async_copy(gate_hbm.at[expert, :, window], gate_buf.at[f], sems.at[0, f]),
            pltpu.make_async_copy(up_hbm.at[expert, :, window], up_buf.at[f], sems.at[1, f]),
        )
        for copy in pair:
            copy.start()
        copies.append(pair)
    down_copy = pltpu.make_async_copy(down_hbm.at[expert], down_buf, sems.at[2, 0])
    down_copy.start()
    gain_copy.wait()
    gain = gain_buf[0:1, :]
    for part, rows_ref in enumerate((same_ref, other_ref)):
        widened = rows_ref[...].astype(jnp.float32)
        meansq = jnp.mean(widened * widened, axis=1, keepdims=True) + 1e-06
        normed_buf[part] = (widened / jnp.sqrt(meansq) * gain).astype(jnp.bfloat16)
    for f in range(chunks):
        for copy in copies[f]:
            copy.wait()
        gate_block = gate_buf[f]
        up_block = up_buf[f]
        for part in range(2):
            rows = normed_buf[part]
            gate_part = jnp.dot(rows, gate_block, preferred_element_type=jnp.float32)
            up_part = jnp.dot(rows, up_block, preferred_element_type=jnp.float32)
            inner_buf[part, :, f * chunk : (f + 1) * chunk] = (
                jax.nn.silu(gate_part) * up_part
            ).astype(jnp.bfloat16)
    down_copy.wait()
    down_block = down_buf[...]
    core = core_ref[0]
    for part in range(2):
        produced = jnp.dot(inner_buf[part], down_block, preferred_element_type=jnp.float32)
        target = (core + part) % 2
        out_ref[:, pl.ds(target, 1)] = (
            produced.reshape(chips, 1, rows_here, -1).astype(out_ref.dtype)
        )


def expert_mlp(core, norm_gain, same_rows, other_rows, w_gate, w_up, w_down, chips):
    local_experts, features, hidden = w_gate.shape
    half = same_rows.shape[0]
    rows_here = half // chips
    chunk = 256 if hidden % 256 == 0 else hidden
    chunks = hidden // chunk
    grid_spec = pltpu.PrefetchScalarGridSpec(
        num_scalar_prefetch=1,
        grid=(local_experts,),
        in_specs=[
            pl.BlockSpec(memory_space=pltpu.HBM),
            pl.BlockSpec((half, features), lambda e, c: (0, 0)),
            pl.BlockSpec((half, features), lambda e, c: (0, 0)),
            pl.BlockSpec(memory_space=pltpu.HBM),
            pl.BlockSpec(memory_space=pltpu.HBM),
            pl.BlockSpec(memory_space=pltpu.HBM),
        ],
        out_specs=pl.BlockSpec(
            (None, chips, 2, rows_here, features), lambda e, c: (e, 0, 0, 0, 0)
        ),
        scratch_shapes=[
            pltpu.VMEM((chunks, features, chunk), jnp.bfloat16),
            pltpu.VMEM((chunks, features, chunk), jnp.bfloat16),
            pltpu.VMEM((hidden, features), jnp.bfloat16),
            pltpu.VMEM((2, half, hidden), jnp.bfloat16),
            pltpu.VMEM((2, half, features), jnp.bfloat16),
            pltpu.VMEM((8, features), jnp.float32),
            pltpu.SemaphoreType.DMA((3, max(chunks, 2))),
        ],
    )
    return pl.pallas_call(
        mlp_kernel,
        grid_spec=grid_spec,
        out_shape=jax.ShapeDtypeStruct(
            (local_experts, chips, 2, rows_here, features), jnp.bfloat16
        ),
        compiler_params=pltpu.CompilerParams(
            dimension_semantics=("arbitrary",), vmem_limit_bytes=50 * 1024 * 1024
        ),
    )(core.reshape(1), norm_gain, same_rows, other_rows, w_gate, w_up, w_down)


def spread_block(states, norm_gain, picks, gate_weights, w_gate, w_up, w_down):
    chips = lax.axis_size("chip")
    cores = lax.axis_size("core")
    core = lax.axis_index("core")
    rows_here, features = states.shape
    local_experts = w_gate.shape[0]
    peers = chips * cores
    experts_all = local_experts * peers
    spread = jnp.broadcast_to(states[None], (chips, rows_here, features))
    same_core = lax.all_to_all(spread, "chip", 0, 0, tiled=True)
    other_core = lax.ppermute(same_core, "core", [(i, (i + 1) % cores) for i in range(cores)])
    gain_rows = jnp.broadcast_to(norm_gain[None, :], (8, features))
    produced = expert_mlp(
        core.astype(jnp.int32),
        gain_rows,
        same_core.reshape(chips * rows_here, features),
        other_core.reshape(chips * rows_here, features),
        w_gate,
        w_up,
        w_down,
        chips,
    )
    if local_experts == 1:
        produced = produced.reshape(peers, rows_here, features)
    else:
        produced = produced.reshape(local_experts, peers, rows_here, features)
        produced = produced.transpose(1, 0, 2, 3)
    returned = lax.all_to_all(produced, NODE, 0, 0, tiled=True)
    returned = returned.reshape(experts_all, rows_here, features)
    shares = gate_weights / jnp.sum(gate_weights, axis=1, keepdims=True)
    expert_ids = jnp.arange(experts_all, dtype=jnp.int32)
    chosen = picks[:, :, None] == expert_ids[None, None, :]
    dense_shares = jnp.sum(jnp.where(chosen, shares[:, :, None], 0.0), axis=1)
    weighted = dense_shares.T[:, :, None] * returned.astype(jnp.float32)
    return jnp.sum(weighted, axis=0).astype(jnp.bfloat16)

def attend(queries, keys, values, incoming_keys, incoming_values, lengths):
    request_rows = queries.shape[0]
    valid_length = keys.shape[1]
    query_groups = QUERY_HEADS // KEY_VALUE_HEADS
    score_scale = 1.0 / math.sqrt(HEAD_WIDTH)
    query_rows = queries.reshape(request_rows, KEY_VALUE_HEADS, query_groups, HEAD_WIDTH)
    stored_keys = keys.reshape(request_rows, valid_length, KEY_VALUE_HEADS, HEAD_WIDTH)
    stored_values = values.reshape(request_rows, valid_length, KEY_VALUE_HEADS, HEAD_WIDTH)
    scores = (
        jnp.einsum("rkgd,rlkd->rkgl", query_rows, stored_keys, preferred_element_type=jnp.float32)
        * score_scale
    )
    new_token_scores = (
        jnp.einsum(
            "behw,bew->beh",
            query_rows,
            incoming_keys.reshape(request_rows, KEY_VALUE_HEADS, HEAD_WIDTH),
            preferred_element_type=jnp.float32,
        )
        * score_scale
    )
    present = (jnp.arange(valid_length, dtype=jnp.int32)[None, :] < lengths[:, None])[
        :, None, None, :
    ]
    masked = jnp.where(present, scores, -1e30)
    highest = jnp.maximum(jnp.max(masked, axis=3), new_token_scores)
    raised = jnp.where(present, jnp.exp(masked - highest[..., None]), 0.0)
    fresh_raised = jnp.exp(new_token_scores - highest)
    denominator = jnp.sum(raised, axis=3) + fresh_raised
    probs = (raised / denominator[..., None]).astype(jnp.bfloat16)
    new_token_probability = (fresh_raised / denominator).astype(jnp.bfloat16)
    blended_output = jnp.einsum(
        "rkgl,rlkd->rkgd", probs, stored_values, preferred_element_type=jnp.float32
    )
    blended_output = blended_output + new_token_probability.astype(jnp.float32)[
        ..., None
    ] * incoming_values.reshape(request_rows, KEY_VALUE_HEADS, 1, HEAD_WIDTH).astype(jnp.float32)
    return blended_output.reshape(request_rows, QUERY_HEADS * HEAD_WIDTH).astype(jnp.bfloat16)


def on_device(
    states,
    norm_gain,
    picks,
    gate_weights,
    w_gate,
    w_up,
    w_down,
    queries,
    keys,
    values,
    incoming_keys,
    incoming_values,
    lengths,
):
    widened = states.astype(jnp.float32)
    meansq = jnp.mean(widened * widened, axis=1, keepdims=True) + 1e-06
    normed = (widened / jnp.sqrt(meansq) * norm_gain[None, :]).astype(jnp.bfloat16)
    experts_all = w_gate.shape[0] * node_size()
    capacity = min(TOK_DEV, max(2, 2 * TOK_DEV * TOPK // experts_all))
    gathered_rows = normed.shape[0] * node_size()
    if gathered_rows <= experts_all * capacity and lax.axis_size("core") == 2:
        moe_output = spread_block(states, norm_gain, picks, gate_weights, w_gate, w_up, w_down)
    else:
        moe_output = route_block(normed, picks, gate_weights, w_gate, w_up, w_down, capacity)
    attention_output = attend(queries, keys, values, incoming_keys, incoming_values, lengths)
    return (moe_output, attention_output)


def solution(mesh):
    groups, peers = mesh.devices.shape
    cores = 2 if peers % 2 == 0 else 1
    fine = Mesh(mesh.devices.reshape(groups, peers // cores, cores), ("group", "chip", "core"))
    in_specs = (
        P(("group", "chip", "core"), None),
        P(),
        P(("group", "chip", "core"), None),
        P(("group", "chip", "core"), None),
        P(NODE, None, None),
        P(NODE, None, None),
        P(NODE, None, None),
        P(("group", "chip", "core"), None),
        P(("group", "chip", "core"), None, None),
        P(("group", "chip", "core"), None, None),
        P(("group", "chip", "core"), None),
        P(("group", "chip", "core"), None),
        P(("group", "chip", "core")),
    )
    out_specs = (P(("group", "chip", "core"), None), P(("group", "chip", "core"), None))
    return jax.shard_map(
        on_device, mesh=fine, in_specs=in_specs, out_specs=out_specs, check_vma=False
    )
```

```python
import math

import jax
import jax.numpy as jnp
from jax import lax
from jax.experimental import pallas as pl
from jax.experimental.pallas import tpu as pltpu
from jax.sharding import Mesh, PartitionSpec as P

QUERY_HEADS = 32
KEY_VALUE_HEADS = 4
HEAD_WIDTH = 128
TOPK = 8
TOK_DEV = 16
NODE = ("chip", "core")


def node_size():
    return lax.axis_size("chip") * lax.axis_size("core")


def node_index():
    return lax.axis_index("chip") * lax.axis_size("core") + lax.axis_index("core")


def expert_block(received, w_gate, w_up, w_down):
    peers = node_size()
    local_experts = w_gate.shape[0]
    slot_count = received.shape[1]
    features = received.shape[2]
    grouped = received.reshape(peers, local_experts, slot_count, features)
    gate_part = jnp.einsum("nesd,edf->nesf", grouped, w_gate, preferred_element_type=jnp.float32)
    up_part = jnp.einsum("nesd,edf->nesf", grouped, w_up, preferred_element_type=jnp.float32)
    inner = (jax.nn.silu(gate_part) * up_part).astype(jnp.bfloat16)
    produced = jnp.einsum(
        "nesf,efd->nesd", inner, w_down, preferred_element_type=jnp.float32
    ).astype(jnp.bfloat16)
    return produced.reshape(peers * local_experts, slot_count, features)


def route_block(normed, picks, gate_weights, w_gate, w_up, w_down, capacity):
    rows_here = picks.shape[0]
    picks_here = picks.shape[1]
    experts_all = w_gate.shape[0] * node_size()
    features = normed.shape[1]
    flattened = picks.reshape(-1)
    expert_ids = jnp.arange(experts_all, dtype=jnp.int32)
    onehot = (flattened[:, None] == expert_ids[None, :]).astype(jnp.int32)
    earlier = jnp.cumsum(onehot, axis=0) - onehot
    slot_of = jnp.sum(earlier * onehot, axis=1)
    target = flattened * capacity + slot_of
    layout = jnp.arange(experts_all * capacity, dtype=jnp.int32)
    placed = jnp.sum(
        (layout[:, None, None] == target.reshape(rows_here, picks_here)[None, :, :]).astype(
            jnp.int32
        ),
        axis=2,
    )
    outgoing = jnp.dot(placed.astype(jnp.bfloat16), normed, preferred_element_type=jnp.float32)
    outgoing = outgoing.astype(jnp.bfloat16).reshape(experts_all, capacity, features)
    produced = expert_block(
        lax.all_to_all(outgoing, NODE, split_axis=0, concat_axis=0, tiled=True),
        w_gate,
        w_up,
        w_down,
    )
    returned = lax.all_to_all(produced, NODE, split_axis=0, concat_axis=0, tiled=True)
    gathered = jnp.take(returned.reshape(experts_all * capacity, features), target, axis=0)
    gathered = gathered.reshape(rows_here, picks_here, features)
    shares = gate_weights / jnp.sum(gate_weights, axis=1, keepdims=True)
    return jnp.einsum("tk,tkd->td", shares, gathered.astype(jnp.float32)).astype(jnp.bfloat16)


def mlp_kernel(
    core_ref, gain_ref, same_ref, other_ref, gate_hbm, up_hbm, down_hbm, out_ref,
    gate_buf, up_buf, down_buf, inner_buf, normed_buf, gain_buf, sems,
):
    expert = pl.program_id(0)
    chunks, _, chunk = gate_buf.shape
    chips = out_ref.shape[0]
    half = same_ref.shape[0]
    rows_here = half // chips
    gain_copy = pltpu.make_async_copy(gain_ref, gain_buf, sems.at[2, 1])
    gain_copy.start()
    copies = []
    for f in range(chunks):
        window = pl.ds(f * chunk, chunk)
        pair = (
            pltpu.make_async_copy(gate_hbm.at[expert, :, window], gate_buf.at[f], sems.at[0, f]),
            pltpu.make_async_copy(up_hbm.at[expert, :, window], up_buf.at[f], sems.at[1, f]),
        )
        for copy in pair:
            copy.start()
        copies.append(pair)
    down_copy = pltpu.make_async_copy(down_hbm.at[expert], down_buf, sems.at[2, 0])
    down_copy.start()
    gain_copy.wait()
    gain = gain_buf[0:1, :]
    for part, rows_ref in enumerate((same_ref, other_ref)):
        widened = rows_ref[...].astype(jnp.float32)
        meansq = jnp.mean(widened * widened, axis=1, keepdims=True) + 1e-06
        normed_buf[part] = (widened / jnp.sqrt(meansq) * gain).astype(jnp.bfloat16)
    for f in range(chunks):
        for copy in copies[f]:
            copy.wait()
        gate_block = gate_buf[f]
        up_block = up_buf[f]
        for part in range(2):
            rows = normed_buf[part]
            gate_part = jnp.dot(rows, gate_block, preferred_element_type=jnp.float32)
            up_part = jnp.dot(rows, up_block, preferred_element_type=jnp.float32)
            inner_buf[part, :, f * chunk : (f + 1) * chunk] = (
                jax.nn.silu(gate_part) * up_part
            ).astype(jnp.bfloat16)
    down_copy.wait()
    down_block = down_buf[...]
    core = core_ref[0]
    for part in range(2):
        produced = jnp.dot(inner_buf[part], down_block, preferred_element_type=jnp.float32)
        target = (core + part) % 2
        out_ref[:, pl.ds(target, 1)] = (
            produced.reshape(chips, 1, rows_here, -1).astype(out_ref.dtype)
        )


def expert_mlp(core, norm_gain, same_rows, other_rows, w_gate, w_up, w_down, chips):
    local_experts, features, hidden = w_gate.shape
    half = same_rows.shape[0]
    rows_here = half // chips
    chunk = 256 if hidden % 256 == 0 else hidden
    chunks = hidden // chunk
    grid_spec = pltpu.PrefetchScalarGridSpec(
        num_scalar_prefetch=2,
        grid=(local_experts,),
        in_specs=[
            pl.BlockSpec((half, features), lambda e, c, g: (0, 0)),
            pl.BlockSpec((half, features), lambda e, c, g: (0, 0)),
            pl.BlockSpec(memory_space=pltpu.HBM),
            pl.BlockSpec(memory_space=pltpu.HBM),
            pl.BlockSpec(memory_space=pltpu.HBM),
        ],
        out_specs=pl.BlockSpec(
            (None, chips, 2, rows_here, features), lambda e, c, g: (e, 0, 0, 0, 0)
        ),
        scratch_shapes=[
            pltpu.VMEM((chunks, features, chunk), jnp.bfloat16),
            pltpu.VMEM((chunks, features, chunk), jnp.bfloat16),
            pltpu.VMEM((hidden, features), jnp.bfloat16),
            pltpu.VMEM((2, half, hidden), jnp.bfloat16),
            pltpu.VMEM((2, half, features), jnp.bfloat16),
            pltpu.VMEM((1, features), jnp.float32),
            pltpu.SemaphoreType.DMA((3, max(chunks, 2))),
        ],
    )
    return pl.pallas_call(
        mlp_kernel,
        grid_spec=grid_spec,
        out_shape=jax.ShapeDtypeStruct(
            (local_experts, chips, 2, rows_here, features), jnp.bfloat16
        ),
        compiler_params=pltpu.CompilerParams(
            dimension_semantics=("arbitrary",), vmem_limit_bytes=50 * 1024 * 1024
        ),
    )(core.reshape(1), norm_gain, same_rows, other_rows, w_gate, w_up, w_down)


def spread_block(states, norm_gain, picks, gate_weights, w_gate, w_up, w_down):
    chips = lax.axis_size("chip")
    cores = lax.axis_size("core")
    core = lax.axis_index("core")
    rows_here, features = states.shape
    local_experts = w_gate.shape[0]
    peers = chips * cores
    experts_all = local_experts * peers
    spread = jnp.broadcast_to(states[None], (chips, rows_here, features))
    same_core = lax.all_to_all(spread, "chip", 0, 0, tiled=True)
    other_core = lax.ppermute(same_core, "core", [(i, (i + 1) % cores) for i in range(cores)])
    gain_rows = norm_gain.reshape(1, features)
    produced = expert_mlp(
        core.astype(jnp.int32),
        gain_rows,
        same_core.reshape(chips * rows_here, features),
        other_core.reshape(chips * rows_here, features),
        w_gate,
        w_up,
        w_down,
        chips,
    )
    if local_experts == 1:
        produced = produced.reshape(peers, rows_here, features)
    else:
        produced = produced.reshape(local_experts, peers, rows_here, features)
        produced = produced.transpose(1, 0, 2, 3)
    returned = lax.all_to_all(produced, NODE, 0, 0, tiled=True)
    returned = returned.reshape(experts_all, rows_here, features)
    shares = gate_weights / jnp.sum(gate_weights, axis=1, keepdims=True)
    expert_ids = jnp.arange(experts_all, dtype=jnp.int32)
    chosen = picks[:, :, None] == expert_ids[None, None, :]
    dense_shares = jnp.sum(jnp.where(chosen, shares[:, :, None], 0.0), axis=1)
    weighted = dense_shares.T[:, :, None] * returned.astype(jnp.float32)
    return jnp.sum(weighted, axis=0).astype(jnp.bfloat16)

def attend(queries, keys, values, incoming_keys, incoming_values, lengths):
    request_rows = queries.shape[0]
    valid_length = keys.shape[1]
    query_groups = QUERY_HEADS // KEY_VALUE_HEADS
    score_scale = 1.0 / math.sqrt(HEAD_WIDTH)
    query_rows = queries.reshape(request_rows, KEY_VALUE_HEADS, query_groups, HEAD_WIDTH)
    stored_keys = keys.reshape(request_rows, valid_length, KEY_VALUE_HEADS, HEAD_WIDTH)
    stored_values = values.reshape(request_rows, valid_length, KEY_VALUE_HEADS, HEAD_WIDTH)
    scores = (
        jnp.einsum("rkgd,rlkd->rkgl", query_rows, stored_keys, preferred_element_type=jnp.float32)
        * score_scale
    )
    new_token_scores = (
        jnp.einsum(
            "behw,bew->beh",
            query_rows,
            incoming_keys.reshape(request_rows, KEY_VALUE_HEADS, HEAD_WIDTH),
            preferred_element_type=jnp.float32,
        )
        * score_scale
    )
    present = (jnp.arange(valid_length, dtype=jnp.int32)[None, :] < lengths[:, None])[
        :, None, None, :
    ]
    masked = jnp.where(present, scores, -1e30)
    highest = jnp.maximum(jnp.max(masked, axis=3), new_token_scores)
    raised = jnp.where(present, jnp.exp(masked - highest[..., None]), 0.0)
    fresh_raised = jnp.exp(new_token_scores - highest)
    denominator = jnp.sum(raised, axis=3) + fresh_raised
    probs = (raised / denominator[..., None]).astype(jnp.bfloat16)
    new_token_probability = (fresh_raised / denominator).astype(jnp.bfloat16)
    blended_output = jnp.einsum(
        "rkgl,rlkd->rkgd", probs, stored_values, preferred_element_type=jnp.float32
    )
    blended_output = blended_output + new_token_probability.astype(jnp.float32)[
        ..., None
    ] * incoming_values.reshape(request_rows, KEY_VALUE_HEADS, 1, HEAD_WIDTH).astype(jnp.float32)
    return blended_output.reshape(request_rows, QUERY_HEADS * HEAD_WIDTH).astype(jnp.bfloat16)


def on_device(
    states,
    norm_gain,
    picks,
    gate_weights,
    w_gate,
    w_up,
    w_down,
    queries,
    keys,
    values,
    incoming_keys,
    incoming_values,
    lengths,
):
    widened = states.astype(jnp.float32)
    meansq = jnp.mean(widened * widened, axis=1, keepdims=True) + 1e-06
    normed = (widened / jnp.sqrt(meansq) * norm_gain[None, :]).astype(jnp.bfloat16)
    experts_all = w_gate.shape[0] * node_size()
    capacity = min(TOK_DEV, max(2, 2 * TOK_DEV * TOPK // experts_all))
    gathered_rows = normed.shape[0] * node_size()
    if gathered_rows <= experts_all * capacity and lax.axis_size("core") == 2:
        moe_output = spread_block(states, norm_gain, picks, gate_weights, w_gate, w_up, w_down)
    else:
        moe_output = route_block(normed, picks, gate_weights, w_gate, w_up, w_down, capacity)
    attention_output = attend(queries, keys, values, incoming_keys, incoming_values, lengths)
    return (moe_output, attention_output)


def solution(mesh):
    groups, peers = mesh.devices.shape
    cores = 2 if peers % 2 == 0 else 1
    fine = Mesh(mesh.devices.reshape(groups, peers // cores, cores), ("group", "chip", "core"))
    in_specs = (
        P(("group", "chip", "core"), None),
        P(),
        P(("group", "chip", "core"), None),
        P(("group", "chip", "core"), None),
        P(NODE, None, None),
        P(NODE, None, None),
        P(NODE, None, None),
        P(("group", "chip", "core"), None),
        P(("group", "chip", "core"), None, None),
        P(("group", "chip", "core"), None, None),
        P(("group", "chip", "core"), None),
        P(("group", "chip", "core"), None),
        P(("group", "chip", "core")),
    )
    out_specs = (P(("group", "chip", "core"), None), P(("group", "chip", "core"), None))
    return jax.shard_map(
        on_device, mesh=fine, in_specs=in_specs, out_specs=out_specs, check_vma=False
    )
```

```python
import math

import jax
import jax.numpy as jnp
from jax import lax
from jax.experimental import pallas as pl
from jax.experimental.pallas import tpu as pltpu
from jax.sharding import Mesh, PartitionSpec as P

QUERY_HEADS = 32
KEY_VALUE_HEADS = 4
HEAD_WIDTH = 128
TOPK = 8
TOK_DEV = 16
NODE = ("chip", "core")


def node_size():
    return lax.axis_size("chip") * lax.axis_size("core")


def node_index():
    return lax.axis_index("chip") * lax.axis_size("core") + lax.axis_index("core")


def expert_block(received, w_gate, w_up, w_down):
    peers = node_size()
    local_experts = w_gate.shape[0]
    slot_count = received.shape[1]
    features = received.shape[2]
    grouped = received.reshape(peers, local_experts, slot_count, features)
    gate_part = jnp.einsum("nesd,edf->nesf", grouped, w_gate, preferred_element_type=jnp.float32)
    up_part = jnp.einsum("nesd,edf->nesf", grouped, w_up, preferred_element_type=jnp.float32)
    inner = (jax.nn.silu(gate_part) * up_part).astype(jnp.bfloat16)
    produced = jnp.einsum(
        "nesf,efd->nesd", inner, w_down, preferred_element_type=jnp.float32
    ).astype(jnp.bfloat16)
    return produced.reshape(peers * local_experts, slot_count, features)


def route_block(normed, picks, gate_weights, w_gate, w_up, w_down, capacity):
    rows_here = picks.shape[0]
    picks_here = picks.shape[1]
    experts_all = w_gate.shape[0] * node_size()
    features = normed.shape[1]
    flattened = picks.reshape(-1)
    expert_ids = jnp.arange(experts_all, dtype=jnp.int32)
    onehot = (flattened[:, None] == expert_ids[None, :]).astype(jnp.int32)
    earlier = jnp.cumsum(onehot, axis=0) - onehot
    slot_of = jnp.sum(earlier * onehot, axis=1)
    target = flattened * capacity + slot_of
    layout = jnp.arange(experts_all * capacity, dtype=jnp.int32)
    placed = jnp.sum(
        (layout[:, None, None] == target.reshape(rows_here, picks_here)[None, :, :]).astype(
            jnp.int32
        ),
        axis=2,
    )
    outgoing = jnp.dot(placed.astype(jnp.bfloat16), normed, preferred_element_type=jnp.float32)
    outgoing = outgoing.astype(jnp.bfloat16).reshape(experts_all, capacity, features)
    produced = expert_block(
        lax.all_to_all(outgoing, NODE, split_axis=0, concat_axis=0, tiled=True),
        w_gate,
        w_up,
        w_down,
    )
    returned = lax.all_to_all(produced, NODE, split_axis=0, concat_axis=0, tiled=True)
    gathered = jnp.take(returned.reshape(experts_all * capacity, features), target, axis=0)
    gathered = gathered.reshape(rows_here, picks_here, features)
    shares = gate_weights / jnp.sum(gate_weights, axis=1, keepdims=True)
    return jnp.einsum("tk,tkd->td", shares, gathered.astype(jnp.float32)).astype(jnp.bfloat16)


def mlp_kernel(
    core_ref, gain_ref, same_ref, other_ref, gate_hbm, up_hbm, down_hbm, out_ref,
    gate_buf, up_buf, down_buf, inner_buf, normed_buf, gain_buf, out_buf, sems,
):
    expert = pl.program_id(0)
    chunks, _, chunk = gate_buf.shape
    chips = out_buf.shape[1]
    half = same_ref.shape[0]
    rows_here = half // chips
    gain_copy = pltpu.make_async_copy(gain_ref, gain_buf, sems.at[2, 1])
    gain_copy.start()
    copies = []
    for f in range(chunks):
        window = pl.ds(f * chunk, chunk)
        pair = (
            pltpu.make_async_copy(gate_hbm.at[expert, :, window], gate_buf.at[f], sems.at[0, f]),
            pltpu.make_async_copy(up_hbm.at[expert, :, window], up_buf.at[f], sems.at[1, f]),
        )
        for copy in pair:
            copy.start()
        copies.append(pair)
    down_copy = pltpu.make_async_copy(down_hbm.at[expert], down_buf, sems.at[2, 0])
    down_copy.start()
    gain_copy.wait()
    gain = gain_buf[0:1, :]
    for part, rows_ref in enumerate((same_ref, other_ref)):
        widened = rows_ref[...].astype(jnp.float32)
        meansq = jnp.mean(widened * widened, axis=1, keepdims=True) + 1e-06
        normed_buf[part] = (widened / jnp.sqrt(meansq) * gain).astype(jnp.bfloat16)
    for f in range(chunks):
        for copy in copies[f]:
            copy.wait()
        gate_block = gate_buf[f]
        up_block = up_buf[f]
        for part in range(2):
            rows = normed_buf[part]
            gate_part = jnp.dot(rows, gate_block, preferred_element_type=jnp.float32)
            up_part = jnp.dot(rows, up_block, preferred_element_type=jnp.float32)
            inner_buf[part, :, f * chunk : (f + 1) * chunk] = (
                jax.nn.silu(gate_part) * up_part
            ).astype(jnp.bfloat16)
    down_copy.wait()
    down_block = down_buf[...]
    core = core_ref[0]
    stores = []
    for part in range(2):
        produced = jnp.dot(inner_buf[part], down_block, preferred_element_type=jnp.float32)
        out_buf[part] = produced.reshape(chips, 1, rows_here, -1).astype(out_buf.dtype)
        target = (core + part) % 2
        store = pltpu.make_async_copy(
            out_buf.at[part], out_ref.at[expert, :, pl.ds(target, 1)], sems.at[2, 2 + part]
        )
        store.start()
        stores.append(store)
    for store in stores:
        store.wait()


def expert_mlp(core, norm_gain, same_rows, other_rows, w_gate, w_up, w_down, chips):
    local_experts, features, hidden = w_gate.shape
    half = same_rows.shape[0]
    rows_here = half // chips
    chunk = 256 if hidden % 256 == 0 else hidden
    chunks = hidden // chunk
    grid_spec = pltpu.PrefetchScalarGridSpec(
        num_scalar_prefetch=1,
        grid=(local_experts,),
        in_specs=[
            pl.BlockSpec(memory_space=pltpu.HBM),
            pl.BlockSpec((half, features), lambda e, c: (0, 0)),
            pl.BlockSpec((half, features), lambda e, c: (0, 0)),
            pl.BlockSpec(memory_space=pltpu.HBM),
            pl.BlockSpec(memory_space=pltpu.HBM),
            pl.BlockSpec(memory_space=pltpu.HBM),
        ],
        out_specs=pl.BlockSpec(memory_space=pltpu.HBM),
        scratch_shapes=[
            pltpu.VMEM((chunks, features, chunk), jnp.bfloat16),
            pltpu.VMEM((chunks, features, chunk), jnp.bfloat16),
            pltpu.VMEM((hidden, features), jnp.bfloat16),
            pltpu.VMEM((2, half, hidden), jnp.bfloat16),
            pltpu.VMEM((2, half, features), jnp.bfloat16),
            pltpu.VMEM((8, features), jnp.float32),
            pltpu.VMEM((2, chips, 1, rows_here, features), jnp.bfloat16),
            pltpu.SemaphoreType.DMA((3, max(chunks, 4))),
        ],
    )
    return pl.pallas_call(
        mlp_kernel,
        grid_spec=grid_spec,
        out_shape=jax.ShapeDtypeStruct(
            (local_experts, chips, 2, rows_here, features), jnp.bfloat16
        ),
        compiler_params=pltpu.CompilerParams(
            dimension_semantics=("arbitrary",), vmem_limit_bytes=50 * 1024 * 1024
        ),
    )(core.reshape(1), norm_gain, same_rows, other_rows, w_gate, w_up, w_down)


def spread_block(states, norm_gain, picks, gate_weights, w_gate, w_up, w_down):
    chips = lax.axis_size("chip")
    cores = lax.axis_size("core")
    core = lax.axis_index("core")
    rows_here, features = states.shape
    local_experts = w_gate.shape[0]
    peers = chips * cores
    experts_all = local_experts * peers
    spread = jnp.broadcast_to(states[None], (chips, rows_here, features))
    same_core = lax.all_to_all(spread, "chip", 0, 0, tiled=True)
    other_core = lax.ppermute(same_core, "core", [(i, (i + 1) % cores) for i in range(cores)])
    gain_rows = jnp.broadcast_to(norm_gain[None, :], (8, features))
    produced = expert_mlp(
        core.astype(jnp.int32),
        gain_rows,
        same_core.reshape(chips * rows_here, features),
        other_core.reshape(chips * rows_here, features),
        w_gate,
        w_up,
        w_down,
        chips,
    )
    produced = produced.reshape(local_experts, peers, rows_here, features)
    produced = produced.transpose(1, 0, 2, 3)
    returned = lax.all_to_all(produced, NODE, 0, 0, tiled=True)
    returned = returned.reshape(experts_all, rows_here, features)
    shares = gate_weights / jnp.sum(gate_weights, axis=1, keepdims=True)
    expert_ids = jnp.arange(experts_all, dtype=jnp.int32)
    chosen = picks[:, :, None] == expert_ids[None, None, :]
    dense_shares = jnp.sum(jnp.where(chosen, shares[:, :, None], 0.0), axis=1)
    weighted = dense_shares.T[:, :, None] * returned.astype(jnp.float32)
    return jnp.sum(weighted, axis=0).astype(jnp.bfloat16)

def attend(queries, keys, values, incoming_keys, incoming_values, lengths):
    request_rows = queries.shape[0]
    valid_length = keys.shape[1]
    query_groups = QUERY_HEADS // KEY_VALUE_HEADS
    score_scale = 1.0 / math.sqrt(HEAD_WIDTH)
    query_rows = queries.reshape(request_rows, KEY_VALUE_HEADS, query_groups, HEAD_WIDTH)
    stored_keys = keys.reshape(request_rows, valid_length, KEY_VALUE_HEADS, HEAD_WIDTH)
    stored_values = values.reshape(request_rows, valid_length, KEY_VALUE_HEADS, HEAD_WIDTH)
    scores = (
        jnp.einsum("rkgd,rlkd->rkgl", query_rows, stored_keys, preferred_element_type=jnp.float32)
        * score_scale
    )
    new_token_scores = (
        jnp.einsum(
            "behw,bew->beh",
            query_rows,
            incoming_keys.reshape(request_rows, KEY_VALUE_HEADS, HEAD_WIDTH),
            preferred_element_type=jnp.float32,
        )
        * score_scale
    )
    present = (jnp.arange(valid_length, dtype=jnp.int32)[None, :] < lengths[:, None])[
        :, None, None, :
    ]
    masked = jnp.where(present, scores, -1e30)
    highest = jnp.maximum(jnp.max(masked, axis=3), new_token_scores)
    raised = jnp.where(present, jnp.exp(masked - highest[..., None]), 0.0)
    fresh_raised = jnp.exp(new_token_scores - highest)
    denominator = jnp.sum(raised, axis=3) + fresh_raised
    probs = (raised / denominator[..., None]).astype(jnp.bfloat16)
    new_token_probability = (fresh_raised / denominator).astype(jnp.bfloat16)
    blended_output = jnp.einsum(
        "rkgl,rlkd->rkgd", probs, stored_values, preferred_element_type=jnp.float32
    )
    blended_output = blended_output + new_token_probability.astype(jnp.float32)[
        ..., None
    ] * incoming_values.reshape(request_rows, KEY_VALUE_HEADS, 1, HEAD_WIDTH).astype(jnp.float32)
    return blended_output.reshape(request_rows, QUERY_HEADS * HEAD_WIDTH).astype(jnp.bfloat16)


def on_device(
    states,
    norm_gain,
    picks,
    gate_weights,
    w_gate,
    w_up,
    w_down,
    queries,
    keys,
    values,
    incoming_keys,
    incoming_values,
    lengths,
):
    widened = states.astype(jnp.float32)
    meansq = jnp.mean(widened * widened, axis=1, keepdims=True) + 1e-06
    normed = (widened / jnp.sqrt(meansq) * norm_gain[None, :]).astype(jnp.bfloat16)
    experts_all = w_gate.shape[0] * node_size()
    capacity = min(TOK_DEV, max(2, 2 * TOK_DEV * TOPK // experts_all))
    gathered_rows = normed.shape[0] * node_size()
    if gathered_rows <= experts_all * capacity and lax.axis_size("core") == 2:
        moe_output = spread_block(states, norm_gain, picks, gate_weights, w_gate, w_up, w_down)
    else:
        moe_output = route_block(normed, picks, gate_weights, w_gate, w_up, w_down, capacity)
    attention_output = attend(queries, keys, values, incoming_keys, incoming_values, lengths)
    return (moe_output, attention_output)


def solution(mesh):
    groups, peers = mesh.devices.shape
    cores = 2 if peers % 2 == 0 else 1
    fine = Mesh(mesh.devices.reshape(groups, peers // cores, cores), ("group", "chip", "core"))
    in_specs = (
        P(("group", "chip", "core"), None),
        P(),
        P(("group", "chip", "core"), None),
        P(("group", "chip", "core"), None),
        P(NODE, None, None),
        P(NODE, None, None),
        P(NODE, None, None),
        P(("group", "chip", "core"), None),
        P(("group", "chip", "core"), None, None),
        P(("group", "chip", "core"), None, None),
        P(("group", "chip", "core"), None),
        P(("group", "chip", "core"), None),
        P(("group", "chip", "core")),
    )
    out_specs = (P(("group", "chip", "core"), None), P(("group", "chip", "core"), None))
    return jax.shard_map(
        on_device, mesh=fine, in_specs=in_specs, out_specs=out_specs, check_vma=False
    )
```

```python
import math

import jax
import jax.numpy as jnp
from jax import lax
from jax.experimental import pallas as pl
from jax.experimental.pallas import tpu as pltpu
from jax.sharding import Mesh, PartitionSpec as P

QUERY_HEADS = 32
KEY_VALUE_HEADS = 4
HEAD_WIDTH = 128
TOPK = 8
TOK_DEV = 16
NODE = ("chip", "core")


def node_size():
    return lax.axis_size("chip") * lax.axis_size("core")


def node_index():
    return lax.axis_index("chip") * lax.axis_size("core") + lax.axis_index("core")


def expert_block(received, w_gate, w_up, w_down):
    peers = node_size()
    local_experts = w_gate.shape[0]
    slot_count = received.shape[1]
    features = received.shape[2]
    grouped = received.reshape(peers, local_experts, slot_count, features)
    gate_part = jnp.einsum("nesd,edf->nesf", grouped, w_gate, preferred_element_type=jnp.float32)
    up_part = jnp.einsum("nesd,edf->nesf", grouped, w_up, preferred_element_type=jnp.float32)
    inner = (jax.nn.silu(gate_part) * up_part).astype(jnp.bfloat16)
    produced = jnp.einsum(
        "nesf,efd->nesd", inner, w_down, preferred_element_type=jnp.float32
    ).astype(jnp.bfloat16)
    return produced.reshape(peers * local_experts, slot_count, features)


def route_block(normed, picks, gate_weights, w_gate, w_up, w_down, capacity):
    rows_here = picks.shape[0]
    picks_here = picks.shape[1]
    experts_all = w_gate.shape[0] * node_size()
    features = normed.shape[1]
    flattened = picks.reshape(-1)
    expert_ids = jnp.arange(experts_all, dtype=jnp.int32)
    onehot = (flattened[:, None] == expert_ids[None, :]).astype(jnp.int32)
    earlier = jnp.cumsum(onehot, axis=0) - onehot
    slot_of = jnp.sum(earlier * onehot, axis=1)
    target = flattened * capacity + slot_of
    layout = jnp.arange(experts_all * capacity, dtype=jnp.int32)
    placed = jnp.sum(
        (layout[:, None, None] == target.reshape(rows_here, picks_here)[None, :, :]).astype(
            jnp.int32
        ),
        axis=2,
    )
    outgoing = jnp.dot(placed.astype(jnp.bfloat16), normed, preferred_element_type=jnp.float32)
    outgoing = outgoing.astype(jnp.bfloat16).reshape(experts_all, capacity, features)
    produced = expert_block(
        lax.all_to_all(outgoing, NODE, split_axis=0, concat_axis=0, tiled=True),
        w_gate,
        w_up,
        w_down,
    )
    returned = lax.all_to_all(produced, NODE, split_axis=0, concat_axis=0, tiled=True)
    gathered = jnp.take(returned.reshape(experts_all * capacity, features), target, axis=0)
    gathered = gathered.reshape(rows_here, picks_here, features)
    shares = gate_weights / jnp.sum(gate_weights, axis=1, keepdims=True)
    return jnp.einsum("tk,tkd->td", shares, gathered.astype(jnp.float32)).astype(jnp.bfloat16)


def mlp_kernel(
    core_ref, gain_ref, same_ref, other_ref, gate_hbm, up_hbm, down_hbm, out_ref,
    gate_buf, up_buf, down_buf, inner_buf, normed_buf, gain_buf, out_buf, sems,
):
    expert = pl.program_id(0)
    chunks, _, chunk = gate_buf.shape
    chips = out_buf.shape[1]
    half = same_ref.shape[0]
    rows_here = half // chips
    gain_copy = pltpu.make_async_copy(gain_ref, gain_buf, sems.at[2, 1])
    gain_copy.start()
    copies = []
    for f in range(chunks):
        window = pl.ds(f * chunk, chunk)
        pair = (
            pltpu.make_async_copy(gate_hbm.at[expert, :, window], gate_buf.at[f], sems.at[0, f]),
            pltpu.make_async_copy(up_hbm.at[expert, :, window], up_buf.at[f], sems.at[1, f]),
        )
        for copy in pair:
            copy.start()
        copies.append(pair)
    down_copy = pltpu.make_async_copy(down_hbm.at[expert], down_buf, sems.at[2, 0])
    down_copy.start()
    gain_copy.wait()
    gain = gain_buf[0:1, :]
    for part, rows_ref in enumerate((same_ref, other_ref)):
        widened = rows_ref[...].astype(jnp.float32)
        meansq = jnp.mean(widened * widened, axis=1, keepdims=True) + 1e-06
        normed_buf[part] = (widened / jnp.sqrt(meansq) * gain).astype(jnp.bfloat16)
    for f in range(chunks):
        for copy in copies[f]:
            copy.wait()
        gate_block = gate_buf[f]
        up_block = up_buf[f]
        for part in range(2):
            rows = normed_buf[part]
            gate_part = jnp.dot(rows, gate_block, preferred_element_type=jnp.float32)
            up_part = jnp.dot(rows, up_block, preferred_element_type=jnp.float32)
            inner_buf[part, :, f * chunk : (f + 1) * chunk] = (
                jax.nn.silu(gate_part) * up_part
            ).astype(jnp.bfloat16)
    down_copy.wait()
    down_block = down_buf[...]
    core = core_ref[0]
    stores = []
    for part in range(2):
        produced = jnp.dot(inner_buf[part], down_block, preferred_element_type=jnp.float32)
        out_buf[part] = produced.reshape(chips, 1, rows_here, -1).astype(out_buf.dtype)
        target = (core + part) % 2
        store = pltpu.make_async_copy(
            out_buf.at[part], out_ref.at[expert, :, pl.ds(target, 1)], sems.at[2, 2 + part]
        )
        store.start()
        stores.append(store)
    for store in stores:
        store.wait()


def expert_mlp(core, norm_gain, same_rows, other_rows, w_gate, w_up, w_down, chips):
    local_experts, features, hidden = w_gate.shape
    half = same_rows.shape[0]
    rows_here = half // chips
    chunk = 256 if hidden % 256 == 0 else hidden
    chunks = hidden // chunk
    grid_spec = pltpu.PrefetchScalarGridSpec(
        num_scalar_prefetch=1,
        grid=(local_experts,),
        in_specs=[
            pl.BlockSpec(memory_space=pltpu.HBM),
            pl.BlockSpec((half, features), lambda e, c: (0, 0)),
            pl.BlockSpec((half, features), lambda e, c: (0, 0)),
            pl.BlockSpec(memory_space=pltpu.HBM),
            pl.BlockSpec(memory_space=pltpu.HBM),
            pl.BlockSpec(memory_space=pltpu.HBM),
        ],
        out_specs=pl.BlockSpec(memory_space=pltpu.HBM),
        scratch_shapes=[
            pltpu.VMEM((chunks, features, chunk), jnp.bfloat16),
            pltpu.VMEM((chunks, features, chunk), jnp.bfloat16),
            pltpu.VMEM((hidden, features), jnp.bfloat16),
            pltpu.VMEM((2, half, hidden), jnp.bfloat16),
            pltpu.VMEM((2, half, features), jnp.bfloat16),
            pltpu.VMEM((8, features), jnp.float32),
            pltpu.VMEM((2, chips, 1, rows_here, features), jnp.bfloat16),
            pltpu.SemaphoreType.DMA((3, max(chunks, 4))),
        ],
    )
    return pl.pallas_call(
        mlp_kernel,
        grid_spec=grid_spec,
        out_shape=jax.ShapeDtypeStruct(
            (local_experts, chips, 2, rows_here, features), jnp.bfloat16
        ),
        compiler_params=pltpu.CompilerParams(
            dimension_semantics=("arbitrary",), vmem_limit_bytes=50 * 1024 * 1024
        ),
    )(core.reshape(1), norm_gain, same_rows, other_rows, w_gate, w_up, w_down)


def spread_block(states, norm_gain, picks, gate_weights, w_gate, w_up, w_down):
    chips = lax.axis_size("chip")
    cores = lax.axis_size("core")
    core = lax.axis_index("core")
    rows_here, features = states.shape
    local_experts = w_gate.shape[0]
    peers = chips * cores
    experts_all = local_experts * peers
    spread = jnp.broadcast_to(states[None], (chips, rows_here, features))
    same_core = lax.all_to_all(spread, "chip", 0, 0, tiled=True)
    other_core = lax.ppermute(same_core, "core", [(i, (i + 1) % cores) for i in range(cores)])
    gain_rows = jnp.broadcast_to(norm_gain[None, :], (8, features))
    produced = expert_mlp(
        core.astype(jnp.int32),
        gain_rows,
        same_core.reshape(chips * rows_here, features),
        other_core.reshape(chips * rows_here, features),
        w_gate,
        w_up,
        w_down,
        chips,
    )
    produced = produced.reshape(local_experts, peers, rows_here, features)
    produced = produced.transpose(1, 0, 2, 3)
    returned = lax.all_to_all(produced, NODE, 0, 0, tiled=True)
    returned = returned.reshape(experts_all, rows_here, features)
    shares = gate_weights / jnp.sum(gate_weights, axis=1, keepdims=True)
    expert_ids = jnp.arange(experts_all, dtype=jnp.int32)
    chosen = picks[:, :, None] == expert_ids[None, None, :]
    dense_shares = jnp.sum(jnp.where(chosen, shares[:, :, None], 0.0), axis=1)
    lanes = 128 if features % 128 == 0 else features
    column_shares = lax.optimization_barrier(
        jnp.broadcast_to(dense_shares.T[:, :, None], dense_shares.T.shape + (lanes,))
    )
    column_shares = jnp.tile(column_shares, (1, 1, features // lanes))
    weighted = column_shares * returned.astype(jnp.float32)
    return jnp.sum(weighted, axis=0).astype(jnp.bfloat16)

def attend(queries, keys, values, incoming_keys, incoming_values, lengths):
    request_rows = queries.shape[0]
    valid_length = keys.shape[1]
    query_groups = QUERY_HEADS // KEY_VALUE_HEADS
    score_scale = 1.0 / math.sqrt(HEAD_WIDTH)
    query_rows = queries.reshape(request_rows, KEY_VALUE_HEADS, query_groups, HEAD_WIDTH)
    stored_keys = keys.reshape(request_rows, valid_length, KEY_VALUE_HEADS, HEAD_WIDTH)
    stored_values = values.reshape(request_rows, valid_length, KEY_VALUE_HEADS, HEAD_WIDTH)
    scores = (
        jnp.einsum("rkgd,rlkd->rkgl", query_rows, stored_keys, preferred_element_type=jnp.float32)
        * score_scale
    )
    new_token_scores = (
        jnp.einsum(
            "behw,bew->beh",
            query_rows,
            incoming_keys.reshape(request_rows, KEY_VALUE_HEADS, HEAD_WIDTH),
            preferred_element_type=jnp.float32,
        )
        * score_scale
    )
    present = (jnp.arange(valid_length, dtype=jnp.int32)[None, :] < lengths[:, None])[
        :, None, None, :
    ]
    masked = jnp.where(present, scores, -1e30)
    highest = jnp.maximum(jnp.max(masked, axis=3), new_token_scores)
    raised = jnp.where(present, jnp.exp(masked - highest[..., None]), 0.0)
    fresh_raised = jnp.exp(new_token_scores - highest)
    denominator = jnp.sum(raised, axis=3) + fresh_raised
    probs = (raised / denominator[..., None]).astype(jnp.bfloat16)
    new_token_probability = (fresh_raised / denominator).astype(jnp.bfloat16)
    blended_output = jnp.einsum(
        "rkgl,rlkd->rkgd", probs, stored_values, preferred_element_type=jnp.float32
    )
    blended_output = blended_output + new_token_probability.astype(jnp.float32)[
        ..., None
    ] * incoming_values.reshape(request_rows, KEY_VALUE_HEADS, 1, HEAD_WIDTH).astype(jnp.float32)
    return blended_output.reshape(request_rows, QUERY_HEADS * HEAD_WIDTH).astype(jnp.bfloat16)


def on_device(
    states,
    norm_gain,
    picks,
    gate_weights,
    w_gate,
    w_up,
    w_down,
    queries,
    keys,
    values,
    incoming_keys,
    incoming_values,
    lengths,
):
    widened = states.astype(jnp.float32)
    meansq = jnp.mean(widened * widened, axis=1, keepdims=True) + 1e-06
    normed = (widened / jnp.sqrt(meansq) * norm_gain[None, :]).astype(jnp.bfloat16)
    experts_all = w_gate.shape[0] * node_size()
    capacity = min(TOK_DEV, max(2, 2 * TOK_DEV * TOPK // experts_all))
    gathered_rows = normed.shape[0] * node_size()
    if gathered_rows <= experts_all * capacity and lax.axis_size("core") == 2:
        moe_output = spread_block(states, norm_gain, picks, gate_weights, w_gate, w_up, w_down)
    else:
        moe_output = route_block(normed, picks, gate_weights, w_gate, w_up, w_down, capacity)
    attention_output = attend(queries, keys, values, incoming_keys, incoming_values, lengths)
    return (moe_output, attention_output)


def solution(mesh):
    groups, peers = mesh.devices.shape
    cores = 2 if peers % 2 == 0 else 1
    fine = Mesh(mesh.devices.reshape(groups, peers // cores, cores), ("group", "chip", "core"))
    in_specs = (
        P(("group", "chip", "core"), None),
        P(),
        P(("group", "chip", "core"), None),
        P(("group", "chip", "core"), None),
        P(NODE, None, None),
        P(NODE, None, None),
        P(NODE, None, None),
        P(("group", "chip", "core"), None),
        P(("group", "chip", "core"), None, None),
        P(("group", "chip", "core"), None, None),
        P(("group", "chip", "core"), None),
        P(("group", "chip", "core"), None),
        P(("group", "chip", "core")),
    )
    out_specs = (P(("group", "chip", "core"), None), P(("group", "chip", "core"), None))
    return jax.shard_map(
        on_device, mesh=fine, in_specs=in_specs, out_specs=out_specs, check_vma=False
    )
```

```python
import math

import jax
import jax.numpy as jnp
from jax import lax
from jax.experimental import pallas as pl
from jax.experimental.pallas import tpu as pltpu
from jax.sharding import Mesh, PartitionSpec as P

QUERY_HEADS = 32
KEY_VALUE_HEADS = 4
HEAD_WIDTH = 128
TOPK = 8
TOK_DEV = 16
NODE = ("chip", "core")


def node_size():
    return lax.axis_size("chip") * lax.axis_size("core")


def node_index():
    return lax.axis_index("chip") * lax.axis_size("core") + lax.axis_index("core")


def expert_block(received, w_gate, w_up, w_down):
    peers = node_size()
    local_experts = w_gate.shape[0]
    slot_count = received.shape[1]
    features = received.shape[2]
    grouped = received.reshape(peers, local_experts, slot_count, features)
    gate_part = jnp.einsum("nesd,edf->nesf", grouped, w_gate, preferred_element_type=jnp.float32)
    up_part = jnp.einsum("nesd,edf->nesf", grouped, w_up, preferred_element_type=jnp.float32)
    inner = (jax.nn.silu(gate_part) * up_part).astype(jnp.bfloat16)
    produced = jnp.einsum(
        "nesf,efd->nesd", inner, w_down, preferred_element_type=jnp.float32
    ).astype(jnp.bfloat16)
    return produced.reshape(peers * local_experts, slot_count, features)


def route_block(normed, picks, gate_weights, w_gate, w_up, w_down, capacity):
    rows_here = picks.shape[0]
    picks_here = picks.shape[1]
    experts_all = w_gate.shape[0] * node_size()
    features = normed.shape[1]
    flattened = picks.reshape(-1)
    expert_ids = jnp.arange(experts_all, dtype=jnp.int32)
    onehot = (flattened[:, None] == expert_ids[None, :]).astype(jnp.int32)
    earlier = jnp.cumsum(onehot, axis=0) - onehot
    slot_of = jnp.sum(earlier * onehot, axis=1)
    target = flattened * capacity + slot_of
    layout = jnp.arange(experts_all * capacity, dtype=jnp.int32)
    placed = jnp.sum(
        (layout[:, None, None] == target.reshape(rows_here, picks_here)[None, :, :]).astype(
            jnp.int32
        ),
        axis=2,
    )
    outgoing = jnp.dot(placed.astype(jnp.bfloat16), normed, preferred_element_type=jnp.float32)
    outgoing = outgoing.astype(jnp.bfloat16).reshape(experts_all, capacity, features)
    produced = expert_block(
        lax.all_to_all(outgoing, NODE, split_axis=0, concat_axis=0, tiled=True),
        w_gate,
        w_up,
        w_down,
    )
    returned = lax.all_to_all(produced, NODE, split_axis=0, concat_axis=0, tiled=True)
    gathered = jnp.take(returned.reshape(experts_all * capacity, features), target, axis=0)
    gathered = gathered.reshape(rows_here, picks_here, features)
    shares = gate_weights / jnp.sum(gate_weights, axis=1, keepdims=True)
    return jnp.einsum("tk,tkd->td", shares, gathered.astype(jnp.float32)).astype(jnp.bfloat16)


def mlp_kernel(
    core_ref, gain_ref, same_ref, other_ref, gate_hbm, up_hbm, down_hbm, out_ref,
    gate_buf, up_buf, down_buf, inner_buf, normed_buf, gain_buf, out_buf, sems,
):
    expert = pl.program_id(0)
    chunks, _, chunk = gate_buf.shape
    chips = out_buf.shape[1]
    half = same_ref.shape[0]
    rows_here = half // chips
    gain_copy = pltpu.make_async_copy(gain_ref, gain_buf, sems.at[2, 1])
    gain_copy.start()
    copies = []
    for f in range(chunks):
        window = pl.ds(f * chunk, chunk)
        pair = (
            pltpu.make_async_copy(gate_hbm.at[expert, :, window], gate_buf.at[f], sems.at[0, f]),
            pltpu.make_async_copy(up_hbm.at[expert, :, window], up_buf.at[f], sems.at[1, f]),
        )
        for copy in pair:
            copy.start()
        copies.append(pair)
    down_copy = pltpu.make_async_copy(down_hbm.at[expert], down_buf, sems.at[2, 0])
    down_copy.start()
    gain_copy.wait()
    gain = gain_buf[0:1, :]
    for part, rows_ref in enumerate((same_ref, other_ref)):
        widened = rows_ref[...].astype(jnp.float32)
        meansq = jnp.mean(widened * widened, axis=1, keepdims=True) + 1e-06
        normed_buf[part] = (widened / jnp.sqrt(meansq) * gain).astype(jnp.bfloat16)
    for f in range(chunks):
        for copy in copies[f]:
            copy.wait()
        gate_block = gate_buf[f]
        up_block = up_buf[f]
        for part in range(2):
            rows = normed_buf[part]
            gate_part = jnp.dot(rows, gate_block, preferred_element_type=jnp.float32)
            up_part = jnp.dot(rows, up_block, preferred_element_type=jnp.float32)
            inner_buf[part, :, f * chunk : (f + 1) * chunk] = (
                jax.nn.silu(gate_part) * up_part
            ).astype(jnp.bfloat16)
    down_copy.wait()
    down_block = down_buf[...]
    core = core_ref[0]
    stores = []
    for part in range(2):
        produced = jnp.dot(inner_buf[part], down_block, preferred_element_type=jnp.float32)
        out_buf[part] = produced.reshape(chips, 1, rows_here, -1).astype(out_buf.dtype)
        target = (core + part) % 2
        store = pltpu.make_async_copy(
            out_buf.at[part], out_ref.at[expert, :, pl.ds(target, 1)], sems.at[2, 2 + part]
        )
        store.start()
        stores.append(store)
    for store in stores:
        store.wait()


def expert_mlp(core, norm_gain, same_rows, other_rows, w_gate, w_up, w_down, chips):
    local_experts, features, hidden = w_gate.shape
    half = same_rows.shape[0]
    rows_here = half // chips
    chunk = 256 if hidden % 256 == 0 else hidden
    chunks = hidden // chunk
    grid_spec = pltpu.PrefetchScalarGridSpec(
        num_scalar_prefetch=1,
        grid=(local_experts,),
        in_specs=[
            pl.BlockSpec(memory_space=pltpu.HBM),
            pl.BlockSpec((half, features), lambda e, c: (0, 0)),
            pl.BlockSpec((half, features), lambda e, c: (0, 0)),
            pl.BlockSpec(memory_space=pltpu.HBM),
            pl.BlockSpec(memory_space=pltpu.HBM),
            pl.BlockSpec(memory_space=pltpu.HBM),
        ],
        out_specs=pl.BlockSpec(memory_space=pltpu.HBM),
        scratch_shapes=[
            pltpu.VMEM((chunks, features, chunk), jnp.bfloat16),
            pltpu.VMEM((chunks, features, chunk), jnp.bfloat16),
            pltpu.VMEM((hidden, features), jnp.bfloat16),
            pltpu.VMEM((2, half, hidden), jnp.bfloat16),
            pltpu.VMEM((2, half, features), jnp.bfloat16),
            pltpu.VMEM((8, features), jnp.float32),
            pltpu.VMEM((2, chips, 1, rows_here, features), jnp.bfloat16),
            pltpu.SemaphoreType.DMA((3, max(chunks, 4))),
        ],
    )
    return pl.pallas_call(
        mlp_kernel,
        grid_spec=grid_spec,
        out_shape=jax.ShapeDtypeStruct(
            (local_experts, chips, 2, rows_here, features), jnp.bfloat16
        ),
        compiler_params=pltpu.CompilerParams(
            dimension_semantics=("arbitrary",), vmem_limit_bytes=50 * 1024 * 1024
        ),
    )(core.reshape(1), norm_gain, same_rows, other_rows, w_gate, w_up, w_down)


def combine_kernel(share_ref, returned_ref, out_ref):
    experts, _, lanes = share_ref.shape
    for j in range(out_ref.shape[1] // lanes):
        window = slice(j * lanes, (j + 1) * lanes)
        total = None
        for e in range(experts):
            term = share_ref[e] * returned_ref[e, :, window].astype(jnp.float32)
            total = term if total is None else total + term
        out_ref[:, window] = total.astype(out_ref.dtype)


def combine(column_shares, returned):
    return pl.pallas_call(
        combine_kernel,
        out_shape=jax.ShapeDtypeStruct(returned.shape[1:], jnp.bfloat16),
    )(column_shares, returned)


def spread_block(states, norm_gain, picks, gate_weights, w_gate, w_up, w_down):
    chips = lax.axis_size("chip")
    cores = lax.axis_size("core")
    core = lax.axis_index("core")
    rows_here, features = states.shape
    local_experts = w_gate.shape[0]
    peers = chips * cores
    experts_all = local_experts * peers
    spread = jnp.broadcast_to(states[None], (chips, rows_here, features))
    same_core = lax.all_to_all(spread, "chip", 0, 0, tiled=True)
    other_core = lax.ppermute(same_core, "core", [(i, (i + 1) % cores) for i in range(cores)])
    gain_rows = jnp.broadcast_to(norm_gain[None, :], (8, features))
    produced = expert_mlp(
        core.astype(jnp.int32),
        gain_rows,
        same_core.reshape(chips * rows_here, features),
        other_core.reshape(chips * rows_here, features),
        w_gate,
        w_up,
        w_down,
        chips,
    )
    produced = produced.reshape(local_experts, peers, rows_here, features)
    produced = produced.transpose(1, 0, 2, 3)
    returned = lax.all_to_all(produced, NODE, 0, 0, tiled=True)
    returned = returned.reshape(experts_all, rows_here, features)
    shares = gate_weights / jnp.sum(gate_weights, axis=1, keepdims=True)
    expert_ids = jnp.arange(experts_all, dtype=jnp.int32)
    chosen = picks[:, :, None] == expert_ids[None, None, :]
    dense_shares = jnp.sum(jnp.where(chosen, shares[:, :, None], 0.0), axis=1)
    lanes = 128 if features % 128 == 0 else features
    column_shares = jnp.broadcast_to(dense_shares.T[:, :, None], dense_shares.T.shape + (lanes,))
    return combine(column_shares, returned)

def attend(queries, keys, values, incoming_keys, incoming_values, lengths):
    request_rows = queries.shape[0]
    valid_length = keys.shape[1]
    query_groups = QUERY_HEADS // KEY_VALUE_HEADS
    score_scale = 1.0 / math.sqrt(HEAD_WIDTH)
    query_rows = queries.reshape(request_rows, KEY_VALUE_HEADS, query_groups, HEAD_WIDTH)
    stored_keys = keys.reshape(request_rows, valid_length, KEY_VALUE_HEADS, HEAD_WIDTH)
    stored_values = values.reshape(request_rows, valid_length, KEY_VALUE_HEADS, HEAD_WIDTH)
    scores = (
        jnp.einsum("rkgd,rlkd->rkgl", query_rows, stored_keys, preferred_element_type=jnp.float32)
        * score_scale
    )
    new_token_scores = (
        jnp.einsum(
            "behw,bew->beh",
            query_rows,
            incoming_keys.reshape(request_rows, KEY_VALUE_HEADS, HEAD_WIDTH),
            preferred_element_type=jnp.float32,
        )
        * score_scale
    )
    present = (jnp.arange(valid_length, dtype=jnp.int32)[None, :] < lengths[:, None])[
        :, None, None, :
    ]
    masked = jnp.where(present, scores, -1e30)
    highest = jnp.maximum(jnp.max(masked, axis=3), new_token_scores)
    raised = jnp.where(present, jnp.exp(masked - highest[..., None]), 0.0)
    fresh_raised = jnp.exp(new_token_scores - highest)
    denominator = jnp.sum(raised, axis=3) + fresh_raised
    probs = (raised / denominator[..., None]).astype(jnp.bfloat16)
    new_token_probability = (fresh_raised / denominator).astype(jnp.bfloat16)
    blended_output = jnp.einsum(
        "rkgl,rlkd->rkgd", probs, stored_values, preferred_element_type=jnp.float32
    )
    blended_output = blended_output + new_token_probability.astype(jnp.float32)[
        ..., None
    ] * incoming_values.reshape(request_rows, KEY_VALUE_HEADS, 1, HEAD_WIDTH).astype(jnp.float32)
    return blended_output.reshape(request_rows, QUERY_HEADS * HEAD_WIDTH).astype(jnp.bfloat16)


def on_device(
    states,
    norm_gain,
    picks,
    gate_weights,
    w_gate,
    w_up,
    w_down,
    queries,
    keys,
    values,
    incoming_keys,
    incoming_values,
    lengths,
):
    widened = states.astype(jnp.float32)
    meansq = jnp.mean(widened * widened, axis=1, keepdims=True) + 1e-06
    normed = (widened / jnp.sqrt(meansq) * norm_gain[None, :]).astype(jnp.bfloat16)
    experts_all = w_gate.shape[0] * node_size()
    capacity = min(TOK_DEV, max(2, 2 * TOK_DEV * TOPK // experts_all))
    gathered_rows = normed.shape[0] * node_size()
    if gathered_rows <= experts_all * capacity and lax.axis_size("core") == 2:
        moe_output = spread_block(states, norm_gain, picks, gate_weights, w_gate, w_up, w_down)
    else:
        moe_output = route_block(normed, picks, gate_weights, w_gate, w_up, w_down, capacity)
    attention_output = attend(queries, keys, values, incoming_keys, incoming_values, lengths)
    return (moe_output, attention_output)


def solution(mesh):
    groups, peers = mesh.devices.shape
    cores = 2 if peers % 2 == 0 else 1
    fine = Mesh(mesh.devices.reshape(groups, peers // cores, cores), ("group", "chip", "core"))
    in_specs = (
        P(("group", "chip", "core"), None),
        P(),
        P(("group", "chip", "core"), None),
        P(("group", "chip", "core"), None),
        P(NODE, None, None),
        P(NODE, None, None),
        P(NODE, None, None),
        P(("group", "chip", "core"), None),
        P(("group", "chip", "core"), None, None),
        P(("group", "chip", "core"), None, None),
        P(("group", "chip", "core"), None),
        P(("group", "chip", "core"), None),
        P(("group", "chip", "core")),
    )
    out_specs = (P(("group", "chip", "core"), None), P(("group", "chip", "core"), None))
    return jax.shard_map(
        on_device, mesh=fine, in_specs=in_specs, out_specs=out_specs, check_vma=False
    )
```
